256 devices in a mesh: lat: 16 (over y_hi, z), lon: 16 (over x, y_lo, core).
Axes of the slice: x: 4, y: 4 (y_hi: 2, y_lo: 2; y = y_hi * 2 + y_lo), z: 8, core: 2. Of those that a mesh axis runs over, the one named last changes fastest.
Arguments:
- fields: bfloat16 [1, 512, 1024, 128], P(None, 'lat', 'lon'), may hold values from -6 to 6
- cotangent: bfloat16 [1, 512, 1024, 128], P(None, 'lat', 'lon'), may hold values from -6 to 6
- spectral_weight: bfloat16 [512, 2, 128, 128], P('lat'), may hold values from -0.375 to 0.375
- local_weight: bfloat16 [3, 128, 128], replicated, may hold values from -0.3125 to 0.3125
- filter_basis: bfloat16 [3, 512, 3, 17], replicated, may hold values from -0.83984375 to 0.83984375
- neighbor_rows: int32 [512, 3], replicated, may hold values from 0 to 511, as said below
Outputs:
- block_output: bfloat16 [1, 512, 1024, 128], P(None, 'lat', 'lon')
- input_grad: bfloat16 [1, 512, 1024, 128], P(None, 'lat', 'lon')
The draws below stay inside these ranges and needn't reach their ends.
Inputs may be any that keep to these rules, and one draw needn't show every extreme that they name: `neighbor_rows`: row i lists the rows that feed output latitude i: its first entry is max(i - 8, 0), its last min(i + 8, 511), and every entry lies within 8 of i.
All inputs are finite; a program needn't handle non-finite values.
Results may differ from the reference program's by a relative error of at most 0.015.
Values may be sent and summed in bfloat16 or wider, within the bound.
No kernel may reach another device: no remote copies, remote signals or barrier semaphores. Data moves between devices by JAX's collectives and lax.ppermute only.
A program may use at most 128 MiB of HBM per device.

```python
import math
import jax
import jax.numpy as jnp
from jax import lax

MEM = 1
C = 128
MDEV = 16
KB = 3
NB = 3
HW = 8
SUP = 17
NLAT = 512
NLON = 1024
MM = 256
L = 512


def draw_neighbor_rows(key, part):
    row_ids = jnp.arange(NLAT, dtype=jnp.int32)[:, None]
    offsets = jax.random.randint(key, (NLAT, NB), -HW, HW + 1, dtype=jnp.int32)
    column_ids = jnp.arange(NB, dtype=jnp.int32)[None, :]
    offsets = jnp.where(column_ids == 0, -HW, jnp.where(column_ids == NB - 1, HW, offsets))
    return jnp.clip(row_ids + offsets, 0, NLAT - 1).astype(jnp.int32)


def shard_levels(own_key, dims, shards, smallest, high):
    def one(position, shards_of):
        steps = jax.random.uniform(jax.random.fold_in(jax.random.fold_in(own_key, 6), position), (shards_of,), jnp.float32, smallest / len(shards), high / len(shards))
        return jnp.repeat(jnp.exp(steps), dims[position] // shards_of).reshape((-1,) + (1,) * (len(dims) - position - 1))

    factor_of = one(*shards[0])
    for cut in shards[1:]:
        factor_of = factor_of * one(*cut)
    return factor_of


def normal_values(stream_key, shape, deviation, limit, pieces=(), kind=jnp.bfloat16):
    values = jax.random.normal(stream_key, shape, jnp.float32) * deviation
    if len(pieces) > 0:
        values = shard_levels(stream_key, shape, pieces, -0.22, 0.18) * values
    return jnp.clip(values, min=-limit, max=limit).astype(kind)


def setup_inputs(seed: int = 0) -> dict:
    keys = jax.random.split(jax.random.key(seed), 7)
    fields = normal_values(keys[0], (MEM, NLAT, NLON, C), 1.0, 6.0, ((1, 16), (2, 16)))
    cotangent = normal_values(keys[1], (MEM, NLAT, NLON, C), 1.0, 6.0, ((1, 16), (2, 16)))
    spectral_weight = normal_values(keys[2], (L, 2, C, C), (2 * C) ** -0.5, 0.375, ((0, 16),))
    local_weight = normal_values(keys[3], (KB, C, C), (KB * C) ** -0.5, 0.3125)
    filter_basis = normal_values(keys[4], (KB, NLAT, NB, SUP), 0.14, 0.83984375)
    neighbor_rows = draw_neighbor_rows(jax.random.fold_in(keys[6], 71), 0)
    return {"fields": fields, "cotangent": cotangent, "spectral_weight": spectral_weight, "local_weight": local_weight, "filter_basis": filter_basis, "neighbor_rows": neighbor_rows}


TANH_SCALE = 0.7978845608028654
CUBIC_TERM = 0.044715

def rounded(values):
    return lax.optimization_barrier(values.astype(jnp.bfloat16))

def gelu_parts(values):
    tanh_input = TANH_SCALE * (values + CUBIC_TERM * values * values * values)
    hyper = jnp.tanh(tanh_input)
    result = 0.5 * values * (1.0 + hyper)
    derivative = 0.5 * (1.0 + hyper) + 0.5 * values * (1.0 - hyper * hyper) * TANH_SCALE * (1.0 + 3.0 * CUBIC_TERM * values * values)
    return (result, derivative)

def mode_tables(lon_count, mode_count):
    angles_int = jnp.arange(lon_count, dtype=jnp.int32)[:, None] * jnp.arange(mode_count, dtype=jnp.int32)[None, :] % lon_count
    angles = angles_int.astype(jnp.float32) * (2.0 * math.pi / lon_count)
    stacked = jnp.stack([jnp.cos(angles), -jnp.sin(angles)], axis=1)
    orders = jnp.arange(mode_count, dtype=jnp.int32)
    factor = jnp.where(orders == 0, 1.0, 2.0).astype(jnp.float32)
    to_modes = (stacked * (2.0 * math.pi / lon_count)).astype(jnp.bfloat16)
    from_modes = (stacked * factor[None, None, :]).astype(jnp.bfloat16)
    return (to_modes, from_modes)

def combine_steps(earlier, later):
    early_aa, early_ab, early_ba, early_bb, early_log = earlier
    late_aa, late_ab, late_ba, late_bb, late_log = later
    joint_aa = late_aa * early_aa + late_ab * early_ba
    joint_ab = late_aa * early_ab + late_ab * early_bb
    joint_ba = late_ba * early_aa + late_bb * early_ba
    joint_bb = late_ba * early_ab + late_bb * early_bb
    largest = jnp.maximum(jnp.maximum(jnp.abs(joint_aa), jnp.abs(joint_ab)), jnp.maximum(jnp.abs(joint_ba), jnp.abs(joint_bb)))
    return (joint_aa / largest, joint_ab / largest, joint_ba / largest, joint_bb / largest, early_log + late_log + jnp.log(largest))

def legendre_rows(orders, degree_count, lat_count):
    colatitude = math.pi * (jnp.arange(lat_count, dtype=jnp.float32) + 0.5) / lat_count
    cosine = jnp.cos(colatitude)
    sine_part = jnp.sin(colatitude)
    order_real = orders.astype(jnp.float32)
    seed_log = 0.5 * (jnp.log((2.0 * order_real + 1.0) / (4.0 * math.pi)) + lax.lgamma(order_real + 0.5) - lax.lgamma(order_real + 1.0) - 0.5 * math.log(math.pi))
    seed_log = seed_log[:, None] + order_real[:, None] * jnp.log(sine_part)[None, :]
    degree_ints = jnp.arange(degree_count, dtype=jnp.int32)
    degree_real = degree_ints.astype(jnp.float32)[:, None]
    order_row = order_real[None, :]
    active = degree_ints[:, None] > orders[None, :]
    forward_gain = jnp.sqrt(jnp.maximum(4.0 * degree_real * degree_real - 1.0, 1.0) / jnp.maximum(degree_real * degree_real - order_row * order_row, 1.0))
    backward_gain = jnp.sqrt(jnp.maximum((degree_real - 1.0) ** 2 - order_row * order_row, 0.0) / jnp.maximum(4.0 * (degree_real - 1.0) ** 2 - 1.0, 1.0))
    grid_shape = (degree_count, orders.shape[0], lat_count)
    active_full = jnp.broadcast_to(active[:, :, None], grid_shape)
    entry_aa = jnp.where(active_full, forward_gain[:, :, None] * cosine[None, None, :], 1.0)
    entry_ab = jnp.where(active_full, jnp.broadcast_to(-(forward_gain * backward_gain)[:, :, None], grid_shape), 0.0)
    entry_ba = jnp.where(active_full, 1.0, 0.0).astype(jnp.float32)
    entry_bb = jnp.where(active_full, 0.0, 1.0).astype(jnp.float32)
    log_start = jnp.zeros(grid_shape, jnp.float32)
    prefix = lax.associative_scan(combine_steps, (entry_aa, entry_ab, entry_ba, entry_bb, log_start), axis=0)
    values = prefix[0] * jnp.exp(prefix[4] + seed_log[None, :, :])
    kept = degree_ints[:, None, None] >= orders[None, :, None]
    return jnp.where(kept, values, 0.0).transpose(1, 0, 2)

def degree_pass(data, use_weights, to_degrees):
    mem_count = data.shape[0]
    count_in = data.shape[1]
    block_count = MM // MDEV
    blocks = data.reshape(mem_count, count_in, 2, block_count, MDEV, C).transpose(3, 0, 1, 2, 4, 5)
    colatitude = math.pi * (jnp.arange(NLAT, dtype=jnp.float32) + 0.5) / NLAT
    quadrature = math.pi / NLAT * jnp.sin(colatitude)

    def one_block(packed):
        block_id, block_data = packed
        orders = block_id * MDEV + jnp.arange(MDEV, dtype=jnp.int32)
        degree_table = legendre_rows(orders, L, NLAT)
        if use_weights:
            degree_table = degree_table * quadrature[None, None, :]
        degree_table = rounded(degree_table).astype(jnp.float32)
        if to_degrees:
            return rounded(jnp.einsum('aikmc,mli->alkmc', block_data.astype(jnp.float32), degree_table))
        return rounded(jnp.einsum('alkmc,mli->aikmc', block_data.astype(jnp.float32), degree_table))
    result = lax.map(one_block, (jnp.arange(block_count, dtype=jnp.int32), blocks))
    count_out = result.shape[2]
    return result.transpose(1, 2, 3, 0, 4, 5).reshape(mem_count, count_out, 2, MM, C)

def local_forward(fields, filter_basis, neighbor_rows, local_weight):
    weight_real = local_weight.astype(jnp.float32)

    def one_row(row_id):
        sources = jnp.take(fields, neighbor_rows[row_id], axis=1).astype(jnp.float32)
        basis_row = lax.dynamic_index_in_dim(filter_basis, row_id, axis=1, keepdims=False).astype(jnp.float32)
        running = jnp.zeros((KB, sources.shape[0], NLON, C), jnp.float32)
        for offset in range(SUP):
            rolled = jnp.roll(sources, HW - offset, axis=2)
            running = running + jnp.einsum('kb,abfc->kafc', basis_row[:, :, offset], rolled)
        local_terms = rounded(running).astype(jnp.float32)
        return jnp.einsum('kafc,kcd->afd', local_terms, weight_real)
    result = lax.map(one_row, jnp.arange(NLAT, dtype=jnp.int32))
    return result.transpose(1, 0, 2, 3)

def local_backward(grad_mix, filter_basis, neighbor_rows, local_weight):
    weight_real = local_weight.astype(jnp.float32)
    mem_count = grad_mix.shape[0]

    def one_row(running, row_id):
        grad_row = lax.dynamic_index_in_dim(grad_mix, row_id, axis=1, keepdims=False).astype(jnp.float32)
        local_row = rounded(jnp.einsum('afd,kcd->kafc', grad_row, weight_real)).astype(jnp.float32)
        basis_row = lax.dynamic_index_in_dim(filter_basis, row_id, axis=1, keepdims=False).astype(jnp.float32)
        contrib = jnp.zeros((NB, mem_count, NLON, C), jnp.float32)
        for offset in range(SUP):
            rolled = jnp.roll(local_row, offset - HW, axis=2)
            contrib = contrib + jnp.einsum('kb,kafc->bafc', basis_row[:, :, offset], rolled)
        running = running.at[:, neighbor_rows[row_id]].add(contrib.transpose(1, 0, 2, 3))
        return (running, None)
    start_sum = jnp.zeros((mem_count, NLAT, NLON, C), jnp.float32)
    running, _ = lax.scan(one_row, start_sum, jnp.arange(NLAT, dtype=jnp.int32))
    return running

def reference(fields, cotangent, spectral_weight, local_weight, filter_basis, neighbor_rows):
    to_modes, from_modes = mode_tables(NLON, MM)
    to_real = lax.optimization_barrier(to_modes).astype(jnp.float32)
    from_real = lax.optimization_barrier(from_modes).astype(jnp.float32)
    real_part = spectral_weight[:, 0]
    imag_part = spectral_weight[:, 1]
    complex_mix = jnp.stack([jnp.stack([real_part, imag_part], axis=2), jnp.stack([-imag_part, real_part], axis=2)], axis=1).astype(jnp.float32)
    fourier = rounded(jnp.einsum('aifc,fkm->aikmc', fields.astype(jnp.float32), to_real))
    harmonics = degree_pass(fourier, True, True)
    filtered = rounded(jnp.einsum('alkmc,lkcjx->aljmx', harmonics.astype(jnp.float32), complex_mix))
    zonal_modes = degree_pass(filtered, False, False)
    spectral = rounded(jnp.einsum('aikmc,fkm->aifc', zonal_modes.astype(jnp.float32), from_real))
    pre_act = spectral.astype(jnp.float32) + local_forward(fields, filter_basis, neighbor_rows, local_weight)
    activation, derivative = gelu_parts(pre_act)
    block_output = (fields.astype(jnp.float32) + activation).astype(jnp.bfloat16)
    grad_mix = rounded(cotangent.astype(jnp.float32) * derivative)
    grad_zonal = rounded(jnp.einsum('aifc,fkm->aikmc', grad_mix.astype(jnp.float32), from_real))
    grad_filtered = degree_pass(grad_zonal, False, True)
    grad_harmonics = rounded(jnp.einsum('aljmx,lkcjx->alkmc', grad_filtered.astype(jnp.float32), complex_mix))
    grad_fourier = degree_pass(grad_harmonics, True, False)
    grad_spectral = rounded(jnp.einsum('aikmc,fkm->aifc', grad_fourier.astype(jnp.float32), to_real))
    grad_sum = local_backward(grad_mix, filter_basis, neighbor_rows, local_weight)
    input_grad = (cotangent.astype(jnp.float32) + grad_spectral.astype(jnp.float32) + grad_sum).astype(jnp.bfloat16)
    return (block_output, input_grad)
```

```python
import math

import jax
import jax.numpy as jnp
from jax import lax
from jax.experimental import pallas as pl
from jax.experimental.pallas import tpu as pltpu
from jax.sharding import PartitionSpec as P

MDEV = 16
HW = 8


TANH_SCALE = 0.7978845608028654
CUBIC_TERM = 0.044715


def extended(cells, sides, width):
    for axis, dim in sides:
        count = lax.axis_size(axis)
        head = lax.slice_in_dim(cells, 0, width, axis=dim)
        tail = lax.slice_in_dim(cells, cells.shape[dim] - width, cells.shape[dim], axis=dim)
        cells = jnp.concatenate(
            [
                lax.ppermute(tail, axis, [(i, (i + 1) % count) for i in range(count)]),
                cells,
                lax.ppermute(head, axis, [((i + 1) % count, i) for i in range(count)]),
            ],
            axis=dim,
        )
    return cells


def gelu_parts(values):
    tanh_input = TANH_SCALE * (values + CUBIC_TERM * values * values * values)
    hyper = jnp.tanh(tanh_input)
    result = 0.5 * values * (1.0 + hyper)
    derivative = 0.5 * (1.0 + hyper) + 0.5 * values * (1.0 - hyper * hyper) * TANH_SCALE * (
        1.0 + 3.0 * CUBIC_TERM * values * values
    )
    return (result, derivative)


def mode_tables(lon_count, mode_count):
    angles_int = (
        jnp.arange(lon_count, dtype=jnp.int32)[:, None]
        * jnp.arange(mode_count, dtype=jnp.int32)[None, :]
        % lon_count
    )
    angles = angles_int.astype(jnp.float32) * (2.0 * math.pi / lon_count)
    stacked = jnp.stack([jnp.cos(angles), -jnp.sin(angles)], axis=1)
    orders = jnp.arange(mode_count, dtype=jnp.int32)
    factor = jnp.where(orders == 0, 1.0, 2.0).astype(jnp.float32)
    to_modes = (stacked * (2.0 * math.pi / lon_count)).astype(jnp.bfloat16)
    from_modes = (stacked * factor[None, None, :]).astype(jnp.bfloat16)
    return (to_modes, from_modes)


def _legendre_kernel(order_ref, gain_ref, cos_ref, seed_ref, out_ref):
    share, degree_count, _ = out_ref.shape
    cosine = cos_ref[...]
    for o in range(share):
        order = order_ref[o]
        seed = seed_ref[pl.ds(o, 1), :]

        def step(j, carry):
            p_now, p_before, log_scale = carry
            gain = gain_ref[2 * o, j]
            cross = gain_ref[2 * o + 1, j]
            active = j > order
            grown = (gain * cosine) * p_now - cross * p_before
            p_next = jnp.where(active, grown, p_now)
            p_prev = jnp.where(active, p_now, p_before)
            largest = jnp.maximum(jnp.maximum(jnp.abs(p_next), jnp.abs(p_prev)), 1e-30)
            inverse = 1.0 / largest
            p_next = p_next * inverse
            p_prev = p_prev * inverse
            log_scale = log_scale + jnp.log(largest)
            value = jnp.where(j >= order, p_next * jnp.exp(log_scale + seed), 0.0)
            out_ref[o, pl.ds(j, 1), :] = value
            return (p_next, p_prev, log_scale)

        ones = jnp.ones_like(cosine)
        zeros = jnp.zeros_like(cosine)
        lax.fori_loop(0, degree_count, step, (ones, zeros, zeros), unroll=4)


def legendre_rows(orders, degree_count, lat_count):
    colatitude = math.pi * (jnp.arange(lat_count, dtype=jnp.float32) + 0.5) / lat_count
    cosine = jnp.cos(colatitude)
    sine_part = jnp.sin(colatitude)
    order_real = orders.astype(jnp.float32)
    seed_log = 0.5 * (
        jnp.log((2.0 * order_real + 1.0) / (4.0 * math.pi))
        + lax.lgamma(order_real + 0.5)
        - lax.lgamma(order_real + 1.0)
        - 0.5 * math.log(math.pi)
    )
    seed_log = seed_log[:, None] + order_real[:, None] * jnp.log(sine_part)[None, :]
    degree_real = jnp.arange(degree_count, dtype=jnp.float32)[None, :]
    order_col = order_real[:, None]
    forward_gain = jnp.sqrt(
        jnp.maximum(4.0 * degree_real * degree_real - 1.0, 1.0)
        / jnp.maximum(degree_real * degree_real - order_col * order_col, 1.0)
    )
    backward_gain = jnp.sqrt(
        jnp.maximum((degree_real - 1.0) ** 2 - order_col * order_col, 0.0)
        / jnp.maximum(4.0 * (degree_real - 1.0) ** 2 - 1.0, 1.0)
    )
    share = orders.shape[0]
    gains = jnp.stack([forward_gain, forward_gain * backward_gain], axis=1).reshape(
        2 * share, degree_count
    )
    return pl.pallas_call(
        _legendre_kernel,
        out_shape=jax.ShapeDtypeStruct((share, degree_count, lat_count), jnp.float32),
        in_specs=[
            pl.BlockSpec(memory_space=pltpu.SMEM),
            pl.BlockSpec(memory_space=pltpu.SMEM),
            pl.BlockSpec(memory_space=pltpu.VMEM),
            pl.BlockSpec(memory_space=pltpu.VMEM),
        ],
        out_specs=pl.BlockSpec(memory_space=pltpu.VMEM),
        cost_estimate=pl.CostEstimate(
            flops=20 * share * degree_count * lat_count,
            transcendentals=3 * share * degree_count * lat_count,
            bytes_accessed=4 * share * degree_count * lat_count,
        ),
    )(orders.astype(jnp.int32), gains, cosine[None, :], seed_log)


def swap_longitude(blocks):
    return lax.all_to_all(blocks, "lon", split_axis=1, concat_axis=1, tiled=True)


def swap_latitude(blocks):
    return lax.all_to_all(blocks, "lat", split_axis=2, concat_axis=2, tiled=True)


def swap_middle(blocks):
    return swap_latitude(swap_longitude(blocks))


def margin(blocks):
    return extended(blocks, (("lat", 1), ("lon", 2)), HW)


def analysis(field_blocks, dft_table, degree_table, lon_count):
    mem_count, lat_dev, lon_dev, channels = field_blocks.shape
    row_count = lat_dev // lon_count
    grouped = swap_longitude(
        field_blocks.reshape(mem_count, lon_count, row_count, lon_dev, channels)
    )
    fourier = jnp.einsum(
        "aqrfc,qfkjbe->ajbrkec", grouped, dft_table, preferred_element_type=jnp.float32
    ).astype(jnp.bfloat16)
    columns = swap_middle(fourier)
    degrees = jnp.einsum(
        "asprkec,ebdpsr->akbdec", columns, degree_table, preferred_element_type=jnp.float32
    ).astype(jnp.bfloat16)
    return swap_latitude(degrees)


def synthesis(spectrum, degree_table, dft_table):
    mem_count = spectrum.shape[0]
    by_degree = swap_latitude(spectrum)
    zonal_modes = jnp.einsum(
        "akbdec,ebdpsr->asprkec", by_degree, degree_table, preferred_element_type=jnp.float32
    ).astype(jnp.bfloat16)
    by_order = swap_middle(zonal_modes)
    grid_blocks = jnp.einsum(
        "ajbrkec,qfkjbe->aqrfc", by_order, dft_table, preferred_element_type=jnp.float32
    ).astype(jnp.bfloat16)
    returned = swap_longitude(grid_blocks)
    return returned.reshape(
        mem_count, returned.shape[1] * returned.shape[2], returned.shape[3], returned.shape[4]
    )


def per_device(fields, cotangent, spectral_weight, local_weight, filter_basis, neighbor_rows):
    lat_count = lax.axis_size("lat")
    lon_count = lax.axis_size("lon")
    lat_index = lax.axis_index("lat")
    lon_index = lax.axis_index("lon")
    mem_count, lat_dev, lon_dev, channels = fields.shape
    degree_dev = spectral_weight.shape[0]
    kernel_count = filter_basis.shape[0]
    band_count = filter_basis.shape[2]
    support = filter_basis.shape[3]
    half_width = HW
    total_lat = lat_dev * lat_count
    total_lon = lon_dev * lon_count
    mode_dev = MDEV
    order_share = mode_dev // lat_count
    row_count = lat_dev // lon_count
    to_modes, from_modes = mode_tables(total_lon, mode_dev * lon_count)
    table_shape = (lon_count, lon_dev, 2, lon_count, lat_count, order_share)
    to_modes = to_modes.reshape(table_shape)
    from_modes = from_modes.reshape(table_shape)
    orders = (
        lon_index * mode_dev + lat_index * order_share + jnp.arange(order_share, dtype=jnp.int32)
    )
    legendre = legendre_rows(orders, degree_dev * lat_count, total_lat)
    colatitude = math.pi * (jnp.arange(total_lat, dtype=jnp.float32) + 0.5) / total_lat
    quadrature = math.pi / total_lat * jnp.sin(colatitude)
    degree_shape = (order_share, lat_count, degree_dev, lat_count, lon_count, row_count)
    weighted = (legendre * quadrature[None, None, :]).astype(jnp.bfloat16).reshape(degree_shape)
    unweighted = legendre.astype(jnp.bfloat16).reshape(degree_shape)
    real_part = spectral_weight[:, 0]
    imag_part = spectral_weight[:, 1]
    complex_mix = jnp.stack(
        [jnp.stack([real_part, imag_part], axis=2), jnp.stack([-imag_part, real_part], axis=2)],
        axis=1,
    )
    harmonics = analysis(fields, to_modes, weighted, lon_count)
    filtered = jnp.einsum(
        "akbdec,dkcjx->ajbdex", harmonics, complex_mix, preferred_element_type=jnp.float32
    ).astype(jnp.bfloat16)
    spectral = synthesis(filtered, unweighted, from_modes)
    padded = margin(fields)
    row_base = lat_index * lat_dev
    my_rows = lax.dynamic_slice_in_dim(neighbor_rows, row_base, lat_dev, 0)
    my_basis = lax.dynamic_slice_in_dim(filter_basis, row_base, lat_dev, 1)
    wide_count = lon_dev + 2 * half_width
    out_pos = jnp.arange(lon_dev, dtype=jnp.int32)[:, None, None]
    in_pos = jnp.arange(wide_count, dtype=jnp.int32)[None, :, None]
    tap_pos = jnp.arange(support, dtype=jnp.int32)[None, None, :]
    forward_pick = (in_pos - out_pos == tap_pos).astype(jnp.float32)
    local_sum = jnp.zeros((kernel_count, mem_count, lat_dev, lon_dev, channels), jnp.float32)
    for band_index in range(band_count):
        source_rows = my_rows[:, band_index] - row_base + half_width
        sources = jnp.take(padded, source_rows, axis=1)
        banded = jnp.einsum(
            "kis,fts->kift", my_basis[:, :, band_index, :].astype(jnp.float32), forward_pick
        ).astype(jnp.bfloat16)
        local_sum = local_sum + jnp.einsum(
            "kift,aitc->kaifc", banded, sources, preferred_element_type=jnp.float32
        )
    local_terms = local_sum.astype(jnp.bfloat16)
    pre_act = spectral.astype(jnp.float32) + jnp.einsum(
        "kaifc,kcd->aifd", local_terms, local_weight, preferred_element_type=jnp.float32
    )
    activation, derivative = gelu_parts(pre_act)
    block_output = (fields.astype(jnp.float32) + activation).astype(jnp.bfloat16)
    grad_mix = (cotangent.astype(jnp.float32) * derivative).astype(jnp.bfloat16)
    grad_filtered = analysis(grad_mix, from_modes, unweighted, lon_count)
    grad_harmonics = jnp.einsum(
        "ajbdex,dkcjx->akbdec", grad_filtered, complex_mix, preferred_element_type=jnp.float32
    ).astype(jnp.bfloat16)
    grad_spectral = synthesis(grad_harmonics, weighted, to_modes)
    grad_padded = margin(grad_mix)
    grad_local = jnp.einsum(
        "aitd,kcd->kaitc", grad_padded, local_weight, preferred_element_type=jnp.float32
    ).astype(jnp.bfloat16)
    tall_count = lat_dev + 2 * half_width
    padded_rows = row_base - half_width + jnp.arange(tall_count, dtype=jnp.int32)
    inside = (padded_rows >= 0) & (padded_rows < total_lat)
    safe_rows = jnp.clip(padded_rows, 0, total_lat - 1)
    pad_neighbors = jnp.take(neighbor_rows, safe_rows, axis=0)
    pad_basis = jnp.take(filter_basis, safe_rows, axis=1)
    back_pick = (out_pos - in_pos + 2 * half_width == tap_pos).astype(jnp.float32)
    targets = jnp.arange(lat_dev, dtype=jnp.int32)
    grad_sum = jnp.zeros((mem_count, lat_dev, lon_dev, channels), jnp.float32)
    for band_index in range(band_count):
        banded = jnp.einsum(
            "kis,qts->kiqt", pad_basis[:, :, band_index, :].astype(jnp.float32), back_pick
        ).astype(jnp.bfloat16)
        spread = jnp.einsum(
            "kiqt,kaitc->aiqc", banded, grad_local, preferred_element_type=jnp.float32
        )
        placing = (
            (pad_neighbors[:, band_index][None, :] - row_base == targets[:, None]) & inside[None, :]
        ).astype(jnp.float32)
        grad_sum = grad_sum + jnp.einsum(
            "ji,aiqc->ajqc", placing, spread, precision=lax.Precision.HIGHEST
        )
    input_grad = (
        cotangent.astype(jnp.float32) + grad_spectral.astype(jnp.float32) + grad_sum
    ).astype(jnp.bfloat16)
    return (block_output, input_grad)


def solution(mesh):
    in_specs = (
        P(None, "lat", "lon", None),
        P(None, "lat", "lon", None),
        P("lat", None, None, None),
        P(),
        P(),
        P(),
    )
    out_specs = (P(None, "lat", "lon", None), P(None, "lat", "lon", None))
    return jax.shard_map(
        per_device, mesh=mesh, in_specs=in_specs, out_specs=out_specs, check_vma=False
    )
```

```python
import math

import jax
import jax.numpy as jnp
from jax import lax
from jax.experimental import pallas as pl
from jax.experimental.pallas import tpu as pltpu
from jax.sharding import PartitionSpec as P

MDEV = 16
HW = 8


TANH_SCALE = 0.7978845608028654
CUBIC_TERM = 0.044715


def extended(cells, sides, width):
    for axis, dim in sides:
        count = lax.axis_size(axis)
        head = lax.slice_in_dim(cells, 0, width, axis=dim)
        tail = lax.slice_in_dim(cells, cells.shape[dim] - width, cells.shape[dim], axis=dim)
        cells = jnp.concatenate(
            [
                lax.ppermute(tail, axis, [(i, (i + 1) % count) for i in range(count)]),
                cells,
                lax.ppermute(head, axis, [((i + 1) % count, i) for i in range(count)]),
            ],
            axis=dim,
        )
    return cells


def gelu_parts(values):
    tanh_input = TANH_SCALE * (values + CUBIC_TERM * values * values * values)
    hyper = jnp.tanh(tanh_input)
    result = 0.5 * values * (1.0 + hyper)
    derivative = 0.5 * (1.0 + hyper) + 0.5 * values * (1.0 - hyper * hyper) * TANH_SCALE * (
        1.0 + 3.0 * CUBIC_TERM * values * values
    )
    return (result, derivative)


def mode_tables(lon_count, mode_count):
    low_count = 32
    high_count = lon_count // low_count
    step = 2.0 * math.pi / lon_count
    modes = jnp.arange(mode_count, dtype=jnp.int32)[None, :]
    high_int = (jnp.arange(high_count, dtype=jnp.int32)[:, None] * low_count) * modes % lon_count
    low_int = jnp.arange(low_count, dtype=jnp.int32)[:, None] * modes % lon_count
    high_angle = high_int.astype(jnp.float32) * step
    low_angle = low_int.astype(jnp.float32) * step
    high_cos = jnp.cos(high_angle)[:, None, :]
    high_sin = jnp.sin(high_angle)[:, None, :]
    low_cos = jnp.cos(low_angle)[None, :, :]
    low_sin = jnp.sin(low_angle)[None, :, :]
    cosine = (high_cos * low_cos - high_sin * low_sin).reshape(lon_count, mode_count)
    sine = (high_sin * low_cos + high_cos * low_sin).reshape(lon_count, mode_count)
    stacked = jnp.stack([cosine, -sine], axis=1)
    orders = jnp.arange(mode_count, dtype=jnp.int32)
    factor = jnp.where(orders == 0, 1.0, 2.0).astype(jnp.float32)
    to_modes = (stacked * step).astype(jnp.bfloat16)
    from_modes = (stacked * factor[None, None, :]).astype(jnp.bfloat16)
    return (to_modes, from_modes)


def _legendre_kernel(order_ref, gain_ref, cos_ref, seed_ref, out_ref, rows_ref):
    share = out_ref.shape[0]
    degree_count = rows_ref.shape[0]
    cosine = cos_ref[...]
    for o in range(share):
        order = order_ref[o]
        seed = seed_ref[pl.ds(o, 1), :]

        def step(j, carry):
            p_now, p_before, log_scale = carry
            gain = gain_ref[2 * o, j]
            cross = gain_ref[2 * o + 1, j]
            active = j > order
            grown = (gain * cosine) * p_now - cross * p_before
            p_next = jnp.where(active, grown, p_now)
            p_prev = jnp.where(active, p_now, p_before)
            largest = jnp.maximum(jnp.maximum(jnp.abs(p_next), jnp.abs(p_prev)), 1e-30)
            inverse = 1.0 / largest
            p_next = p_next * inverse
            p_prev = p_prev * inverse
            log_scale = log_scale + jnp.log(largest)
            value = jnp.where(j >= order, p_next * jnp.exp(log_scale + seed), 0.0)
            rows_ref[pl.ds(j, 1), :] = value
            return (p_next, p_prev, log_scale)

        ones = jnp.ones_like(cosine)
        zeros = jnp.zeros_like(cosine)
        lax.fori_loop(0, degree_count, step, (ones, zeros, zeros), unroll=4)
        out_ref[o] = rows_ref[...].T


def legendre_rows(orders, degree_count, colatitude):
    lat_count = colatitude.shape[0]
    cosine = jnp.cos(colatitude)
    sine_part = jnp.sin(colatitude)
    order_real = orders.astype(jnp.float32)
    seed_log = 0.5 * (
        jnp.log((2.0 * order_real + 1.0) / (4.0 * math.pi))
        + lax.lgamma(order_real + 0.5)
        - lax.lgamma(order_real + 1.0)
        - 0.5 * math.log(math.pi)
    )
    seed_log = seed_log[:, None] + order_real[:, None] * jnp.log(sine_part)[None, :]
    degree_real = jnp.arange(degree_count, dtype=jnp.float32)[None, :]
    order_col = order_real[:, None]
    forward_gain = jnp.sqrt(
        jnp.maximum(4.0 * degree_real * degree_real - 1.0, 1.0)
        / jnp.maximum(degree_real * degree_real - order_col * order_col, 1.0)
    )
    backward_gain = jnp.sqrt(
        jnp.maximum((degree_real - 1.0) ** 2 - order_col * order_col, 0.0)
        / jnp.maximum(4.0 * (degree_real - 1.0) ** 2 - 1.0, 1.0)
    )
    share = orders.shape[0]
    gains = jnp.stack([forward_gain, forward_gain * backward_gain], axis=1).reshape(
        2 * share, degree_count
    )
    return pl.pallas_call(
        _legendre_kernel,
        out_shape=jax.ShapeDtypeStruct((share, lat_count, degree_count), jnp.float32),
        in_specs=[
            pl.BlockSpec(memory_space=pltpu.SMEM),
            pl.BlockSpec(memory_space=pltpu.SMEM),
            pl.BlockSpec(memory_space=pltpu.VMEM),
            pl.BlockSpec(memory_space=pltpu.VMEM),
        ],
        out_specs=pl.BlockSpec(memory_space=pltpu.VMEM),
        scratch_shapes=[pltpu.VMEM((degree_count, lat_count), jnp.float32)],
        cost_estimate=pl.CostEstimate(
            flops=20 * share * degree_count * lat_count,
            transcendentals=3 * share * degree_count * lat_count,
            bytes_accessed=4 * share * degree_count * lat_count,
        ),
    )(orders.astype(jnp.int32), gains, cosine[None, :], seed_log)


def swap_longitude(blocks):
    return lax.all_to_all(blocks, "lon", split_axis=1, concat_axis=1, tiled=True)


def swap_latitude(blocks):
    return lax.all_to_all(blocks, "lat", split_axis=2, concat_axis=2, tiled=True)


def swap_middle(blocks):
    return swap_latitude(swap_longitude(blocks))


def margin(blocks):
    return extended(blocks, (("lat", 1), ("lon", 2)), HW)


def analysis(field_blocks, dft_table, degree_table, lon_count, lat_count):
    mem_count, lat_dev, lon_dev, channels = field_blocks.shape
    row_count = lat_dev // lon_count
    grouped = swap_longitude(
        field_blocks.reshape(mem_count, lon_count, row_count, lon_dev, channels)
    )
    fourier = jnp.einsum(
        "aqrfc,qfkjbe->ajbrkec", grouped, dft_table, preferred_element_type=jnp.float32
    ).astype(jnp.bfloat16)
    columns = swap_middle(fourier)
    a, s, p, r, k, e, c = columns.shape
    flat = columns.transpose(5, 1, 2, 3, 0, 4, 6).reshape(e, s * p * r, a * k * c)
    degrees = jnp.einsum(
        "eln,eld->edn", flat, degree_table, preferred_element_type=jnp.float32
    ).astype(jnp.bfloat16)
    degree_total = degree_table.shape[2]
    degrees = degrees.reshape(e, lat_count, degree_total // lat_count, a, k, c)
    degrees = degrees.transpose(1, 0, 2, 3, 4, 5)
    return lax.all_to_all(degrees, "lat", split_axis=0, concat_axis=0, tiled=True)


def synthesis(spectrum, degree_table, dft_table, lon_count):
    by_degree = lax.all_to_all(spectrum, "lat", split_axis=0, concat_axis=0, tiled=True)
    b, e, d, a, k, c = by_degree.shape
    flat = by_degree.transpose(1, 0, 2, 3, 4, 5).reshape(e, b * d, a * k * c)
    zonal = jnp.einsum(
        "edn,eld->eln", flat, degree_table, preferred_element_type=jnp.float32
    ).astype(jnp.bfloat16)
    total_lat = zonal.shape[1]
    row_count = total_lat // (lon_count * b)
    zonal_modes = zonal.reshape(e, lon_count, b, row_count, a, k, c).transpose(4, 1, 2, 3, 5, 0, 6)
    by_order = swap_middle(zonal_modes)
    grid_blocks = jnp.einsum(
        "ajbrkec,qfkjbe->aqrfc", by_order, dft_table, preferred_element_type=jnp.float32
    ).astype(jnp.bfloat16)
    returned = swap_longitude(grid_blocks)
    return returned.reshape(
        a, returned.shape[1] * returned.shape[2], returned.shape[3], returned.shape[4]
    )


def per_device(fields, cotangent, spectral_weight, local_weight, filter_basis, neighbor_rows):
    lat_count = lax.axis_size("lat")
    lon_count = lax.axis_size("lon")
    lat_index = lax.axis_index("lat")
    lon_index = lax.axis_index("lon")
    mem_count, lat_dev, lon_dev, channels = fields.shape
    degree_dev = spectral_weight.shape[0]
    kernel_count = filter_basis.shape[0]
    band_count = filter_basis.shape[2]
    support = filter_basis.shape[3]
    half_width = HW
    total_lat = lat_dev * lat_count
    total_lon = lon_dev * lon_count
    mode_dev = MDEV
    order_share = mode_dev // lat_count
    row_count = lat_dev // lon_count
    to_modes, from_modes = mode_tables(total_lon, mode_dev * lon_count)
    table_shape = (lon_count, lon_dev, 2, lon_count, lat_count, order_share)
    to_modes = to_modes.reshape(table_shape)
    from_modes = from_modes.reshape(table_shape)
    orders = (
        lon_index * mode_dev + lat_index * order_share + jnp.arange(order_share, dtype=jnp.int32)
    )
    lat_order = (
        jnp.arange(lat_count, dtype=jnp.int32)[None, :, None] * lat_dev
        + jnp.arange(lon_count, dtype=jnp.int32)[:, None, None] * row_count
        + jnp.arange(row_count, dtype=jnp.int32)[None, None, :]
    ).reshape(total_lat)
    colatitude = math.pi * (lat_order.astype(jnp.float32) + 0.5) / total_lat
    legendre = legendre_rows(orders, degree_dev * lat_count, colatitude)
    quadrature = math.pi / total_lat * jnp.sin(colatitude)
    weighted = (legendre * quadrature[None, :, None]).astype(jnp.bfloat16)
    unweighted = legendre.astype(jnp.bfloat16)
    real_part = spectral_weight[:, 0]
    imag_part = spectral_weight[:, 1]
    complex_mix = jnp.stack(
        [jnp.stack([real_part, imag_part], axis=2), jnp.stack([-imag_part, real_part], axis=2)],
        axis=1,
    )
    harmonics = analysis(fields, to_modes, weighted, lon_count, lat_count)
    filtered = jnp.einsum(
        "pedakc,dkcjx->pedajx", harmonics, complex_mix, preferred_element_type=jnp.float32
    ).astype(jnp.bfloat16)
    spectral = synthesis(filtered, unweighted, from_modes, lon_count)
    padded = margin(fields)
    row_base = lat_index * lat_dev
    my_rows = lax.dynamic_slice_in_dim(neighbor_rows, row_base, lat_dev, 0)
    my_basis = lax.dynamic_slice_in_dim(filter_basis, row_base, lat_dev, 1)
    wide_count = lon_dev + 2 * half_width
    out_pos = jnp.arange(lon_dev, dtype=jnp.int32)[:, None, None]
    in_pos = jnp.arange(wide_count, dtype=jnp.int32)[None, :, None]
    tap_pos = jnp.arange(support, dtype=jnp.int32)[None, None, :]
    forward_pick = (in_pos - out_pos == tap_pos).astype(jnp.float32)
    local_sum = jnp.zeros((kernel_count, mem_count, lat_dev, lon_dev, channels), jnp.float32)
    for band_index in range(band_count):
        source_rows = my_rows[:, band_index] - row_base + half_width
        sources = jnp.take(padded, source_rows, axis=1)
        banded = jnp.einsum(
            "kis,fts->kift", my_basis[:, :, band_index, :].astype(jnp.float32), forward_pick
        ).astype(jnp.bfloat16)
        local_sum = local_sum + jnp.einsum(
            "kift,aitc->kaifc", banded, sources, preferred_element_type=jnp.float32
        )
    local_terms = local_sum.astype(jnp.bfloat16)
    pre_act = spectral.astype(jnp.float32) + jnp.einsum(
        "kaifc,kcd->aifd", local_terms, local_weight, preferred_element_type=jnp.float32
    )
    activation, derivative = gelu_parts(pre_act)
    block_output = (fields.astype(jnp.float32) + activation).astype(jnp.bfloat16)
    grad_mix = (cotangent.astype(jnp.float32) * derivative).astype(jnp.bfloat16)
    grad_filtered = analysis(grad_mix, from_modes, unweighted, lon_count, lat_count)
    grad_harmonics = jnp.einsum(
        "pedajx,dkcjx->pedakc", grad_filtered, complex_mix, preferred_element_type=jnp.float32
    ).astype(jnp.bfloat16)
    grad_spectral = synthesis(grad_harmonics, weighted, to_modes, lon_count)
    grad_padded = margin(grad_mix)
    grad_local = jnp.einsum(
        "aitd,kcd->kaitc", grad_padded, local_weight, preferred_element_type=jnp.float32
    ).astype(jnp.bfloat16)
    tall_count = lat_dev + 2 * half_width
    padded_rows = row_base - half_width + jnp.arange(tall_count, dtype=jnp.int32)
    inside = (padded_rows >= 0) & (padded_rows < total_lat)
    safe_rows = jnp.clip(padded_rows, 0, total_lat - 1)
    pad_neighbors = jnp.take(neighbor_rows, safe_rows, axis=0)
    pad_basis = jnp.take(filter_basis, safe_rows, axis=1)
    back_pick = (out_pos - in_pos + 2 * half_width == tap_pos).astype(jnp.float32)
    targets = jnp.arange(lat_dev, dtype=jnp.int32)
    grad_sum = jnp.zeros((mem_count, lat_dev, lon_dev, channels), jnp.float32)
    for band_index in range(band_count):
        banded = jnp.einsum(
            "kis,qts->kiqt", pad_basis[:, :, band_index, :].astype(jnp.float32), back_pick
        ).astype(jnp.bfloat16)
        spread = jnp.einsum(
            "kiqt,kaitc->aiqc", banded, grad_local, preferred_element_type=jnp.float32
        )
        placing = (
            (pad_neighbors[:, band_index][None, :] - row_base == targets[:, None]) & inside[None, :]
        ).astype(jnp.float32)
        grad_sum = grad_sum + jnp.einsum(
            "ji,aiqc->ajqc", placing, spread, precision=lax.Precision.HIGHEST
        )
    input_grad = (
        cotangent.astype(jnp.float32) + grad_spectral.astype(jnp.float32) + grad_sum
    ).astype(jnp.bfloat16)
    return (block_output, input_grad)


def solution(mesh):
    in_specs = (
        P(None, "lat", "lon", None),
        P(None, "lat", "lon", None),
        P("lat", None, None, None),
        P(),
        P(),
        P(),
    )
    out_specs = (P(None, "lat", "lon", None), P(None, "lat", "lon", None))
    return jax.shard_map(
        per_device, mesh=mesh, in_specs=in_specs, out_specs=out_specs, check_vma=False
    )
```

```python
import math

import jax
import jax.numpy as jnp
from jax import lax
from jax.experimental import pallas as pl
from jax.experimental.pallas import tpu as pltpu
from jax.sharding import PartitionSpec as P

MDEV = 16
HW = 8


TANH_SCALE = 0.7978845608028654
CUBIC_TERM = 0.044715


def extended(cells, sides, width):
    for axis, dim in sides:
        count = lax.axis_size(axis)
        head = lax.slice_in_dim(cells, 0, width, axis=dim)
        tail = lax.slice_in_dim(cells, cells.shape[dim] - width, cells.shape[dim], axis=dim)
        cells = jnp.concatenate(
            [
                lax.ppermute(tail, axis, [(i, (i + 1) % count) for i in range(count)]),
                cells,
                lax.ppermute(head, axis, [((i + 1) % count, i) for i in range(count)]),
            ],
            axis=dim,
        )
    return cells


def gelu_parts(values):
    tanh_input = TANH_SCALE * (values + CUBIC_TERM * values * values * values)
    hyper = jnp.tanh(tanh_input)
    result = 0.5 * values * (1.0 + hyper)
    derivative = 0.5 * (1.0 + hyper) + 0.5 * values * (1.0 - hyper * hyper) * TANH_SCALE * (
        1.0 + 3.0 * CUBIC_TERM * values * values
    )
    return (result, derivative)


def mode_tables(lon_count, mode_count):
    low_count = 32
    high_count = lon_count // low_count
    step = 2.0 * math.pi / lon_count
    modes = jnp.arange(mode_count, dtype=jnp.int32)[None, :]
    high_int = (jnp.arange(high_count, dtype=jnp.int32)[:, None] * low_count) * modes % lon_count
    low_int = jnp.arange(low_count, dtype=jnp.int32)[:, None] * modes % lon_count
    high_angle = high_int.astype(jnp.float32) * step
    low_angle = low_int.astype(jnp.float32) * step
    high_cos, high_sin, low_cos, low_sin = lax.optimization_barrier(
        (jnp.cos(high_angle), jnp.sin(high_angle), jnp.cos(low_angle), jnp.sin(low_angle))
    )
    high_cos = high_cos[:, None, :]
    high_sin = high_sin[:, None, :]
    low_cos = low_cos[None, :, :]
    low_sin = low_sin[None, :, :]
    cosine = (high_cos * low_cos - high_sin * low_sin).reshape(lon_count, mode_count)
    sine = (high_sin * low_cos + high_cos * low_sin).reshape(lon_count, mode_count)
    stacked = jnp.stack([cosine, -sine], axis=1)
    orders = jnp.arange(mode_count, dtype=jnp.int32)
    factor = jnp.where(orders == 0, 1.0, 2.0).astype(jnp.float32)
    to_modes = (stacked * step).astype(jnp.bfloat16)
    from_modes = (stacked * factor[None, None, :]).astype(jnp.bfloat16)
    return (to_modes, from_modes)


def _legendre_kernel(order_ref, gain_ref, cos_ref, seed_ref, out_ref, rows_ref):
    share = out_ref.shape[0]
    degree_count = rows_ref.shape[0]
    cosine = cos_ref[...]
    for o in range(share):
        order = order_ref[o]
        seed = seed_ref[pl.ds(o, 1), :]

        def step(j, carry):
            p_now, p_before, log_scale = carry
            gain = gain_ref[2 * o, j]
            cross = gain_ref[2 * o + 1, j]
            active = j > order
            grown = (gain * cosine) * p_now - cross * p_before
            p_next = jnp.where(active, grown, p_now)
            p_prev = jnp.where(active, p_now, p_before)
            largest = jnp.maximum(jnp.maximum(jnp.abs(p_next), jnp.abs(p_prev)), 1e-30)
            inverse = 1.0 / largest
            p_next = p_next * inverse
            p_prev = p_prev * inverse
            log_scale = log_scale + jnp.log(largest)
            value = jnp.where(j >= order, p_next * jnp.exp(log_scale + seed), 0.0)
            rows_ref[pl.ds(j, 1), :] = value
            return (p_next, p_prev, log_scale)

        ones = jnp.ones_like(cosine)
        zeros = jnp.zeros_like(cosine)
        lax.fori_loop(0, degree_count, step, (ones, zeros, zeros), unroll=4)
        out_ref[o] = rows_ref[...].T


def legendre_rows(orders, degree_count, colatitude):
    lat_count = colatitude.shape[0]
    cosine = jnp.cos(colatitude)
    sine_part = jnp.sin(colatitude)
    order_real = orders.astype(jnp.float32)
    seed_log = 0.5 * (
        jnp.log((2.0 * order_real + 1.0) / (4.0 * math.pi))
        + lax.lgamma(order_real + 0.5)
        - lax.lgamma(order_real + 1.0)
        - 0.5 * math.log(math.pi)
    )
    seed_log = seed_log[:, None] + order_real[:, None] * jnp.log(sine_part)[None, :]
    degree_real = jnp.arange(degree_count, dtype=jnp.float32)[None, :]
    order_col = order_real[:, None]
    forward_gain = jnp.sqrt(
        jnp.maximum(4.0 * degree_real * degree_real - 1.0, 1.0)
        / jnp.maximum(degree_real * degree_real - order_col * order_col, 1.0)
    )
    backward_gain = jnp.sqrt(
        jnp.maximum((degree_real - 1.0) ** 2 - order_col * order_col, 0.0)
        / jnp.maximum(4.0 * (degree_real - 1.0) ** 2 - 1.0, 1.0)
    )
    share = orders.shape[0]
    gains = jnp.stack([forward_gain, forward_gain * backward_gain], axis=1).reshape(
        2 * share, degree_count
    )
    return pl.pallas_call(
        _legendre_kernel,
        out_shape=jax.ShapeDtypeStruct((share, lat_count, degree_count), jnp.float32),
        in_specs=[
            pl.BlockSpec(memory_space=pltpu.SMEM),
            pl.BlockSpec(memory_space=pltpu.SMEM),
            pl.BlockSpec(memory_space=pltpu.VMEM),
            pl.BlockSpec(memory_space=pltpu.VMEM),
        ],
        out_specs=pl.BlockSpec(memory_space=pltpu.VMEM),
        scratch_shapes=[pltpu.VMEM((degree_count, lat_count), jnp.float32)],
        cost_estimate=pl.CostEstimate(
            flops=20 * share * degree_count * lat_count,
            transcendentals=3 * share * degree_count * lat_count,
            bytes_accessed=4 * share * degree_count * lat_count,
        ),
    )(orders.astype(jnp.int32), gains, cosine[None, :], seed_log)


def swap_longitude(blocks):
    return lax.all_to_all(blocks, "lon", split_axis=1, concat_axis=1, tiled=True)


def swap_latitude(blocks):
    return lax.all_to_all(blocks, "lat", split_axis=2, concat_axis=2, tiled=True)


def swap_middle(blocks):
    shape = blocks.shape
    joined = blocks.reshape(shape[0], shape[1] * shape[2], *shape[3:])
    swapped = lax.all_to_all(joined, ("lon", "lat"), split_axis=1, concat_axis=1, tiled=True)
    return swapped.reshape(shape)


def margin(blocks):
    return extended(blocks, (("lat", 1), ("lon", 2)), HW)


def analysis(field_blocks, dft_table, degree_table, lon_count, lat_count):
    mem_count, lat_dev, lon_dev, channels = field_blocks.shape
    row_count = lat_dev // lon_count
    grouped = swap_longitude(
        field_blocks.reshape(mem_count, lon_count, row_count, lon_dev, channels)
    )
    fourier = jnp.einsum(
        "aqrfc,qfkjbe->ajbrkec", grouped, dft_table, preferred_element_type=jnp.float32
    ).astype(jnp.bfloat16)
    columns = swap_middle(fourier)
    a, s, p, r, k, e, c = columns.shape
    flat = columns.transpose(5, 1, 2, 3, 0, 4, 6).reshape(e, s * p * r, a * k * c)
    degrees = jnp.einsum(
        "eln,eld->edn", flat, degree_table, preferred_element_type=jnp.float32
    ).astype(jnp.bfloat16)
    degree_total = degree_table.shape[2]
    degrees = degrees.reshape(e, lat_count, degree_total // lat_count, a, k, c)
    degrees = degrees.transpose(1, 0, 2, 3, 4, 5)
    return lax.all_to_all(degrees, "lat", split_axis=0, concat_axis=0, tiled=True)


def synthesis(spectrum, degree_table, dft_table, lon_count):
    by_degree = lax.all_to_all(spectrum, "lat", split_axis=0, concat_axis=0, tiled=True)
    b, e, d, a, k, c = by_degree.shape
    flat = by_degree.transpose(1, 0, 2, 3, 4, 5).reshape(e, b * d, a * k * c)
    zonal = jnp.einsum(
        "edn,eld->eln", flat, degree_table, preferred_element_type=jnp.float32
    ).astype(jnp.bfloat16)
    total_lat = zonal.shape[1]
    row_count = total_lat // (lon_count * b)
    zonal_modes = zonal.reshape(e, lon_count, b, row_count, a, k, c).transpose(4, 1, 2, 3, 5, 0, 6)
    by_order = swap_middle(zonal_modes)
    grid_blocks = jnp.einsum(
        "ajbrkec,qfkjbe->aqrfc", by_order, dft_table, preferred_element_type=jnp.float32
    ).astype(jnp.bfloat16)
    returned = swap_longitude(grid_blocks)
    return returned.reshape(
        a, returned.shape[1] * returned.shape[2], returned.shape[3], returned.shape[4]
    )


def per_device(fields, cotangent, spectral_weight, local_weight, filter_basis, neighbor_rows):
    lat_count = lax.axis_size("lat")
    lon_count = lax.axis_size("lon")
    lat_index = lax.axis_index("lat")
    lon_index = lax.axis_index("lon")
    mem_count, lat_dev, lon_dev, channels = fields.shape
    degree_dev = spectral_weight.shape[0]
    kernel_count = filter_basis.shape[0]
    band_count = filter_basis.shape[2]
    support = filter_basis.shape[3]
    half_width = HW
    total_lat = lat_dev * lat_count
    total_lon = lon_dev * lon_count
    mode_dev = MDEV
    order_share = mode_dev // lat_count
    row_count = lat_dev // lon_count
    to_modes, from_modes = mode_tables(total_lon, mode_dev * lon_count)
    table_shape = (lon_count, lon_dev, 2, lon_count, lat_count, order_share)
    to_modes = to_modes.reshape(table_shape)
    from_modes = from_modes.reshape(table_shape)
    orders = (
        lon_index * mode_dev + lat_index * order_share + jnp.arange(order_share, dtype=jnp.int32)
    )
    lat_order = (
        jnp.arange(lat_count, dtype=jnp.int32)[None, :, None] * lat_dev
        + jnp.arange(lon_count, dtype=jnp.int32)[:, None, None] * row_count
        + jnp.arange(row_count, dtype=jnp.int32)[None, None, :]
    ).reshape(total_lat)
    colatitude = math.pi * (lat_order.astype(jnp.float32) + 0.5) / total_lat
    legendre = legendre_rows(orders, degree_dev * lat_count, colatitude)
    quadrature = math.pi / total_lat * jnp.sin(colatitude)
    weighted = (legendre * quadrature[None, :, None]).astype(jnp.bfloat16)
    unweighted = legendre.astype(jnp.bfloat16)
    real_part = spectral_weight[:, 0]
    imag_part = spectral_weight[:, 1]
    complex_mix = jnp.stack(
        [jnp.stack([real_part, imag_part], axis=2), jnp.stack([-imag_part, real_part], axis=2)],
        axis=1,
    )
    harmonics = analysis(fields, to_modes, weighted, lon_count, lat_count)
    filtered = jnp.einsum(
        "pedakc,dkcjx->pedajx", harmonics, complex_mix, preferred_element_type=jnp.float32
    ).astype(jnp.bfloat16)
    spectral = synthesis(filtered, unweighted, from_modes, lon_count)
    padded = margin(fields)
    row_base = lat_index * lat_dev
    my_rows = lax.dynamic_slice_in_dim(neighbor_rows, row_base, lat_dev, 0)
    my_basis = lax.dynamic_slice_in_dim(filter_basis, row_base, lat_dev, 1)
    wide_count = lon_dev + 2 * half_width
    out_pos = jnp.arange(lon_dev, dtype=jnp.int32)[:, None, None]
    in_pos = jnp.arange(wide_count, dtype=jnp.int32)[None, :, None]
    tap_pos = jnp.arange(support, dtype=jnp.int32)[None, None, :]
    forward_pick = (in_pos - out_pos == tap_pos).astype(jnp.float32)
    local_sum = jnp.zeros((kernel_count, mem_count, lat_dev, lon_dev, channels), jnp.float32)
    for band_index in range(band_count):
        source_rows = my_rows[:, band_index] - row_base + half_width
        sources = jnp.take(padded, source_rows, axis=1)
        banded = jnp.einsum(
            "kis,fts->kift", my_basis[:, :, band_index, :].astype(jnp.float32), forward_pick
        ).astype(jnp.bfloat16)
        local_sum = local_sum + jnp.einsum(
            "kift,aitc->kaifc", banded, sources, preferred_element_type=jnp.float32
        )
    local_terms = local_sum.astype(jnp.bfloat16)
    pre_act = spectral.astype(jnp.float32) + jnp.einsum(
        "kaifc,kcd->aifd", local_terms, local_weight, preferred_element_type=jnp.float32
    )
    activation, derivative = gelu_parts(pre_act)
    block_output = (fields.astype(jnp.float32) + activation).astype(jnp.bfloat16)
    grad_mix = (cotangent.astype(jnp.float32) * derivative).astype(jnp.bfloat16)
    grad_filtered = analysis(grad_mix, from_modes, unweighted, lon_count, lat_count)
    grad_harmonics = jnp.einsum(
        "pedajx,dkcjx->pedakc", grad_filtered, complex_mix, preferred_element_type=jnp.float32
    ).astype(jnp.bfloat16)
    grad_spectral = synthesis(grad_harmonics, weighted, to_modes, lon_count)
    grad_padded = margin(grad_mix)
    grad_local = jnp.einsum(
        "aitd,kcd->kaitc", grad_padded, local_weight, preferred_element_type=jnp.float32
    ).astype(jnp.bfloat16)
    tall_count = lat_dev + 2 * half_width
    padded_rows = row_base - half_width + jnp.arange(tall_count, dtype=jnp.int32)
    inside = (padded_rows >= 0) & (padded_rows < total_lat)
    safe_rows = jnp.clip(padded_rows, 0, total_lat - 1)
    pad_neighbors = jnp.take(neighbor_rows, safe_rows, axis=0)
    pad_basis = jnp.take(filter_basis, safe_rows, axis=1)
    back_pick = (out_pos - in_pos + 2 * half_width == tap_pos).astype(jnp.float32)
    targets = jnp.arange(lat_dev, dtype=jnp.int32)
    grad_sum = jnp.zeros((mem_count, lat_dev, lon_dev, channels), jnp.float32)
    for band_index in range(band_count):
        banded = jnp.einsum(
            "kis,qts->kiqt", pad_basis[:, :, band_index, :].astype(jnp.float32), back_pick
        ).astype(jnp.bfloat16)
        spread = jnp.einsum(
            "kiqt,kaitc->aiqc", banded, grad_local, preferred_element_type=jnp.float32
        )
        placing = (
            (pad_neighbors[:, band_index][None, :] - row_base == targets[:, None]) & inside[None, :]
        ).astype(jnp.float32)
        grad_sum = grad_sum + jnp.einsum(
            "ji,aiqc->ajqc", placing, spread, precision=lax.Precision.HIGHEST
        )
    input_grad = (
        cotangent.astype(jnp.float32) + grad_spectral.astype(jnp.float32) + grad_sum
    ).astype(jnp.bfloat16)
    return (block_output, input_grad)


def solution(mesh):
    in_specs = (
        P(None, "lat", "lon", None),
        P(None, "lat", "lon", None),
        P("lat", None, None, None),
        P(),
        P(),
        P(),
    )
    out_specs = (P(None, "lat", "lon", None), P(None, "lat", "lon", None))
    return jax.shard_map(
        per_device, mesh=mesh, in_specs=in_specs, out_specs=out_specs, check_vma=False
    )
```

```python
import math

import ml_dtypes
import numpy as np

import jax
import jax.numpy as jnp
from jax import lax
from jax.experimental import pallas as pl
from jax.experimental.pallas import tpu as pltpu
from jax.sharding import PartitionSpec as P

MDEV = 16
HW = 8


TANH_SCALE = 0.7978845608028654
CUBIC_TERM = 0.044715


def extended(cells, sides, width):
    for axis, dim in sides:
        count = lax.axis_size(axis)
        head = lax.slice_in_dim(cells, 0, width, axis=dim)
        tail = lax.slice_in_dim(cells, cells.shape[dim] - width, cells.shape[dim], axis=dim)
        cells = jnp.concatenate(
            [
                lax.ppermute(tail, axis, [(i, (i + 1) % count) for i in range(count)]),
                cells,
                lax.ppermute(head, axis, [((i + 1) % count, i) for i in range(count)]),
            ],
            axis=dim,
        )
    return cells


def gelu_parts(values):
    tanh_input = TANH_SCALE * (values + CUBIC_TERM * values * values * values)
    hyper = jnp.tanh(tanh_input)
    result = 0.5 * values * (1.0 + hyper)
    derivative = 0.5 * (1.0 + hyper) + 0.5 * values * (1.0 - hyper * hyper) * TANH_SCALE * (
        1.0 + 3.0 * CUBIC_TERM * values * values
    )
    return (result, derivative)


def mode_tables(lon_count, mode_count):
    angles_int = (
        np.arange(lon_count, dtype=np.int64)[:, None]
        * np.arange(mode_count, dtype=np.int64)[None, :]
        % lon_count
    )
    angles = angles_int.astype(np.float64) * (2.0 * math.pi / lon_count)
    stacked = np.stack([np.cos(angles), -np.sin(angles)], axis=1)
    factor = np.where(np.arange(mode_count) == 0, 1.0, 2.0)
    to_modes = (stacked * (2.0 * math.pi / lon_count)).astype(ml_dtypes.bfloat16)
    from_modes = (stacked * factor[None, None, :]).astype(ml_dtypes.bfloat16)
    return lax.optimization_barrier((jnp.asarray(to_modes), jnp.asarray(from_modes)))


def _legendre_kernel(order_ref, gain_ref, cos_ref, seed_ref, out_ref, rows_ref):
    share = out_ref.shape[0]
    degree_count = rows_ref.shape[0]
    cosine = cos_ref[...]
    for o in range(share):
        order = order_ref[o]
        seed = seed_ref[pl.ds(o, 1), :]

        def step(j, carry):
            p_now, p_before, log_scale = carry
            gain = gain_ref[2 * o, j]
            cross = gain_ref[2 * o + 1, j]
            active = j > order
            grown = (gain * cosine) * p_now - cross * p_before
            p_next = jnp.where(active, grown, p_now)
            p_prev = jnp.where(active, p_now, p_before)
            largest = jnp.maximum(jnp.maximum(jnp.abs(p_next), jnp.abs(p_prev)), 1e-30)
            inverse = 1.0 / largest
            p_next = p_next * inverse
            p_prev = p_prev * inverse
            log_scale = log_scale + jnp.log(largest)
            value = jnp.where(j >= order, p_next * jnp.exp(log_scale + seed), 0.0)
            rows_ref[pl.ds(j, 1), :] = value
            return (p_next, p_prev, log_scale)

        ones = jnp.ones_like(cosine)
        zeros = jnp.zeros_like(cosine)
        lax.fori_loop(0, degree_count, step, (ones, zeros, zeros), unroll=4)
        out_ref[o] = rows_ref[...].T


def legendre_rows(orders, degree_count, colatitude):
    lat_count = colatitude.shape[0]
    cosine = jnp.cos(colatitude)
    sine_part = jnp.sin(colatitude)
    order_real = orders.astype(jnp.float32)
    seed_log = 0.5 * (
        jnp.log((2.0 * order_real + 1.0) / (4.0 * math.pi))
        + lax.lgamma(order_real + 0.5)
        - lax.lgamma(order_real + 1.0)
        - 0.5 * math.log(math.pi)
    )
    seed_log = seed_log[:, None] + order_real[:, None] * jnp.log(sine_part)[None, :]
    degree_real = jnp.arange(degree_count, dtype=jnp.float32)[None, :]
    order_col = order_real[:, None]
    forward_gain = jnp.sqrt(
        jnp.maximum(4.0 * degree_real * degree_real - 1.0, 1.0)
        / jnp.maximum(degree_real * degree_real - order_col * order_col, 1.0)
    )
    backward_gain = jnp.sqrt(
        jnp.maximum((degree_real - 1.0) ** 2 - order_col * order_col, 0.0)
        / jnp.maximum(4.0 * (degree_real - 1.0) ** 2 - 1.0, 1.0)
    )
    share = orders.shape[0]
    gains = jnp.stack([forward_gain, forward_gain * backward_gain], axis=1).reshape(
        2 * share, degree_count
    )
    return pl.pallas_call(
        _legendre_kernel,
        out_shape=jax.ShapeDtypeStruct((share, lat_count, degree_count), jnp.float32),
        in_specs=[
            pl.BlockSpec(memory_space=pltpu.SMEM),
            pl.BlockSpec(memory_space=pltpu.SMEM),
            pl.BlockSpec(memory_space=pltpu.VMEM),
            pl.BlockSpec(memory_space=pltpu.VMEM),
        ],
        out_specs=pl.BlockSpec(memory_space=pltpu.VMEM),
        scratch_shapes=[pltpu.VMEM((degree_count, lat_count), jnp.float32)],
        cost_estimate=pl.CostEstimate(
            flops=20 * share * degree_count * lat_count,
            transcendentals=3 * share * degree_count * lat_count,
            bytes_accessed=4 * share * degree_count * lat_count,
        ),
    )(orders.astype(jnp.int32), gains, cosine[None, :], seed_log)


def swap_longitude(blocks):
    return lax.all_to_all(blocks, "lon", split_axis=1, concat_axis=1, tiled=True)


def swap_latitude(blocks):
    return lax.all_to_all(blocks, "lat", split_axis=2, concat_axis=2, tiled=True)


def swap_middle(blocks):
    shape = blocks.shape
    joined = blocks.reshape(shape[0], shape[1] * shape[2], *shape[3:])
    swapped = lax.all_to_all(joined, ("lon", "lat"), split_axis=1, concat_axis=1, tiled=True)
    return swapped.reshape(shape)


def margin(blocks):
    return extended(blocks, (("lat", 1), ("lon", 2)), HW)


def analysis(field_blocks, dft_table, degree_table, lon_count, lat_count):
    mem_count, lat_dev, lon_dev, channels = field_blocks.shape
    row_count = lat_dev // lon_count
    grouped = swap_longitude(
        field_blocks.reshape(mem_count, lon_count, row_count, lon_dev, channels)
    )
    fourier = jnp.einsum(
        "aqrfc,qfkjbe->ajbrkec", grouped, dft_table, preferred_element_type=jnp.float32
    ).astype(jnp.bfloat16)
    columns = swap_middle(fourier)
    a, s, p, r, k, e, c = columns.shape
    flat = columns.transpose(5, 1, 2, 3, 0, 4, 6).reshape(e, s * p * r, a * k * c)
    degrees = jnp.einsum(
        "eln,eld->edn", flat, degree_table, preferred_element_type=jnp.float32
    ).astype(jnp.bfloat16)
    degree_total = degree_table.shape[2]
    degrees = degrees.reshape(e, lat_count, degree_total // lat_count, a, k, c)
    degrees = degrees.transpose(1, 0, 2, 3, 4, 5)
    return lax.all_to_all(degrees, "lat", split_axis=0, concat_axis=0, tiled=True)


def synthesis(spectrum, degree_table, dft_table, lon_count):
    by_degree = lax.all_to_all(spectrum, "lat", split_axis=0, concat_axis=0, tiled=True)
    b, e, d, a, k, c = by_degree.shape
    flat = by_degree.transpose(1, 0, 2, 3, 4, 5).reshape(e, b * d, a * k * c)
    zonal = jnp.einsum(
        "edn,eld->eln", flat, degree_table, preferred_element_type=jnp.float32
    ).astype(jnp.bfloat16)
    total_lat = zonal.shape[1]
    row_count = total_lat // (lon_count * b)
    zonal_modes = zonal.reshape(e, lon_count, b, row_count, a, k, c).transpose(4, 1, 2, 3, 5, 0, 6)
    by_order = swap_middle(zonal_modes)
    grid_blocks = jnp.einsum(
        "ajbrkec,qfkjbe->aqrfc", by_order, dft_table, preferred_element_type=jnp.float32
    ).astype(jnp.bfloat16)
    returned = swap_longitude(grid_blocks)
    return returned.reshape(
        a, returned.shape[1] * returned.shape[2], returned.shape[3], returned.shape[4]
    )


def per_device(fields, cotangent, spectral_weight, local_weight, filter_basis, neighbor_rows):
    lat_count = lax.axis_size("lat")
    lon_count = lax.axis_size("lon")
    lat_index = lax.axis_index("lat")
    lon_index = lax.axis_index("lon")
    mem_count, lat_dev, lon_dev, channels = fields.shape
    degree_dev = spectral_weight.shape[0]
    kernel_count = filter_basis.shape[0]
    band_count = filter_basis.shape[2]
    support = filter_basis.shape[3]
    half_width = HW
    total_lat = lat_dev * lat_count
    total_lon = lon_dev * lon_count
    mode_dev = MDEV
    order_share = mode_dev // lat_count
    row_count = lat_dev // lon_count
    to_modes, from_modes = mode_tables(total_lon, mode_dev * lon_count)
    table_shape = (lon_count, lon_dev, 2, lon_count, lat_count, order_share)
    to_modes = to_modes.reshape(table_shape)
    from_modes = from_modes.reshape(table_shape)
    orders = (
        lon_index * mode_dev + lat_index * order_share + jnp.arange(order_share, dtype=jnp.int32)
    )
    lat_order = (
        jnp.arange(lat_count, dtype=jnp.int32)[None, :, None] * lat_dev
        + jnp.arange(lon_count, dtype=jnp.int32)[:, None, None] * row_count
        + jnp.arange(row_count, dtype=jnp.int32)[None, None, :]
    ).reshape(total_lat)
    colatitude = math.pi * (lat_order.astype(jnp.float32) + 0.5) / total_lat
    legendre = legendre_rows(orders, degree_dev * lat_count, colatitude)
    quadrature = math.pi / total_lat * jnp.sin(colatitude)
    weighted = (legendre * quadrature[None, :, None]).astype(jnp.bfloat16)
    unweighted = legendre.astype(jnp.bfloat16)
    real_part = spectral_weight[:, 0]
    imag_part = spectral_weight[:, 1]
    complex_mix = jnp.stack(
        [jnp.stack([real_part, imag_part], axis=2), jnp.stack([-imag_part, real_part], axis=2)],
        axis=1,
    )
    harmonics = analysis(fields, to_modes, weighted, lon_count, lat_count)
    filtered = jnp.einsum(
        "pedakc,dkcjx->pedajx", harmonics, complex_mix, preferred_element_type=jnp.float32
    ).astype(jnp.bfloat16)
    spectral = synthesis(filtered, unweighted, from_modes, lon_count)
    padded = margin(fields)
    row_base = lat_index * lat_dev
    my_rows = lax.dynamic_slice_in_dim(neighbor_rows, row_base, lat_dev, 0)
    my_basis = lax.dynamic_slice_in_dim(filter_basis, row_base, lat_dev, 1)
    wide_count = lon_dev + 2 * half_width
    out_pos = jnp.arange(lon_dev, dtype=jnp.int32)[:, None, None]
    in_pos = jnp.arange(wide_count, dtype=jnp.int32)[None, :, None]
    tap_pos = jnp.arange(support, dtype=jnp.int32)[None, None, :]
    forward_pick = (in_pos - out_pos == tap_pos).astype(jnp.float32)
    local_sum = jnp.zeros((kernel_count, mem_count, lat_dev, lon_dev, channels), jnp.float32)
    for band_index in range(band_count):
        source_rows = my_rows[:, band_index] - row_base + half_width
        sources = jnp.take(padded, source_rows, axis=1)
        banded = jnp.einsum(
            "kis,fts->kift", my_basis[:, :, band_index, :].astype(jnp.float32), forward_pick
        ).astype(jnp.bfloat16)
        local_sum = local_sum + jnp.einsum(
            "kift,aitc->kaifc", banded, sources, preferred_element_type=jnp.float32
        )
    local_terms = local_sum.astype(jnp.bfloat16)
    pre_act = spectral.astype(jnp.float32) + jnp.einsum(
        "kaifc,kcd->aifd", local_terms, local_weight, preferred_element_type=jnp.float32
    )
    activation, derivative = gelu_parts(pre_act)
    block_output = (fields.astype(jnp.float32) + activation).astype(jnp.bfloat16)
    grad_mix = (cotangent.astype(jnp.float32) * derivative).astype(jnp.bfloat16)
    grad_filtered = analysis(grad_mix, from_modes, unweighted, lon_count, lat_count)
    grad_harmonics = jnp.einsum(
        "pedajx,dkcjx->pedakc", grad_filtered, complex_mix, preferred_element_type=jnp.float32
    ).astype(jnp.bfloat16)
    grad_spectral = synthesis(grad_harmonics, weighted, to_modes, lon_count)
    grad_padded = margin(grad_mix)
    grad_local = jnp.einsum(
        "aitd,kcd->kaitc", grad_padded, local_weight, preferred_element_type=jnp.float32
    ).astype(jnp.bfloat16)
    tall_count = lat_dev + 2 * half_width
    padded_rows = row_base - half_width + jnp.arange(tall_count, dtype=jnp.int32)
    inside = (padded_rows >= 0) & (padded_rows < total_lat)
    safe_rows = jnp.clip(padded_rows, 0, total_lat - 1)
    pad_neighbors = jnp.take(neighbor_rows, safe_rows, axis=0)
    pad_basis = jnp.take(filter_basis, safe_rows, axis=1)
    back_pick = (out_pos - in_pos + 2 * half_width == tap_pos).astype(jnp.float32)
    targets = jnp.arange(lat_dev, dtype=jnp.int32)
    grad_sum = jnp.zeros((mem_count, lat_dev, lon_dev, channels), jnp.float32)
    for band_index in range(band_count):
        banded = jnp.einsum(
            "kis,qts->kiqt", pad_basis[:, :, band_index, :].astype(jnp.float32), back_pick
        ).astype(jnp.bfloat16)
        spread = jnp.einsum(
            "kiqt,kaitc->aiqc", banded, grad_local, preferred_element_type=jnp.float32
        )
        placing = (
            (pad_neighbors[:, band_index][None, :] - row_base == targets[:, None]) & inside[None, :]
        ).astype(jnp.float32)
        grad_sum = grad_sum + jnp.einsum(
            "ji,aiqc->ajqc", placing, spread, precision=lax.Precision.HIGHEST
        )
    input_grad = (
        cotangent.astype(jnp.float32) + grad_spectral.astype(jnp.float32) + grad_sum
    ).astype(jnp.bfloat16)
    return (block_output, input_grad)


def solution(mesh):
    in_specs = (
        P(None, "lat", "lon", None),
        P(None, "lat", "lon", None),
        P("lat", None, None, None),
        P(),
        P(),
        P(),
    )
    out_specs = (P(None, "lat", "lon", None), P(None, "lat", "lon", None))
    return jax.shard_map(
        per_device, mesh=mesh, in_specs=in_specs, out_specs=out_specs, check_vma=False
    )
```

```python
import math

import ml_dtypes
import numpy as np

import jax
import jax.numpy as jnp
from jax import lax
from jax.experimental import pallas as pl
from jax.experimental.pallas import tpu as pltpu
from jax.sharding import PartitionSpec as P

MDEV = 16
HW = 8


TANH_SCALE = 0.7978845608028654
CUBIC_TERM = 0.044715


def extended(cells, sides, width):
    for axis, dim in sides:
        count = lax.axis_size(axis)
        head = lax.slice_in_dim(cells, 0, width, axis=dim)
        tail = lax.slice_in_dim(cells, cells.shape[dim] - width, cells.shape[dim], axis=dim)
        cells = jnp.concatenate(
            [
                lax.ppermute(tail, axis, [(i, (i + 1) % count) for i in range(count)]),
                cells,
                lax.ppermute(head, axis, [((i + 1) % count, i) for i in range(count)]),
            ],
            axis=dim,
        )
    return cells


def gelu_parts(values):
    tanh_input = TANH_SCALE * (values + CUBIC_TERM * values * values * values)
    hyper = jnp.tanh(tanh_input)
    result = 0.5 * values * (1.0 + hyper)
    derivative = 0.5 * (1.0 + hyper) + 0.5 * values * (1.0 - hyper * hyper) * TANH_SCALE * (
        1.0 + 3.0 * CUBIC_TERM * values * values
    )
    return (result, derivative)


def mode_tables(lon_count, mode_count):
    angles_int = (
        np.arange(lon_count, dtype=np.int64)[:, None]
        * np.arange(mode_count, dtype=np.int64)[None, :]
        % lon_count
    )
    angles = angles_int.astype(np.float64) * (2.0 * math.pi / lon_count)
    stacked = np.stack([np.cos(angles), -np.sin(angles)], axis=1)
    factor = np.where(np.arange(mode_count) == 0, 1.0, 2.0)
    to_modes = (stacked * (2.0 * math.pi / lon_count)).astype(ml_dtypes.bfloat16)
    from_modes = (stacked * factor[None, None, :]).astype(ml_dtypes.bfloat16)
    return lax.optimization_barrier((jnp.asarray(to_modes), jnp.asarray(from_modes)))


def _legendre_kernel(order_ref, gain_ref, cos_ref, seed_ref, out_ref, rows_ref):
    share = out_ref.shape[0]
    degree_count = rows_ref.shape[0]
    cosine = cos_ref[...]
    for o in range(share):
        order = order_ref[o]
        seed = seed_ref[pl.ds(o, 1), :]

        def step(j, carry):
            p_now, p_before, log_scale = carry
            gain = gain_ref[2 * o, j]
            cross = gain_ref[2 * o + 1, j]
            active = j > order
            grown = (gain * cosine) * p_now - cross * p_before
            p_next = jnp.where(active, grown, p_now)
            p_prev = jnp.where(active, p_now, p_before)
            largest = jnp.maximum(jnp.maximum(jnp.abs(p_next), jnp.abs(p_prev)), 1e-30)
            inverse = 1.0 / largest
            p_next = p_next * inverse
            p_prev = p_prev * inverse
            log_scale = log_scale + jnp.log(largest)
            value = jnp.where(j >= order, p_next * jnp.exp(log_scale + seed), 0.0)
            rows_ref[pl.ds(j, 1), :] = value
            return (p_next, p_prev, log_scale)

        ones = jnp.ones_like(cosine)
        zeros = jnp.zeros_like(cosine)
        lax.fori_loop(0, degree_count, step, (ones, zeros, zeros), unroll=4)
        out_ref[o] = rows_ref[...].T


def legendre_rows(orders, degree_count, colatitude):
    lat_count = colatitude.shape[0]
    cosine = jnp.cos(colatitude)
    sine_part = jnp.sin(colatitude)
    order_real = orders.astype(jnp.float32)
    seed_log = 0.5 * (
        jnp.log((2.0 * order_real + 1.0) / (4.0 * math.pi))
        + lax.lgamma(order_real + 0.5)
        - lax.lgamma(order_real + 1.0)
        - 0.5 * math.log(math.pi)
    )
    seed_log = seed_log[:, None] + order_real[:, None] * jnp.log(sine_part)[None, :]
    degree_real = jnp.arange(degree_count, dtype=jnp.float32)[None, :]
    order_col = order_real[:, None]
    forward_gain = jnp.sqrt(
        jnp.maximum(4.0 * degree_real * degree_real - 1.0, 1.0)
        / jnp.maximum(degree_real * degree_real - order_col * order_col, 1.0)
    )
    backward_gain = jnp.sqrt(
        jnp.maximum((degree_real - 1.0) ** 2 - order_col * order_col, 0.0)
        / jnp.maximum(4.0 * (degree_real - 1.0) ** 2 - 1.0, 1.0)
    )
    share = orders.shape[0]
    gains = jnp.stack([forward_gain, forward_gain * backward_gain], axis=1).reshape(
        2 * share, degree_count
    )
    return pl.pallas_call(
        _legendre_kernel,
        out_shape=jax.ShapeDtypeStruct((share, lat_count, degree_count), jnp.float32),
        in_specs=[
            pl.BlockSpec(memory_space=pltpu.SMEM),
            pl.BlockSpec(memory_space=pltpu.SMEM),
            pl.BlockSpec(memory_space=pltpu.VMEM),
            pl.BlockSpec(memory_space=pltpu.VMEM),
        ],
        out_specs=pl.BlockSpec(memory_space=pltpu.VMEM),
        scratch_shapes=[pltpu.VMEM((degree_count, lat_count), jnp.float32)],
        cost_estimate=pl.CostEstimate(
            flops=20 * share * degree_count * lat_count,
            transcendentals=3 * share * degree_count * lat_count,
            bytes_accessed=4 * share * degree_count * lat_count,
        ),
    )(orders.astype(jnp.int32), gains, cosine[None, :], seed_log)


def swap_longitude(blocks):
    return lax.all_to_all(blocks, "lon", split_axis=1, concat_axis=1, tiled=True)


def swap_latitude(blocks):
    return lax.all_to_all(blocks, "lat", split_axis=2, concat_axis=2, tiled=True)


def swap_middle(blocks):
    shape = blocks.shape
    joined = blocks.reshape(shape[0], shape[1] * shape[2], *shape[3:])
    swapped = lax.all_to_all(joined, ("lon", "lat"), split_axis=1, concat_axis=1, tiled=True)
    return swapped.reshape(shape)


def margin(blocks):
    return extended(blocks, (("lat", 1), ("lon", 2)), HW)


def analysis(field_blocks, dft_table, degree_table, lon_count, lat_count):
    mem_count, lat_dev, lon_dev, channels = field_blocks.shape
    row_count = lat_dev // lon_count
    grouped = swap_longitude(
        field_blocks.reshape(mem_count, lon_count, row_count, lon_dev, channels)
    )
    fourier = jnp.einsum(
        "aqrfc,qfkjbe->ajbrkec", grouped, dft_table, preferred_element_type=jnp.float32
    ).astype(jnp.bfloat16)
    columns = swap_middle(fourier)
    if callable(degree_table):
        degree_table = degree_table(fourier)
    a, s, p, r, k, e, c = columns.shape
    flat = columns.transpose(5, 1, 2, 3, 0, 4, 6).reshape(e, s * p * r, a * k * c)
    degrees = jnp.einsum(
        "eln,eld->edn", flat, degree_table, preferred_element_type=jnp.float32
    ).astype(jnp.bfloat16)
    degree_total = degree_table.shape[2]
    degrees = degrees.reshape(e, lat_count, degree_total // lat_count, a, k, c)
    degrees = degrees.transpose(1, 0, 2, 3, 4, 5)
    return lax.all_to_all(degrees, "lat", split_axis=0, concat_axis=0, tiled=True)


def synthesis(spectrum, degree_table, dft_table, lon_count):
    by_degree = lax.all_to_all(spectrum, "lat", split_axis=0, concat_axis=0, tiled=True)
    b, e, d, a, k, c = by_degree.shape
    flat = by_degree.transpose(1, 0, 2, 3, 4, 5).reshape(e, b * d, a * k * c)
    zonal = jnp.einsum(
        "edn,eld->eln", flat, degree_table, preferred_element_type=jnp.float32
    ).astype(jnp.bfloat16)
    total_lat = zonal.shape[1]
    row_count = total_lat // (lon_count * b)
    zonal_modes = zonal.reshape(e, lon_count, b, row_count, a, k, c).transpose(4, 1, 2, 3, 5, 0, 6)
    by_order = swap_middle(zonal_modes)
    grid_blocks = jnp.einsum(
        "ajbrkec,qfkjbe->aqrfc", by_order, dft_table, preferred_element_type=jnp.float32
    ).astype(jnp.bfloat16)
    returned = swap_longitude(grid_blocks)
    return returned.reshape(
        a, returned.shape[1] * returned.shape[2], returned.shape[3], returned.shape[4]
    )


def per_device(fields, cotangent, spectral_weight, local_weight, filter_basis, neighbor_rows):
    lat_count = lax.axis_size("lat")
    lon_count = lax.axis_size("lon")
    lat_index = lax.axis_index("lat")
    lon_index = lax.axis_index("lon")
    mem_count, lat_dev, lon_dev, channels = fields.shape
    degree_dev = spectral_weight.shape[0]
    kernel_count = filter_basis.shape[0]
    band_count = filter_basis.shape[2]
    support = filter_basis.shape[3]
    half_width = HW
    total_lat = lat_dev * lat_count
    total_lon = lon_dev * lon_count
    mode_dev = MDEV
    order_share = mode_dev // lat_count
    row_count = lat_dev // lon_count
    to_modes, from_modes = mode_tables(total_lon, mode_dev * lon_count)
    table_shape = (lon_count, lon_dev, 2, lon_count, lat_count, order_share)
    to_modes = to_modes.reshape(table_shape)
    from_modes = from_modes.reshape(table_shape)
    orders = (
        lon_index * mode_dev + lat_index * order_share + jnp.arange(order_share, dtype=jnp.int32)
    )
    lat_order = (
        jnp.arange(lat_count, dtype=jnp.int32)[None, :, None] * lat_dev
        + jnp.arange(lon_count, dtype=jnp.int32)[:, None, None] * row_count
        + jnp.arange(row_count, dtype=jnp.int32)[None, None, :]
    ).reshape(total_lat)
    colatitude = math.pi * (lat_order.astype(jnp.float32) + 0.5) / total_lat
    tables = {}

    def weighted_after(gate):
        _, colat = lax.optimization_barrier((gate, colatitude))
        legendre = legendre_rows(orders, degree_dev * lat_count, colat)
        quadrature = math.pi / total_lat * jnp.sin(colat)
        tables["weighted"] = (legendre * quadrature[None, :, None]).astype(jnp.bfloat16)
        tables["unweighted"] = legendre.astype(jnp.bfloat16)
        return tables["weighted"]

    real_part = spectral_weight[:, 0]
    imag_part = spectral_weight[:, 1]
    complex_mix = jnp.stack(
        [jnp.stack([real_part, imag_part], axis=2), jnp.stack([-imag_part, real_part], axis=2)],
        axis=1,
    )
    harmonics = analysis(fields, to_modes, weighted_after, lon_count, lat_count)
    weighted = tables["weighted"]
    unweighted = tables["unweighted"]
    filtered = jnp.einsum(
        "pedakc,dkcjx->pedajx", harmonics, complex_mix, preferred_element_type=jnp.float32
    ).astype(jnp.bfloat16)
    spectral = synthesis(filtered, unweighted, from_modes, lon_count)
    padded = margin(fields)
    row_base = lat_index * lat_dev
    my_rows = lax.dynamic_slice_in_dim(neighbor_rows, row_base, lat_dev, 0)
    my_basis = lax.dynamic_slice_in_dim(filter_basis, row_base, lat_dev, 1)
    wide_count = lon_dev + 2 * half_width
    out_pos = jnp.arange(lon_dev, dtype=jnp.int32)[:, None, None]
    in_pos = jnp.arange(wide_count, dtype=jnp.int32)[None, :, None]
    tap_pos = jnp.arange(support, dtype=jnp.int32)[None, None, :]
    forward_pick = (in_pos - out_pos == tap_pos).astype(jnp.float32)
    local_sum = jnp.zeros((kernel_count, mem_count, lat_dev, lon_dev, channels), jnp.float32)
    for band_index in range(band_count):
        source_rows = my_rows[:, band_index] - row_base + half_width
        sources = jnp.take(padded, source_rows, axis=1)
        banded = jnp.einsum(
            "kis,fts->kift", my_basis[:, :, band_index, :].astype(jnp.float32), forward_pick
        ).astype(jnp.bfloat16)
        local_sum = local_sum + jnp.einsum(
            "kift,aitc->kaifc", banded, sources, preferred_element_type=jnp.float32
        )
    local_terms = local_sum.astype(jnp.bfloat16)
    pre_act = spectral.astype(jnp.float32) + jnp.einsum(
        "kaifc,kcd->aifd", local_terms, local_weight, preferred_element_type=jnp.float32
    )
    activation, derivative = gelu_parts(pre_act)
    block_output = (fields.astype(jnp.float32) + activation).astype(jnp.bfloat16)
    grad_mix = (cotangent.astype(jnp.float32) * derivative).astype(jnp.bfloat16)
    grad_filtered = analysis(grad_mix, from_modes, unweighted, lon_count, lat_count)
    grad_harmonics = jnp.einsum(
        "pedajx,dkcjx->pedakc", grad_filtered, complex_mix, preferred_element_type=jnp.float32
    ).astype(jnp.bfloat16)
    grad_spectral = synthesis(grad_harmonics, weighted, to_modes, lon_count)
    grad_padded = margin(grad_mix)
    grad_local = jnp.einsum(
        "aitd,kcd->kaitc", grad_padded, local_weight, preferred_element_type=jnp.float32
    ).astype(jnp.bfloat16)
    tall_count = lat_dev + 2 * half_width
    padded_rows = row_base - half_width + jnp.arange(tall_count, dtype=jnp.int32)
    inside = (padded_rows >= 0) & (padded_rows < total_lat)
    safe_rows = jnp.clip(padded_rows, 0, total_lat - 1)
    pad_neighbors = jnp.take(neighbor_rows, safe_rows, axis=0)
    pad_basis = jnp.take(filter_basis, safe_rows, axis=1)
    back_pick = (out_pos - in_pos + 2 * half_width == tap_pos).astype(jnp.float32)
    targets = jnp.arange(lat_dev, dtype=jnp.int32)
    grad_sum = jnp.zeros((mem_count, lat_dev, lon_dev, channels), jnp.float32)
    for band_index in range(band_count):
        banded = jnp.einsum(
            "kis,qts->kiqt", pad_basis[:, :, band_index, :].astype(jnp.float32), back_pick
        ).astype(jnp.bfloat16)
        spread = jnp.einsum(
            "kiqt,kaitc->aiqc", banded, grad_local, preferred_element_type=jnp.float32
        )
        placing = (
            (pad_neighbors[:, band_index][None, :] - row_base == targets[:, None]) & inside[None, :]
        ).astype(jnp.float32)
        grad_sum = grad_sum + jnp.einsum(
            "ji,aiqc->ajqc", placing, spread, precision=lax.Precision.HIGHEST
        )
    input_grad = (
        cotangent.astype(jnp.float32) + grad_spectral.astype(jnp.float32) + grad_sum
    ).astype(jnp.bfloat16)
    return (block_output, input_grad)


def solution(mesh):
    in_specs = (
        P(None, "lat", "lon", None),
        P(None, "lat", "lon", None),
        P("lat", None, None, None),
        P(),
        P(),
        P(),
    )
    out_specs = (P(None, "lat", "lon", None), P(None, "lat", "lon", None))
    return jax.shard_map(
        per_device, mesh=mesh, in_specs=in_specs, out_specs=out_specs, check_vma=False
    )
```

```python
import math

import ml_dtypes
import numpy as np

import jax
import jax.numpy as jnp
from jax import lax
from jax.experimental import pallas as pl
from jax.experimental.pallas import tpu as pltpu
from jax.sharding import PartitionSpec as P

MDEV = 16
HW = 8


TANH_SCALE = 0.7978845608028654
CUBIC_TERM = 0.044715


def extended(cells, sides, width):
    for axis, dim in sides:
        count = lax.axis_size(axis)
        head = lax.slice_in_dim(cells, 0, width, axis=dim)
        tail = lax.slice_in_dim(cells, cells.shape[dim] - width, cells.shape[dim], axis=dim)
        cells = jnp.concatenate(
            [
                lax.ppermute(tail, axis, [(i, (i + 1) % count) for i in range(count)]),
                cells,
                lax.ppermute(head, axis, [((i + 1) % count, i) for i in range(count)]),
            ],
            axis=dim,
        )
    return cells


def gelu_parts(values):
    tanh_input = TANH_SCALE * (values + CUBIC_TERM * values * values * values)
    hyper = jnp.tanh(tanh_input)
    result = 0.5 * values * (1.0 + hyper)
    derivative = 0.5 * (1.0 + hyper) + 0.5 * values * (1.0 - hyper * hyper) * TANH_SCALE * (
        1.0 + 3.0 * CUBIC_TERM * values * values
    )
    return (result, derivative)


def mode_tables(lon_count, mode_count):
    angles_int = (
        np.arange(lon_count, dtype=np.int64)[:, None]
        * np.arange(mode_count, dtype=np.int64)[None, :]
        % lon_count
    )
    angles = angles_int.astype(np.float64) * (2.0 * math.pi / lon_count)
    stacked = np.stack([np.cos(angles), -np.sin(angles)], axis=1)
    factor = np.where(np.arange(mode_count) == 0, 1.0, 2.0)
    to_modes = (stacked * (2.0 * math.pi / lon_count)).astype(ml_dtypes.bfloat16)
    from_modes = (stacked * factor[None, None, :]).astype(ml_dtypes.bfloat16)
    return lax.optimization_barrier((jnp.asarray(to_modes), jnp.asarray(from_modes)))


def _legendre_kernel(order_ref, gain_ref, cos_ref, seed_ref, out_ref, rows_ref):
    share = out_ref.shape[0]
    degree_count = rows_ref.shape[0]
    cosine = cos_ref[...]
    for o in range(share):
        order = order_ref[o]
        seed = seed_ref[pl.ds(o, 1), :]

        def step(j, carry):
            p_now, p_before, log_scale = carry
            gain = gain_ref[2 * o, j]
            cross = gain_ref[2 * o + 1, j]
            active = j > order
            grown = (gain * cosine) * p_now - cross * p_before
            p_next = jnp.where(active, grown, p_now)
            p_prev = jnp.where(active, p_now, p_before)
            largest = jnp.maximum(jnp.maximum(jnp.abs(p_next), jnp.abs(p_prev)), 1e-30)
            inverse = 1.0 / largest
            p_next = p_next * inverse
            p_prev = p_prev * inverse
            log_scale = log_scale + jnp.log(largest)
            value = jnp.where(j >= order, p_next * jnp.exp(log_scale + seed), 0.0)
            rows_ref[pl.ds(j, 1), :] = value
            return (p_next, p_prev, log_scale)

        ones = jnp.ones_like(cosine)
        zeros = jnp.zeros_like(cosine)
        lax.fori_loop(0, degree_count, step, (ones, zeros, zeros), unroll=4)
        out_ref[o] = rows_ref[...].T


def legendre_rows(orders, degree_count, colatitude):
    lat_count = colatitude.shape[0]
    cosine = jnp.cos(colatitude)
    sine_part = jnp.sin(colatitude)
    order_real = orders.astype(jnp.float32)
    seed_log = 0.5 * (
        jnp.log((2.0 * order_real + 1.0) / (4.0 * math.pi))
        + lax.lgamma(order_real + 0.5)
        - lax.lgamma(order_real + 1.0)
        - 0.5 * math.log(math.pi)
    )
    seed_log = seed_log[:, None] + order_real[:, None] * jnp.log(sine_part)[None, :]
    degree_real = jnp.arange(degree_count, dtype=jnp.float32)[None, :]
    order_col = order_real[:, None]
    forward_gain = jnp.sqrt(
        jnp.maximum(4.0 * degree_real * degree_real - 1.0, 1.0)
        / jnp.maximum(degree_real * degree_real - order_col * order_col, 1.0)
    )
    backward_gain = jnp.sqrt(
        jnp.maximum((degree_real - 1.0) ** 2 - order_col * order_col, 0.0)
        / jnp.maximum(4.0 * (degree_real - 1.0) ** 2 - 1.0, 1.0)
    )
    share = orders.shape[0]
    gains = jnp.stack([forward_gain, forward_gain * backward_gain], axis=1).reshape(
        2 * share, degree_count
    )
    return pl.pallas_call(
        _legendre_kernel,
        out_shape=jax.ShapeDtypeStruct((share, lat_count, degree_count), jnp.float32),
        in_specs=[
            pl.BlockSpec(memory_space=pltpu.SMEM),
            pl.BlockSpec(memory_space=pltpu.SMEM),
            pl.BlockSpec(memory_space=pltpu.VMEM),
            pl.BlockSpec(memory_space=pltpu.VMEM),
        ],
        out_specs=pl.BlockSpec(memory_space=pltpu.VMEM),
        scratch_shapes=[pltpu.VMEM((degree_count, lat_count), jnp.float32)],
        cost_estimate=pl.CostEstimate(
            flops=20 * share * degree_count * lat_count,
            transcendentals=3 * share * degree_count * lat_count,
            bytes_accessed=4 * share * degree_count * lat_count,
        ),
    )(orders.astype(jnp.int32), gains, cosine[None, :], seed_log)


def swap_longitude(blocks):
    return lax.all_to_all(blocks, "lon", split_axis=1, concat_axis=1, tiled=True)


def swap_latitude(blocks):
    return lax.all_to_all(blocks, "lat", split_axis=2, concat_axis=2, tiled=True)


def swap_middle(blocks):
    shape = blocks.shape
    joined = blocks.reshape(shape[0], shape[1] * shape[2], *shape[3:])
    swapped = lax.all_to_all(joined, ("lon", "lat"), split_axis=1, concat_axis=1, tiled=True)
    return swapped.reshape(shape)


def margin(blocks):
    return extended(blocks, (("lat", 1), ("lon", 2)), HW)


def analysis(field_blocks, dft_table, degree_table, lon_count, lat_count):
    mem_count, lat_dev, lon_dev, channels = field_blocks.shape
    row_count = lat_dev // lon_count
    grouped = swap_longitude(
        field_blocks.reshape(mem_count, lon_count, row_count, lon_dev, channels)
    )
    fourier = jnp.einsum(
        "aqrfc,qfkjbe->ajbrkec", grouped, dft_table, preferred_element_type=jnp.float32
    ).astype(jnp.bfloat16)
    columns = swap_middle(fourier)
    if callable(degree_table):
        degree_table = degree_table(fourier)
    a, s, p, r, k, e, c = columns.shape
    flat = columns.transpose(5, 1, 2, 3, 0, 4, 6).reshape(e, s * p * r, a * k * c)
    degrees = jnp.einsum(
        "eln,eld->edn", flat, degree_table, preferred_element_type=jnp.float32
    ).astype(jnp.bfloat16)
    degree_total = degree_table.shape[2]
    degrees = degrees.reshape(e, lat_count, degree_total // lat_count, a, k, c)
    degrees = degrees.transpose(1, 0, 2, 3, 4, 5)
    return lax.all_to_all(degrees, "lat", split_axis=0, concat_axis=0, tiled=True)


def synthesis(spectrum, degree_table, dft_table, lon_count):
    by_degree = lax.all_to_all(spectrum, "lat", split_axis=0, concat_axis=0, tiled=True)
    b, e, d, a, k, c = by_degree.shape
    flat = by_degree.transpose(1, 0, 2, 3, 4, 5).reshape(e, b * d, a * k * c)
    zonal = jnp.einsum(
        "edn,eld->eln", flat, degree_table, preferred_element_type=jnp.float32
    ).astype(jnp.bfloat16)
    total_lat = zonal.shape[1]
    row_count = total_lat // (lon_count * b)
    zonal_modes = zonal.reshape(e, lon_count, b, row_count, a, k, c).transpose(4, 1, 2, 3, 5, 0, 6)
    by_order = swap_middle(zonal_modes)
    grid_blocks = jnp.einsum(
        "ajbrkec,qfkjbe->aqrfc", by_order, dft_table, preferred_element_type=jnp.float32
    ).astype(jnp.bfloat16)
    returned = swap_longitude(grid_blocks)
    return returned.reshape(
        a, returned.shape[1] * returned.shape[2], returned.shape[3], returned.shape[4]
    )


def per_device(fields, cotangent, spectral_weight, local_weight, filter_basis, neighbor_rows):
    lat_count = lax.axis_size("lat")
    lon_count = lax.axis_size("lon")
    lat_index = lax.axis_index("lat")
    lon_index = lax.axis_index("lon")
    mem_count, lat_dev, lon_dev, channels = fields.shape
    degree_dev = spectral_weight.shape[0]
    kernel_count = filter_basis.shape[0]
    band_count = filter_basis.shape[2]
    support = filter_basis.shape[3]
    half_width = HW
    total_lat = lat_dev * lat_count
    total_lon = lon_dev * lon_count
    mode_dev = MDEV
    order_share = mode_dev // lat_count
    row_count = lat_dev // lon_count
    to_modes, from_modes = mode_tables(total_lon, mode_dev * lon_count)
    table_shape = (lon_count, lon_dev, 2, lon_count, lat_count, order_share)
    to_modes = to_modes.reshape(table_shape)
    from_modes = from_modes.reshape(table_shape)
    orders = (
        lon_index * mode_dev + lat_index * order_share + jnp.arange(order_share, dtype=jnp.int32)
    )
    lat_order = (
        jnp.arange(lat_count, dtype=jnp.int32)[None, :, None] * lat_dev
        + jnp.arange(lon_count, dtype=jnp.int32)[:, None, None] * row_count
        + jnp.arange(row_count, dtype=jnp.int32)[None, None, :]
    ).reshape(total_lat)
    colatitude = math.pi * (lat_order.astype(jnp.float32) + 0.5) / total_lat
    tables = {}

    def weighted_after(gate):
        _, colat = lax.optimization_barrier((gate, colatitude))
        legendre = legendre_rows(orders, degree_dev * lat_count, colat)
        quadrature = math.pi / total_lat * jnp.sin(colat)
        tables["weighted"] = (legendre * quadrature[None, :, None]).astype(jnp.bfloat16)
        tables["unweighted"] = legendre.astype(jnp.bfloat16)
        return tables["weighted"]

    real_part = spectral_weight[:, 0]
    imag_part = spectral_weight[:, 1]
    complex_mix = jnp.stack(
        [jnp.stack([real_part, imag_part], axis=2), jnp.stack([-imag_part, real_part], axis=2)],
        axis=1,
    )
    harmonics = analysis(fields, to_modes, weighted_after, lon_count, lat_count)
    weighted = tables["weighted"]
    unweighted = tables["unweighted"]
    harmonics, local_fields, filter_basis, neighbor_rows = lax.optimization_barrier(
        (harmonics, fields, filter_basis, neighbor_rows)
    )
    filtered = jnp.einsum(
        "pedakc,dkcjx->pedajx", harmonics, complex_mix, preferred_element_type=jnp.float32
    ).astype(jnp.bfloat16)
    spectral = synthesis(filtered, unweighted, from_modes, lon_count)
    padded = margin(local_fields)
    row_base = lat_index * lat_dev
    my_rows = lax.dynamic_slice_in_dim(neighbor_rows, row_base, lat_dev, 0)
    my_basis = lax.dynamic_slice_in_dim(filter_basis, row_base, lat_dev, 1)
    wide_count = lon_dev + 2 * half_width
    out_pos = jnp.arange(lon_dev, dtype=jnp.int32)[:, None, None]
    in_pos = jnp.arange(wide_count, dtype=jnp.int32)[None, :, None]
    tap_pos = jnp.arange(support, dtype=jnp.int32)[None, None, :]
    forward_pick = (in_pos - out_pos == tap_pos).astype(jnp.float32)
    local_sum = jnp.zeros((kernel_count, mem_count, lat_dev, lon_dev, channels), jnp.float32)
    for band_index in range(band_count):
        source_rows = my_rows[:, band_index] - row_base + half_width
        sources = jnp.take(padded, source_rows, axis=1)
        banded = jnp.einsum(
            "kis,fts->kift", my_basis[:, :, band_index, :].astype(jnp.float32), forward_pick
        ).astype(jnp.bfloat16)
        local_sum = local_sum + jnp.einsum(
            "kift,aitc->kaifc", banded, sources, preferred_element_type=jnp.float32
        )
    local_terms = local_sum.astype(jnp.bfloat16)
    pre_act = spectral.astype(jnp.float32) + jnp.einsum(
        "kaifc,kcd->aifd", local_terms, local_weight, preferred_element_type=jnp.float32
    )
    activation, derivative = gelu_parts(pre_act)
    block_output = (fields.astype(jnp.float32) + activation).astype(jnp.bfloat16)
    grad_mix = (cotangent.astype(jnp.float32) * derivative).astype(jnp.bfloat16)
    grad_filtered = analysis(grad_mix, from_modes, unweighted, lon_count, lat_count)
    grad_harmonics = jnp.einsum(
        "pedajx,dkcjx->pedakc", grad_filtered, complex_mix, preferred_element_type=jnp.float32
    ).astype(jnp.bfloat16)
    grad_spectral = synthesis(grad_harmonics, weighted, to_modes, lon_count)
    grad_padded = margin(grad_mix)
    grad_local = jnp.einsum(
        "aitd,kcd->kaitc", grad_padded, local_weight, preferred_element_type=jnp.float32
    ).astype(jnp.bfloat16)
    tall_count = lat_dev + 2 * half_width
    padded_rows = row_base - half_width + jnp.arange(tall_count, dtype=jnp.int32)
    inside = (padded_rows >= 0) & (padded_rows < total_lat)
    safe_rows = jnp.clip(padded_rows, 0, total_lat - 1)
    pad_neighbors = jnp.take(neighbor_rows, safe_rows, axis=0)
    pad_basis = jnp.take(filter_basis, safe_rows, axis=1)
    back_pick = (out_pos - in_pos + 2 * half_width == tap_pos).astype(jnp.float32)
    targets = jnp.arange(lat_dev, dtype=jnp.int32)
    grad_sum = jnp.zeros((mem_count, lat_dev, lon_dev, channels), jnp.float32)
    for band_index in range(band_count):
        banded = jnp.einsum(
            "kis,qts->kiqt", pad_basis[:, :, band_index, :].astype(jnp.float32), back_pick
        ).astype(jnp.bfloat16)
        spread = jnp.einsum(
            "kiqt,kaitc->aiqc", banded, grad_local, preferred_element_type=jnp.float32
        )
        placing = (
            (pad_neighbors[:, band_index][None, :] - row_base == targets[:, None]) & inside[None, :]
        ).astype(jnp.float32)
        grad_sum = grad_sum + jnp.einsum(
            "ji,aiqc->ajqc", placing, spread, precision=lax.Precision.HIGHEST
        )
    input_grad = (
        cotangent.astype(jnp.float32) + grad_spectral.astype(jnp.float32) + grad_sum
    ).astype(jnp.bfloat16)
    return (block_output, input_grad)


def solution(mesh):
    in_specs = (
        P(None, "lat", "lon", None),
        P(None, "lat", "lon", None),
        P("lat", None, None, None),
        P(),
        P(),
        P(),
    )
    out_specs = (P(None, "lat", "lon", None), P(None, "lat", "lon", None))
    return jax.shard_map(
        per_device, mesh=mesh, in_specs=in_specs, out_specs=out_specs, check_vma=False
    )
```

```python
import math

import ml_dtypes
import numpy as np

import jax
import jax.numpy as jnp
from jax import lax
from jax.experimental import pallas as pl
from jax.experimental.pallas import tpu as pltpu
from jax.sharding import PartitionSpec as P

MDEV = 16
HW = 8


TANH_SCALE = 0.7978845608028654
CUBIC_TERM = 0.044715


def extended(cells, sides, width):
    for axis, dim in sides:
        count = lax.axis_size(axis)
        head = lax.slice_in_dim(cells, 0, width, axis=dim)
        tail = lax.slice_in_dim(cells, cells.shape[dim] - width, cells.shape[dim], axis=dim)
        cells = jnp.concatenate(
            [
                lax.ppermute(tail, axis, [(i, (i + 1) % count) for i in range(count)]),
                cells,
                lax.ppermute(head, axis, [((i + 1) % count, i) for i in range(count)]),
            ],
            axis=dim,
        )
    return cells


def gelu_parts(values):
    tanh_input = TANH_SCALE * (values + CUBIC_TERM * values * values * values)
    hyper = jnp.tanh(tanh_input)
    result = 0.5 * values * (1.0 + hyper)
    derivative = 0.5 * (1.0 + hyper) + 0.5 * values * (1.0 - hyper * hyper) * TANH_SCALE * (
        1.0 + 3.0 * CUBIC_TERM * values * values
    )
    return (result, derivative)


def mode_tables(lon_count, mode_count):
    angles_int = (
        np.arange(lon_count, dtype=np.int64)[:, None]
        * np.arange(mode_count, dtype=np.int64)[None, :]
        % lon_count
    )
    angles = angles_int.astype(np.float64) * (2.0 * math.pi / lon_count)
    stacked = np.stack([np.cos(angles), -np.sin(angles)], axis=1)
    factor = np.where(np.arange(mode_count) == 0, 1.0, 2.0)
    to_modes = (stacked * (2.0 * math.pi / lon_count)).astype(ml_dtypes.bfloat16)
    from_modes = (stacked * factor[None, None, :]).astype(ml_dtypes.bfloat16)
    return lax.optimization_barrier((jnp.asarray(to_modes), jnp.asarray(from_modes)))


def _legendre_kernel(order_ref, gain_ref, cos_ref, seed_ref, out_ref, rows_ref):
    share = out_ref.shape[0]
    degree_count = rows_ref.shape[0]
    cosine = cos_ref[...]
    for o in range(share):
        order = order_ref[o]
        seed = seed_ref[pl.ds(o, 1), :]

        def step(j, carry):
            p_now, p_before, log_scale = carry
            gain = gain_ref[2 * o, j]
            cross = gain_ref[2 * o + 1, j]
            active = j > order
            grown = (gain * cosine) * p_now - cross * p_before
            p_next = jnp.where(active, grown, p_now)
            p_prev = jnp.where(active, p_now, p_before)
            largest = jnp.maximum(jnp.maximum(jnp.abs(p_next), jnp.abs(p_prev)), 1e-30)
            inverse = 1.0 / largest
            p_next = p_next * inverse
            p_prev = p_prev * inverse
            log_scale = log_scale + jnp.log(largest)
            value = jnp.where(j >= order, p_next * jnp.exp(log_scale + seed), 0.0)
            rows_ref[pl.ds(j, 1), :] = value
            return (p_next, p_prev, log_scale)

        ones = jnp.ones_like(cosine)
        zeros = jnp.zeros_like(cosine)
        lax.fori_loop(0, degree_count, step, (ones, zeros, zeros), unroll=4)
        out_ref[o] = rows_ref[...].T


def legendre_rows(orders, degree_count, colatitude):
    lat_count = colatitude.shape[0]
    cosine = jnp.cos(colatitude)
    sine_part = jnp.sin(colatitude)
    order_real = orders.astype(jnp.float32)
    seed_log = 0.5 * (
        jnp.log((2.0 * order_real + 1.0) / (4.0 * math.pi))
        + lax.lgamma(order_real + 0.5)
        - lax.lgamma(order_real + 1.0)
        - 0.5 * math.log(math.pi)
    )
    seed_log = seed_log[:, None] + order_real[:, None] * jnp.log(sine_part)[None, :]
    degree_real = jnp.arange(degree_count, dtype=jnp.float32)[None, :]
    order_col = order_real[:, None]
    forward_gain = jnp.sqrt(
        jnp.maximum(4.0 * degree_real * degree_real - 1.0, 1.0)
        / jnp.maximum(degree_real * degree_real - order_col * order_col, 1.0)
    )
    backward_gain = jnp.sqrt(
        jnp.maximum((degree_real - 1.0) ** 2 - order_col * order_col, 0.0)
        / jnp.maximum(4.0 * (degree_real - 1.0) ** 2 - 1.0, 1.0)
    )
    share = orders.shape[0]
    gains = jnp.stack([forward_gain, forward_gain * backward_gain], axis=1).reshape(
        2 * share, degree_count
    )
    return pl.pallas_call(
        _legendre_kernel,
        out_shape=jax.ShapeDtypeStruct((share, lat_count, degree_count), jnp.float32),
        in_specs=[
            pl.BlockSpec(memory_space=pltpu.SMEM),
            pl.BlockSpec(memory_space=pltpu.SMEM),
            pl.BlockSpec(memory_space=pltpu.VMEM),
            pl.BlockSpec(memory_space=pltpu.VMEM),
        ],
        out_specs=pl.BlockSpec(memory_space=pltpu.VMEM),
        scratch_shapes=[pltpu.VMEM((degree_count, lat_count), jnp.float32)],
        cost_estimate=pl.CostEstimate(
            flops=20 * share * degree_count * lat_count,
            transcendentals=3 * share * degree_count * lat_count,
            bytes_accessed=4 * share * degree_count * lat_count,
        ),
    )(orders.astype(jnp.int32), gains, cosine[None, :], seed_log)


def swap_longitude(blocks):
    return lax.all_to_all(blocks, "lon", split_axis=1, concat_axis=1, tiled=True)


def swap_latitude(blocks):
    return lax.all_to_all(blocks, "lat", split_axis=2, concat_axis=2, tiled=True)


def swap_middle(blocks):
    shape = blocks.shape
    joined = blocks.reshape(shape[0], shape[1] * shape[2], *shape[3:])
    swapped = lax.all_to_all(joined, ("lon", "lat"), split_axis=1, concat_axis=1, tiled=True)
    return swapped.reshape(shape)


def margin(blocks):
    return extended(blocks, (("lat", 1), ("lon", 2)), HW)


def analysis(field_blocks, dft_table, degree_table, lon_count, lat_count):
    mem_count, lat_dev, lon_dev, channels = field_blocks.shape
    row_count = lat_dev // lon_count
    grouped = swap_longitude(
        field_blocks.reshape(mem_count, lon_count, row_count, lon_dev, channels)
    )
    fourier = jnp.einsum(
        "aqrfc,qfkjbe->ajbrkec", grouped, dft_table, preferred_element_type=jnp.float32
    ).astype(jnp.bfloat16)
    columns = swap_middle(fourier)
    if callable(degree_table):
        degree_table = degree_table(fourier)
    a, s, p, r, k, e, c = columns.shape
    flat = columns.transpose(5, 1, 2, 3, 0, 4, 6).reshape(e, s * p * r, a * k * c)
    degrees = jnp.einsum(
        "eln,eld->edn", flat, degree_table, preferred_element_type=jnp.float32
    ).astype(jnp.bfloat16)
    degree_total = degree_table.shape[2]
    degrees = degrees.reshape(e, lat_count, degree_total // lat_count, a, k, c)
    degrees = degrees.transpose(1, 0, 2, 3, 4, 5)
    return lax.all_to_all(degrees, "lat", split_axis=0, concat_axis=0, tiled=True)


def synthesis(spectrum, degree_table, dft_table, lon_count):
    by_degree = lax.all_to_all(spectrum, "lat", split_axis=0, concat_axis=0, tiled=True)
    b, e, d, a, k, c = by_degree.shape
    flat = by_degree.transpose(1, 0, 2, 3, 4, 5).reshape(e, b * d, a * k * c)
    zonal = jnp.einsum(
        "edn,eld->eln", flat, degree_table, preferred_element_type=jnp.float32
    ).astype(jnp.bfloat16)
    total_lat = zonal.shape[1]
    row_count = total_lat // (lon_count * b)
    zonal_modes = zonal.reshape(e, lon_count, b, row_count, a, k, c).transpose(4, 1, 2, 3, 5, 0, 6)
    by_order = swap_middle(zonal_modes)
    grid_blocks = jnp.einsum(
        "ajbrkec,qfkjbe->aqrfc", by_order, dft_table, preferred_element_type=jnp.float32
    ).astype(jnp.bfloat16)
    returned = swap_longitude(grid_blocks)
    return returned.reshape(
        a, returned.shape[1] * returned.shape[2], returned.shape[3], returned.shape[4]
    )


def per_device(fields, cotangent, spectral_weight, local_weight, filter_basis, neighbor_rows):
    lat_count = lax.axis_size("lat")
    lon_count = lax.axis_size("lon")
    lat_index = lax.axis_index("lat")
    lon_index = lax.axis_index("lon")
    mem_count, lat_dev, lon_dev, channels = fields.shape
    degree_dev = spectral_weight.shape[0]
    kernel_count = filter_basis.shape[0]
    band_count = filter_basis.shape[2]
    support = filter_basis.shape[3]
    half_width = HW
    total_lat = lat_dev * lat_count
    total_lon = lon_dev * lon_count
    mode_dev = MDEV
    order_share = mode_dev // lat_count
    row_count = lat_dev // lon_count
    to_modes, from_modes = mode_tables(total_lon, mode_dev * lon_count)
    table_shape = (lon_count, lon_dev, 2, lon_count, lat_count, order_share)
    to_modes = to_modes.reshape(table_shape)
    from_modes = from_modes.reshape(table_shape)
    orders = (
        lon_index * mode_dev + lat_index * order_share + jnp.arange(order_share, dtype=jnp.int32)
    )
    lat_order = (
        jnp.arange(lat_count, dtype=jnp.int32)[None, :, None] * lat_dev
        + jnp.arange(lon_count, dtype=jnp.int32)[:, None, None] * row_count
        + jnp.arange(row_count, dtype=jnp.int32)[None, None, :]
    ).reshape(total_lat)
    colatitude = math.pi * (lat_order.astype(jnp.float32) + 0.5) / total_lat
    tables = {}

    def weighted_after(gate):
        _, colat = lax.optimization_barrier((gate, colatitude))
        legendre = legendre_rows(orders, degree_dev * lat_count, colat)
        quadrature = math.pi / total_lat * jnp.sin(colat)
        tables["weighted"] = (legendre * quadrature[None, :, None]).astype(jnp.bfloat16)
        tables["unweighted"] = legendre.astype(jnp.bfloat16)
        return tables["weighted"]

    real_part = spectral_weight[:, 0]
    imag_part = spectral_weight[:, 1]
    harmonics = analysis(fields, to_modes, weighted_after, lon_count, lat_count)
    weighted = tables["weighted"]
    unweighted = tables["unweighted"]
    harmonics, local_fields, filter_basis, neighbor_rows = lax.optimization_barrier(
        (harmonics, fields, filter_basis, neighbor_rows)
    )
    by_real = jnp.einsum(
        "pedakc,dcx->pedakx", harmonics, real_part, preferred_element_type=jnp.float32
    )
    by_imag = jnp.einsum(
        "pedakc,dcx->pedakx", harmonics, imag_part, preferred_element_type=jnp.float32
    )
    filtered = jnp.stack(
        [by_real[:, :, :, :, 0] - by_imag[:, :, :, :, 1], by_imag[:, :, :, :, 0] + by_real[:, :, :, :, 1]],
        axis=4,
    ).astype(jnp.bfloat16)
    spectral = synthesis(filtered, unweighted, from_modes, lon_count)
    padded = margin(local_fields)
    row_base = lat_index * lat_dev
    my_rows = lax.dynamic_slice_in_dim(neighbor_rows, row_base, lat_dev, 0)
    my_basis = lax.dynamic_slice_in_dim(filter_basis, row_base, lat_dev, 1)
    wide_count = lon_dev + 2 * half_width
    out_pos = jnp.arange(lon_dev, dtype=jnp.int32)[:, None, None]
    in_pos = jnp.arange(wide_count, dtype=jnp.int32)[None, :, None]
    tap_pos = jnp.arange(support, dtype=jnp.int32)[None, None, :]
    forward_pick = (in_pos - out_pos == tap_pos).astype(jnp.float32)
    local_sum = jnp.zeros((kernel_count, mem_count, lat_dev, lon_dev, channels), jnp.float32)
    for band_index in range(band_count):
        source_rows = my_rows[:, band_index] - row_base + half_width
        sources = jnp.take(padded, source_rows, axis=1)
        banded = jnp.einsum(
            "kis,fts->kift", my_basis[:, :, band_index, :].astype(jnp.float32), forward_pick
        ).astype(jnp.bfloat16)
        local_sum = local_sum + jnp.einsum(
            "kift,aitc->kaifc", banded, sources, preferred_element_type=jnp.float32
        )
    local_terms = local_sum.astype(jnp.bfloat16)
    pre_act = spectral.astype(jnp.float32) + jnp.einsum(
        "kaifc,kcd->aifd", local_terms, local_weight, preferred_element_type=jnp.float32
    )
    activation, derivative = gelu_parts(pre_act)
    block_output = (fields.astype(jnp.float32) + activation).astype(jnp.bfloat16)
    grad_mix = (cotangent.astype(jnp.float32) * derivative).astype(jnp.bfloat16)
    grad_filtered = analysis(grad_mix, from_modes, unweighted, lon_count, lat_count)
    back_real = jnp.einsum(
        "pedajx,dcx->pedajc", grad_filtered, real_part, preferred_element_type=jnp.float32
    )
    back_imag = jnp.einsum(
        "pedajx,dcx->pedajc", grad_filtered, imag_part, preferred_element_type=jnp.float32
    )
    grad_harmonics = jnp.stack(
        [
            back_real[:, :, :, :, 0] + back_imag[:, :, :, :, 1],
            back_real[:, :, :, :, 1] - back_imag[:, :, :, :, 0],
        ],
        axis=4,
    ).astype(jnp.bfloat16)
    grad_spectral = synthesis(grad_harmonics, weighted, to_modes, lon_count)
    grad_padded = margin(grad_mix)
    grad_local = jnp.einsum(
        "aitd,kcd->kaitc", grad_padded, local_weight, preferred_element_type=jnp.float32
    ).astype(jnp.bfloat16)
    tall_count = lat_dev + 2 * half_width
    padded_rows = row_base - half_width + jnp.arange(tall_count, dtype=jnp.int32)
    inside = (padded_rows >= 0) & (padded_rows < total_lat)
    safe_rows = jnp.clip(padded_rows, 0, total_lat - 1)
    pad_neighbors = jnp.take(neighbor_rows, safe_rows, axis=0)
    pad_basis = jnp.take(filter_basis, safe_rows, axis=1)
    back_pick = (out_pos - in_pos + 2 * half_width == tap_pos).astype(jnp.float32)
    targets = jnp.arange(lat_dev, dtype=jnp.int32)
    grad_sum = jnp.zeros((mem_count, lat_dev, lon_dev, channels), jnp.float32)
    for band_index in range(band_count):
        banded = jnp.einsum(
            "kis,qts->kiqt", pad_basis[:, :, band_index, :].astype(jnp.float32), back_pick
        ).astype(jnp.bfloat16)
        spread = jnp.einsum(
            "kiqt,kaitc->aiqc", banded, grad_local, preferred_element_type=jnp.float32
        )
        placing = (
            (pad_neighbors[:, band_index][None, :] - row_base == targets[:, None]) & inside[None, :]
        ).astype(jnp.float32)
        grad_sum = grad_sum + jnp.einsum(
            "ji,aiqc->ajqc", placing, spread, precision=lax.Precision.HIGHEST
        )
    input_grad = (
        cotangent.astype(jnp.float32) + grad_spectral.astype(jnp.float32) + grad_sum
    ).astype(jnp.bfloat16)
    return (block_output, input_grad)


def solution(mesh):
    in_specs = (
        P(None, "lat", "lon", None),
        P(None, "lat", "lon", None),
        P("lat", None, None, None),
        P(),
        P(),
        P(),
    )
    out_specs = (P(None, "lat", "lon", None), P(None, "lat", "lon", None))
    return jax.shard_map(
        per_device, mesh=mesh, in_specs=in_specs, out_specs=out_specs, check_vma=False
    )
```

```python
import math

import ml_dtypes
import numpy as np

import jax
import jax.numpy as jnp
from jax import lax
from jax.experimental import pallas as pl
from jax.experimental.pallas import tpu as pltpu
from jax.sharding import PartitionSpec as P

MDEV = 16
HW = 8


TANH_SCALE = 0.7978845608028654
CUBIC_TERM = 0.044715


def extended(cells, sides, width):
    for axis, dim in sides:
        count = lax.axis_size(axis)
        head = lax.slice_in_dim(cells, 0, width, axis=dim)
        tail = lax.slice_in_dim(cells, cells.shape[dim] - width, cells.shape[dim], axis=dim)
        cells = jnp.concatenate(
            [
                lax.ppermute(tail, axis, [(i, (i + 1) % count) for i in range(count)]),
                cells,
                lax.ppermute(head, axis, [((i + 1) % count, i) for i in range(count)]),
            ],
            axis=dim,
        )
    return cells


def gelu_parts(values):
    tanh_input = TANH_SCALE * (values + CUBIC_TERM * values * values * values)
    hyper = jnp.tanh(tanh_input)
    result = 0.5 * values * (1.0 + hyper)
    derivative = 0.5 * (1.0 + hyper) + 0.5 * values * (1.0 - hyper * hyper) * TANH_SCALE * (
        1.0 + 3.0 * CUBIC_TERM * values * values
    )
    return (result, derivative)


def mode_tables(lon_count, mode_count):
    angles_int = (
        np.arange(lon_count, dtype=np.int64)[:, None]
        * np.arange(mode_count, dtype=np.int64)[None, :]
        % lon_count
    )
    angles = angles_int.astype(np.float64) * (2.0 * math.pi / lon_count)
    stacked = np.stack([np.cos(angles), -np.sin(angles)], axis=1)
    factor = np.where(np.arange(mode_count) == 0, 1.0, 2.0)
    to_modes = (stacked * (2.0 * math.pi / lon_count)).astype(ml_dtypes.bfloat16)
    from_modes = (stacked * factor[None, None, :]).astype(ml_dtypes.bfloat16)
    return lax.optimization_barrier((jnp.asarray(to_modes), jnp.asarray(from_modes)))


def _legendre_kernel(order_ref, gain_ref, cos_ref, seed_ref, out_ref, rows_ref):
    share = out_ref.shape[0]
    degree_count = rows_ref.shape[0]
    cosine = cos_ref[...]
    for o in range(share):
        order = order_ref[o]
        seed = seed_ref[pl.ds(o, 1), :]

        def step(j, carry):
            p_now, p_before, log_scale = carry
            gain = gain_ref[2 * o, j]
            cross = gain_ref[2 * o + 1, j]
            active = j > order
            grown = (gain * cosine) * p_now - cross * p_before
            p_next = jnp.where(active, grown, p_now)
            p_prev = jnp.where(active, p_now, p_before)
            largest = jnp.maximum(jnp.maximum(jnp.abs(p_next), jnp.abs(p_prev)), 1e-30)
            inverse = 1.0 / largest
            p_next = p_next * inverse
            p_prev = p_prev * inverse
            log_scale = log_scale + jnp.log(largest)
            value = jnp.where(j >= order, p_next * jnp.exp(log_scale + seed), 0.0)
            rows_ref[pl.ds(j, 1), :] = value
            return (p_next, p_prev, log_scale)

        ones = jnp.ones_like(cosine)
        zeros = jnp.zeros_like(cosine)
        lax.fori_loop(0, degree_count, step, (ones, zeros, zeros), unroll=4)
        out_ref[o] = rows_ref[...].T


def legendre_rows(orders, degree_count, colatitude):
    lat_count = colatitude.shape[0]
    cosine = jnp.cos(colatitude)
    sine_part = jnp.sin(colatitude)
    order_real = orders.astype(jnp.float32)
    seed_log = 0.5 * (
        jnp.log((2.0 * order_real + 1.0) / (4.0 * math.pi))
        + lax.lgamma(order_real + 0.5)
        - lax.lgamma(order_real + 1.0)
        - 0.5 * math.log(math.pi)
    )
    seed_log = seed_log[:, None] + order_real[:, None] * jnp.log(sine_part)[None, :]
    degree_real = jnp.arange(degree_count, dtype=jnp.float32)[None, :]
    order_col = order_real[:, None]
    forward_gain = jnp.sqrt(
        jnp.maximum(4.0 * degree_real * degree_real - 1.0, 1.0)
        / jnp.maximum(degree_real * degree_real - order_col * order_col, 1.0)
    )
    backward_gain = jnp.sqrt(
        jnp.maximum((degree_real - 1.0) ** 2 - order_col * order_col, 0.0)
        / jnp.maximum(4.0 * (degree_real - 1.0) ** 2 - 1.0, 1.0)
    )
    share = orders.shape[0]
    gains = jnp.stack([forward_gain, forward_gain * backward_gain], axis=1).reshape(
        2 * share, degree_count
    )
    return pl.pallas_call(
        _legendre_kernel,
        out_shape=jax.ShapeDtypeStruct((share, lat_count, degree_count), jnp.float32),
        in_specs=[
            pl.BlockSpec(memory_space=pltpu.SMEM),
            pl.BlockSpec(memory_space=pltpu.SMEM),
            pl.BlockSpec(memory_space=pltpu.VMEM),
            pl.BlockSpec(memory_space=pltpu.VMEM),
        ],
        out_specs=pl.BlockSpec(memory_space=pltpu.VMEM),
        scratch_shapes=[pltpu.VMEM((degree_count, lat_count), jnp.float32)],
        cost_estimate=pl.CostEstimate(
            flops=20 * share * degree_count * lat_count,
            transcendentals=3 * share * degree_count * lat_count,
            bytes_accessed=4 * share * degree_count * lat_count,
        ),
    )(orders.astype(jnp.int32), gains, cosine[None, :], seed_log)


def swap_longitude(blocks):
    return lax.all_to_all(blocks, "lon", split_axis=1, concat_axis=1, tiled=True)


def swap_latitude(blocks):
    return lax.all_to_all(blocks, "lat", split_axis=2, concat_axis=2, tiled=True)


def swap_middle(blocks):
    shape = blocks.shape
    joined = blocks.reshape(shape[0], shape[1] * shape[2], *shape[3:])
    swapped = lax.all_to_all(joined, ("lon", "lat"), split_axis=1, concat_axis=1, tiled=True)
    return swapped.reshape(shape)


def margin(blocks):
    return extended(blocks, (("lat", 1), ("lon", 2)), HW)


def analysis(field_blocks, dft_table, degree_table, lon_count, lat_count):
    mem_count, lat_dev, lon_dev, channels = field_blocks.shape
    row_count = lat_dev // lon_count
    grouped = swap_longitude(
        field_blocks.reshape(mem_count, lon_count, row_count, lon_dev, channels)
    )
    fourier = jnp.einsum(
        "aqrfc,qfkjbe->ajbrkec", grouped, dft_table, preferred_element_type=jnp.float32
    ).astype(jnp.bfloat16)
    columns = swap_middle(fourier)
    if callable(degree_table):
        degree_table = degree_table(fourier)
    a, s, p, r, k, e, c = columns.shape
    flat = columns.transpose(5, 1, 2, 3, 0, 4, 6).reshape(e, s * p * r, a * k * c)
    degrees = jnp.einsum(
        "eln,eld->edn", flat, degree_table, preferred_element_type=jnp.float32
    ).astype(jnp.bfloat16)
    degree_total = degree_table.shape[2]
    degrees = degrees.reshape(e, lat_count, degree_total // lat_count, a, k, c)
    degrees = degrees.transpose(1, 0, 2, 3, 4, 5)
    return lax.all_to_all(degrees, "lat", split_axis=0, concat_axis=0, tiled=True)


def synthesis(spectrum, degree_table, dft_table, lon_count):
    by_degree = lax.all_to_all(spectrum, "lat", split_axis=0, concat_axis=0, tiled=True)
    b, e, d, a, k, c = by_degree.shape
    flat = by_degree.transpose(1, 0, 2, 3, 4, 5).reshape(e, b * d, a * k * c)
    zonal = jnp.einsum(
        "edn,eld->eln", flat, degree_table, preferred_element_type=jnp.float32
    ).astype(jnp.bfloat16)
    total_lat = zonal.shape[1]
    row_count = total_lat // (lon_count * b)
    zonal_modes = zonal.reshape(e, lon_count, b, row_count, a, k, c).transpose(4, 1, 2, 3, 5, 0, 6)
    by_order = swap_middle(zonal_modes)
    grid_blocks = jnp.einsum(
        "ajbrkec,qfkjbe->aqrfc", by_order, dft_table, preferred_element_type=jnp.float32
    ).astype(jnp.bfloat16)
    returned = swap_longitude(grid_blocks)
    return returned.reshape(
        a, returned.shape[1] * returned.shape[2], returned.shape[3], returned.shape[4]
    )


def per_device(fields, cotangent, spectral_weight, local_weight, filter_basis, neighbor_rows):
    lat_count = lax.axis_size("lat")
    lon_count = lax.axis_size("lon")
    lat_index = lax.axis_index("lat")
    lon_index = lax.axis_index("lon")
    mem_count, lat_dev, lon_dev, channels = fields.shape
    degree_dev = spectral_weight.shape[0]
    kernel_count = filter_basis.shape[0]
    band_count = filter_basis.shape[2]
    support = filter_basis.shape[3]
    half_width = HW
    total_lat = lat_dev * lat_count
    total_lon = lon_dev * lon_count
    mode_dev = MDEV
    order_share = mode_dev // lat_count
    row_count = lat_dev // lon_count
    to_modes, from_modes = mode_tables(total_lon, mode_dev * lon_count)
    table_shape = (lon_count, lon_dev, 2, lon_count, lat_count, order_share)
    to_modes = to_modes.reshape(table_shape)
    from_modes = from_modes.reshape(table_shape)
    orders = (
        lon_index * mode_dev + lat_index * order_share + jnp.arange(order_share, dtype=jnp.int32)
    )
    lat_order = (
        jnp.arange(lat_count, dtype=jnp.int32)[None, :, None] * lat_dev
        + jnp.arange(lon_count, dtype=jnp.int32)[:, None, None] * row_count
        + jnp.arange(row_count, dtype=jnp.int32)[None, None, :]
    ).reshape(total_lat)
    colatitude = math.pi * (lat_order.astype(jnp.float32) + 0.5) / total_lat
    tables = {}

    def weighted_after(gate):
        _, colat = lax.optimization_barrier((gate, colatitude))
        legendre = legendre_rows(orders, degree_dev * lat_count, colat)
        quadrature = math.pi / total_lat * jnp.sin(colat)
        tables["weighted"] = (legendre * quadrature[None, :, None]).astype(jnp.bfloat16)
        tables["unweighted"] = legendre.astype(jnp.bfloat16)
        return tables["weighted"]

    real_part = spectral_weight[:, 0]
    imag_part = spectral_weight[:, 1]
    harmonics = analysis(fields, to_modes, weighted_after, lon_count, lat_count)
    weighted = tables["weighted"]
    unweighted = tables["unweighted"]
    harmonics, local_fields, filter_basis, neighbor_rows = lax.optimization_barrier(
        (harmonics, fields, filter_basis, neighbor_rows)
    )
    by_real = jnp.einsum(
        "pedakc,dcx->pedakx", harmonics, real_part, preferred_element_type=jnp.float32
    )
    by_imag = jnp.einsum(
        "pedakc,dcx->pedakx", harmonics, imag_part, preferred_element_type=jnp.float32
    )
    filtered = jnp.stack(
        [by_real[:, :, :, :, 0] - by_imag[:, :, :, :, 1], by_imag[:, :, :, :, 0] + by_real[:, :, :, :, 1]],
        axis=4,
    ).astype(jnp.bfloat16)
    spectral = synthesis(filtered, unweighted, from_modes, lon_count)
    padded = margin(local_fields)
    row_base = lat_index * lat_dev
    my_rows = lax.dynamic_slice_in_dim(neighbor_rows, row_base, lat_dev, 0)
    my_basis = lax.dynamic_slice_in_dim(filter_basis, row_base, lat_dev, 1)
    wide_count = lon_dev + 2 * half_width
    out_pos = jnp.arange(lon_dev, dtype=jnp.int32)[:, None, None]
    in_pos = jnp.arange(wide_count, dtype=jnp.int32)[None, :, None]
    tap_pos = jnp.arange(support, dtype=jnp.int32)[None, None, :]
    forward_pick = (in_pos - out_pos == tap_pos).astype(jnp.float32)
    local_sum = jnp.zeros((kernel_count, mem_count, lat_dev, lon_dev, channels), jnp.float32)
    for band_index in range(band_count):
        source_rows = my_rows[:, band_index] - row_base + half_width
        sources = jnp.take(padded, source_rows, axis=1)
        banded = jnp.einsum(
            "kis,fts->kift", my_basis[:, :, band_index, :].astype(jnp.float32), forward_pick
        ).astype(jnp.bfloat16)
        local_sum = local_sum + jnp.einsum(
            "kift,aitc->kaifc", banded, sources, preferred_element_type=jnp.float32
        )
    local_terms = local_sum.astype(jnp.bfloat16)
    pre_act = spectral.astype(jnp.float32) + jnp.einsum(
        "kaifc,kcd->aifd", local_terms, local_weight, preferred_element_type=jnp.float32
    )
    activation, derivative = gelu_parts(pre_act)
    block_output = (fields.astype(jnp.float32) + activation).astype(jnp.bfloat16)
    grad_mix = (cotangent.astype(jnp.float32) * derivative).astype(jnp.bfloat16)
    grad_filtered = analysis(grad_mix, from_modes, unweighted, lon_count, lat_count)
    back_real = jnp.einsum(
        "pedajx,dcx->pedajc", grad_filtered, real_part, preferred_element_type=jnp.float32
    )
    back_imag = jnp.einsum(
        "pedajx,dcx->pedajc", grad_filtered, imag_part, preferred_element_type=jnp.float32
    )
    grad_harmonics = jnp.stack(
        [
            back_real[:, :, :, :, 0] + back_imag[:, :, :, :, 1],
            back_real[:, :, :, :, 1] - back_imag[:, :, :, :, 0],
        ],
        axis=4,
    ).astype(jnp.bfloat16)
    grad_spectral = synthesis(grad_harmonics, weighted, to_modes, lon_count)
    grad_padded = margin(grad_mix)
    grad_local = jnp.einsum(
        "aitd,kcd->kaitc", grad_padded, local_weight, preferred_element_type=jnp.float32
    ).astype(jnp.bfloat16)
    tall_count = lat_dev + 2 * half_width
    padded_rows = row_base - half_width + jnp.arange(tall_count, dtype=jnp.int32)
    inside = (padded_rows >= 0) & (padded_rows < total_lat)
    safe_rows = jnp.clip(padded_rows, 0, total_lat - 1)
    pad_neighbors = jnp.take(neighbor_rows, safe_rows, axis=0)
    pad_basis = jnp.take(filter_basis, safe_rows, axis=1)
    back_pick = (out_pos - in_pos + 2 * half_width == tap_pos).astype(jnp.float32)
    targets = jnp.arange(lat_dev, dtype=jnp.int32)
    grad_sum = jnp.zeros((mem_count, lat_dev, lon_dev, channels), jnp.float32)
    for band_index in range(band_count):
        banded = jnp.einsum(
            "kis,qts->kiqt", pad_basis[:, :, band_index, :].astype(jnp.float32), back_pick
        ).astype(jnp.bfloat16)
        spread = jnp.einsum(
            "kiqt,kaitc->aiqc", banded, grad_local, preferred_element_type=jnp.float32
        )
        placing = (
            (pad_neighbors[:, band_index][None, :] - row_base == targets[:, None]) & inside[None, :]
        ).astype(jnp.float32)
        spread_rows = spread.transpose(1, 0, 2, 3).reshape(spread.shape[1], -1)
        grad_sum = grad_sum + jnp.einsum(
            "ji,im->jm", placing, spread_rows, precision=lax.Precision.HIGHEST
        ).reshape(lat_dev, mem_count, lon_dev, channels).transpose(1, 0, 2, 3)
    input_grad = (
        cotangent.astype(jnp.float32) + grad_spectral.astype(jnp.float32) + grad_sum
    ).astype(jnp.bfloat16)
    return (block_output, input_grad)


def solution(mesh):
    in_specs = (
        P(None, "lat", "lon", None),
        P(None, "lat", "lon", None),
        P("lat", None, None, None),
        P(),
        P(),
        P(),
    )
    out_specs = (P(None, "lat", "lon", None), P(None, "lat", "lon", None))
    return jax.shard_map(
        per_device, mesh=mesh, in_specs=in_specs, out_specs=out_specs, check_vma=False
    )
```

```python
import math

import ml_dtypes
import numpy as np

import jax
import jax.numpy as jnp
from jax import lax
from jax.experimental import pallas as pl
from jax.experimental.pallas import tpu as pltpu
from jax.sharding import PartitionSpec as P

MDEV = 16
HW = 8


TANH_SCALE = 0.7978845608028654
CUBIC_TERM = 0.044715


def extended(cells, sides, width):
    for axis, dim in sides:
        count = lax.axis_size(axis)
        head = lax.slice_in_dim(cells, 0, width, axis=dim)
        tail = lax.slice_in_dim(cells, cells.shape[dim] - width, cells.shape[dim], axis=dim)
        cells = jnp.concatenate(
            [
                lax.ppermute(tail, axis, [(i, (i + 1) % count) for i in range(count)]),
                cells,
                lax.ppermute(head, axis, [((i + 1) % count, i) for i in range(count)]),
            ],
            axis=dim,
        )
    return cells


def gelu_parts(values):
    tanh_input = TANH_SCALE * (values + CUBIC_TERM * values * values * values)
    hyper = jnp.tanh(tanh_input)
    result = 0.5 * values * (1.0 + hyper)
    derivative = 0.5 * (1.0 + hyper) + 0.5 * values * (1.0 - hyper * hyper) * TANH_SCALE * (
        1.0 + 3.0 * CUBIC_TERM * values * values
    )
    return (result, derivative)


def mode_tables(lon_count, mode_count):
    angles_int = (
        np.arange(lon_count, dtype=np.int64)[:, None]
        * np.arange(mode_count, dtype=np.int64)[None, :]
        % lon_count
    )
    angles = angles_int.astype(np.float64) * (2.0 * math.pi / lon_count)
    stacked = np.stack([np.cos(angles), -np.sin(angles)], axis=1)
    factor = np.where(np.arange(mode_count) == 0, 1.0, 2.0)
    to_modes = (stacked * (2.0 * math.pi / lon_count)).astype(ml_dtypes.bfloat16)
    from_modes = (stacked * factor[None, None, :]).astype(ml_dtypes.bfloat16)
    return lax.optimization_barrier((jnp.asarray(to_modes), jnp.asarray(from_modes)))


def _legendre_kernel(order_ref, gain_ref, cos_ref, seed_ref, out_ref, rows_ref):
    share = out_ref.shape[0]
    degree_count = rows_ref.shape[0]
    cosine = cos_ref[...]
    for o in range(share):
        order = order_ref[o]
        seed = seed_ref[pl.ds(o, 1), :]

        def step(j, carry):
            p_now, p_before, log_scale = carry
            gain = gain_ref[2 * o, j]
            cross = gain_ref[2 * o + 1, j]
            active = j > order
            grown = (gain * cosine) * p_now - cross * p_before
            p_next = jnp.where(active, grown, p_now)
            p_prev = jnp.where(active, p_now, p_before)
            largest = jnp.maximum(jnp.maximum(jnp.abs(p_next), jnp.abs(p_prev)), 1e-30)
            inverse = 1.0 / largest
            p_next = p_next * inverse
            p_prev = p_prev * inverse
            log_scale = log_scale + jnp.log(largest)
            value = jnp.where(j >= order, p_next * jnp.exp(log_scale + seed), 0.0)
            rows_ref[pl.ds(j, 1), :] = value
            return (p_next, p_prev, log_scale)

        ones = jnp.ones_like(cosine)
        zeros = jnp.zeros_like(cosine)
        lax.fori_loop(0, degree_count, step, (ones, zeros, zeros), unroll=4)
        out_ref[o] = rows_ref[...].T


def legendre_rows(orders, degree_count, colatitude):
    lat_count = colatitude.shape[0]
    cosine = jnp.cos(colatitude)
    sine_part = jnp.sin(colatitude)
    order_real = orders.astype(jnp.float32)
    seed_log = 0.5 * (
        jnp.log((2.0 * order_real + 1.0) / (4.0 * math.pi))
        + lax.lgamma(order_real + 0.5)
        - lax.lgamma(order_real + 1.0)
        - 0.5 * math.log(math.pi)
    )
    seed_log = seed_log[:, None] + order_real[:, None] * jnp.log(sine_part)[None, :]
    degree_real = jnp.arange(degree_count, dtype=jnp.float32)[None, :]
    order_col = order_real[:, None]
    forward_gain = jnp.sqrt(
        jnp.maximum(4.0 * degree_real * degree_real - 1.0, 1.0)
        / jnp.maximum(degree_real * degree_real - order_col * order_col, 1.0)
    )
    backward_gain = jnp.sqrt(
        jnp.maximum((degree_real - 1.0) ** 2 - order_col * order_col, 0.0)
        / jnp.maximum(4.0 * (degree_real - 1.0) ** 2 - 1.0, 1.0)
    )
    share = orders.shape[0]
    gains = jnp.stack([forward_gain, forward_gain * backward_gain], axis=1).reshape(
        2 * share, degree_count
    )
    return pl.pallas_call(
        _legendre_kernel,
        out_shape=jax.ShapeDtypeStruct((share, lat_count, degree_count), jnp.float32),
        in_specs=[
            pl.BlockSpec(memory_space=pltpu.SMEM),
            pl.BlockSpec(memory_space=pltpu.SMEM),
            pl.BlockSpec(memory_space=pltpu.VMEM),
            pl.BlockSpec(memory_space=pltpu.VMEM),
        ],
        out_specs=pl.BlockSpec(memory_space=pltpu.VMEM),
        scratch_shapes=[pltpu.VMEM((degree_count, lat_count), jnp.float32)],
        cost_estimate=pl.CostEstimate(
            flops=20 * share * degree_count * lat_count,
            transcendentals=3 * share * degree_count * lat_count,
            bytes_accessed=4 * share * degree_count * lat_count,
        ),
    )(orders.astype(jnp.int32), gains, cosine[None, :], seed_log)


def swap_longitude(blocks):
    return lax.all_to_all(blocks, "lon", split_axis=1, concat_axis=1, tiled=True)


def swap_latitude(blocks):
    return lax.all_to_all(blocks, "lat", split_axis=2, concat_axis=2, tiled=True)


def swap_middle(blocks):
    shape = blocks.shape
    joined = blocks.reshape(shape[0], shape[1] * shape[2], *shape[3:])
    swapped = lax.all_to_all(joined, ("lon", "lat"), split_axis=1, concat_axis=1, tiled=True)
    return swapped.reshape(shape)


def margin(blocks):
    return extended(blocks, (("lat", 1), ("lon", 2)), HW)


def analysis(field_blocks, dft_table, degree_table, lon_count, lat_count):
    mem_count, lat_dev, lon_dev, channels = field_blocks.shape
    row_count = lat_dev // lon_count
    grouped = swap_longitude(
        field_blocks.reshape(mem_count, lon_count, row_count, lon_dev, channels)
    )
    fourier = jnp.einsum(
        "aqrfc,qfkjbe->ajbrkec", grouped, dft_table, preferred_element_type=jnp.float32
    ).astype(jnp.bfloat16)
    columns = swap_middle(fourier)
    if callable(degree_table):
        degree_table = degree_table(fourier)
    a, s, p, r, k, e, c = columns.shape
    flat = columns.transpose(5, 1, 2, 3, 0, 4, 6).reshape(e, s * p * r, a * k * c)
    degrees = jnp.einsum(
        "eln,eld->edn", flat, degree_table, preferred_element_type=jnp.float32
    ).astype(jnp.bfloat16)
    degree_total = degree_table.shape[2]
    degrees = degrees.reshape(e, lat_count, degree_total // lat_count, a, k, c)
    degrees = degrees.transpose(1, 0, 2, 3, 4, 5)
    return lax.all_to_all(degrees, "lat", split_axis=0, concat_axis=0, tiled=True)


def synthesis(spectrum, degree_table, dft_table, lon_count):
    by_degree = lax.all_to_all(spectrum, "lat", split_axis=0, concat_axis=0, tiled=True)
    b, e, d, a, k, c = by_degree.shape
    flat = by_degree.transpose(1, 0, 2, 3, 4, 5).reshape(e, b * d, a * k * c)
    zonal = jnp.einsum(
        "edn,eld->eln", flat, degree_table, preferred_element_type=jnp.float32
    ).astype(jnp.bfloat16)
    total_lat = zonal.shape[1]
    row_count = total_lat // (lon_count * b)
    zonal_modes = zonal.reshape(e, lon_count, b, row_count, a, k, c).transpose(4, 1, 2, 3, 5, 0, 6)
    by_order = swap_middle(zonal_modes)
    grid_blocks = jnp.einsum(
        "ajbrkec,qfkjbe->aqrfc", by_order, dft_table, preferred_element_type=jnp.float32
    ).astype(jnp.bfloat16)
    returned = swap_longitude(grid_blocks)
    return returned.reshape(
        a, returned.shape[1] * returned.shape[2], returned.shape[3], returned.shape[4]
    )


def per_device(fields, cotangent, spectral_weight, local_weight, filter_basis, neighbor_rows):
    lat_count = lax.axis_size("lat")
    lon_count = lax.axis_size("lon")
    lat_index = lax.axis_index("lat")
    lon_index = lax.axis_index("lon")
    mem_count, lat_dev, lon_dev, channels = fields.shape
    degree_dev = spectral_weight.shape[0]
    kernel_count = filter_basis.shape[0]
    band_count = filter_basis.shape[2]
    support = filter_basis.shape[3]
    half_width = HW
    total_lat = lat_dev * lat_count
    total_lon = lon_dev * lon_count
    mode_dev = MDEV
    order_share = mode_dev // lat_count
    row_count = lat_dev // lon_count
    to_modes, from_modes = mode_tables(total_lon, mode_dev * lon_count)
    table_shape = (lon_count, lon_dev, 2, lon_count, lat_count, order_share)
    to_modes = to_modes.reshape(table_shape)
    from_modes = from_modes.reshape(table_shape)
    orders = (
        lon_index * mode_dev + lat_index * order_share + jnp.arange(order_share, dtype=jnp.int32)
    )
    lat_order = (
        jnp.arange(lat_count, dtype=jnp.int32)[None, :, None] * lat_dev
        + jnp.arange(lon_count, dtype=jnp.int32)[:, None, None] * row_count
        + jnp.arange(row_count, dtype=jnp.int32)[None, None, :]
    ).reshape(total_lat)
    colatitude = math.pi * (lat_order.astype(jnp.float32) + 0.5) / total_lat
    tables = {}

    def weighted_after(gate):
        _, colat, local_fields, basis, rows = lax.optimization_barrier(
            (gate, colatitude, fields, filter_basis, neighbor_rows)
        )
        tables["local"] = (local_fields, basis, rows)
        legendre = legendre_rows(orders, degree_dev * lat_count, colat)
        quadrature = math.pi / total_lat * jnp.sin(colat)
        tables["weighted"] = (legendre * quadrature[None, :, None]).astype(jnp.bfloat16)
        tables["unweighted"] = legendre.astype(jnp.bfloat16)
        return tables["weighted"]

    real_part = spectral_weight[:, 0]
    imag_part = spectral_weight[:, 1]
    harmonics = analysis(fields, to_modes, weighted_after, lon_count, lat_count)
    weighted = tables["weighted"]
    unweighted = tables["unweighted"]
    local_fields, filter_basis, neighbor_rows = tables["local"]
    by_real = jnp.einsum(
        "pedakc,dcx->pedakx", harmonics, real_part, preferred_element_type=jnp.float32
    )
    by_imag = jnp.einsum(
        "pedakc,dcx->pedakx", harmonics, imag_part, preferred_element_type=jnp.float32
    )
    filtered = jnp.stack(
        [by_real[:, :, :, :, 0] - by_imag[:, :, :, :, 1], by_imag[:, :, :, :, 0] + by_real[:, :, :, :, 1]],
        axis=4,
    ).astype(jnp.bfloat16)
    spectral = synthesis(filtered, unweighted, from_modes, lon_count)
    padded = margin(local_fields)
    row_base = lat_index * lat_dev
    my_rows = lax.dynamic_slice_in_dim(neighbor_rows, row_base, lat_dev, 0)
    my_basis = lax.dynamic_slice_in_dim(filter_basis, row_base, lat_dev, 1)
    wide_count = lon_dev + 2 * half_width
    out_pos = jnp.arange(lon_dev, dtype=jnp.int32)[:, None, None]
    in_pos = jnp.arange(wide_count, dtype=jnp.int32)[None, :, None]
    tap_pos = jnp.arange(support, dtype=jnp.int32)[None, None, :]
    forward_pick = (in_pos - out_pos == tap_pos).astype(jnp.float32)
    local_sum = jnp.zeros((kernel_count, mem_count, lat_dev, lon_dev, channels), jnp.float32)
    for band_index in range(band_count):
        source_rows = my_rows[:, band_index] - row_base + half_width
        sources = jnp.take(padded, source_rows, axis=1)
        banded = jnp.einsum(
            "kis,fts->kift", my_basis[:, :, band_index, :].astype(jnp.float32), forward_pick
        ).astype(jnp.bfloat16)
        local_sum = local_sum + jnp.einsum(
            "kift,aitc->kaifc", banded, sources, preferred_element_type=jnp.float32
        )
    local_terms = local_sum.astype(jnp.bfloat16)
    pre_act = spectral.astype(jnp.float32) + jnp.einsum(
        "kaifc,kcd->aifd", local_terms, local_weight, preferred_element_type=jnp.float32
    )
    activation, derivative = gelu_parts(pre_act)
    block_output = (fields.astype(jnp.float32) + activation).astype(jnp.bfloat16)
    grad_mix = (cotangent.astype(jnp.float32) * derivative).astype(jnp.bfloat16)
    grad_filtered = analysis(grad_mix, from_modes, unweighted, lon_count, lat_count)
    back_real = jnp.einsum(
        "pedajx,dcx->pedajc", grad_filtered, real_part, preferred_element_type=jnp.float32
    )
    back_imag = jnp.einsum(
        "pedajx,dcx->pedajc", grad_filtered, imag_part, preferred_element_type=jnp.float32
    )
    grad_harmonics = jnp.stack(
        [
            back_real[:, :, :, :, 0] + back_imag[:, :, :, :, 1],
            back_real[:, :, :, :, 1] - back_imag[:, :, :, :, 0],
        ],
        axis=4,
    ).astype(jnp.bfloat16)
    grad_spectral = synthesis(grad_harmonics, weighted, to_modes, lon_count)
    grad_padded = margin(grad_mix)
    grad_local = jnp.einsum(
        "aitd,kcd->kaitc", grad_padded, local_weight, preferred_element_type=jnp.float32
    ).astype(jnp.bfloat16)
    tall_count = lat_dev + 2 * half_width
    padded_rows = row_base - half_width + jnp.arange(tall_count, dtype=jnp.int32)
    inside = (padded_rows >= 0) & (padded_rows < total_lat)
    safe_rows = jnp.clip(padded_rows, 0, total_lat - 1)
    pad_neighbors = jnp.take(neighbor_rows, safe_rows, axis=0)
    pad_basis = jnp.take(filter_basis, safe_rows, axis=1)
    back_pick = (out_pos - in_pos + 2 * half_width == tap_pos).astype(jnp.float32)
    targets = jnp.arange(lat_dev, dtype=jnp.int32)
    grad_sum = jnp.zeros((mem_count, lat_dev, lon_dev, channels), jnp.float32)
    for band_index in range(band_count):
        banded = jnp.einsum(
            "kis,qts->kiqt", pad_basis[:, :, band_index, :].astype(jnp.float32), back_pick
        ).astype(jnp.bfloat16)
        spread = jnp.einsum(
            "kiqt,kaitc->aiqc", banded, grad_local, preferred_element_type=jnp.float32
        )
        placing = (
            (pad_neighbors[:, band_index][None, :] - row_base == targets[:, None]) & inside[None, :]
        ).astype(jnp.float32)
        spread_rows = spread.transpose(1, 0, 2, 3).reshape(spread.shape[1], -1)
        grad_sum = grad_sum + jnp.einsum(
            "ji,im->jm", placing, spread_rows, precision=lax.Precision.HIGHEST
        ).reshape(lat_dev, mem_count, lon_dev, channels).transpose(1, 0, 2, 3)
    input_grad = (
        cotangent.astype(jnp.float32) + grad_spectral.astype(jnp.float32) + grad_sum
    ).astype(jnp.bfloat16)
    return (block_output, input_grad)


def solution(mesh):
    in_specs = (
        P(None, "lat", "lon", None),
        P(None, "lat", "lon", None),
        P("lat", None, None, None),
        P(),
        P(),
        P(),
    )
    out_specs = (P(None, "lat", "lon", None), P(None, "lat", "lon", None))
    return jax.shard_map(
        per_device, mesh=mesh, in_specs=in_specs, out_specs=out_specs, check_vma=False
    )
```

```python
import math

import ml_dtypes
import numpy as np

import jax
import jax.numpy as jnp
from jax import lax
from jax.experimental import pallas as pl
from jax.experimental.pallas import tpu as pltpu
from jax.sharding import PartitionSpec as P

MDEV = 16
HW = 8


TANH_SCALE = 0.7978845608028654
CUBIC_TERM = 0.044715


def extended(cells, sides, width):
    for axis, dim in sides:
        count = lax.axis_size(axis)
        head = lax.slice_in_dim(cells, 0, width, axis=dim)
        tail = lax.slice_in_dim(cells, cells.shape[dim] - width, cells.shape[dim], axis=dim)
        cells = jnp.concatenate(
            [
                lax.ppermute(tail, axis, [(i, (i + 1) % count) for i in range(count)]),
                cells,
                lax.ppermute(head, axis, [((i + 1) % count, i) for i in range(count)]),
            ],
            axis=dim,
        )
    return cells


def gelu_parts(values):
    tanh_input = TANH_SCALE * (values + CUBIC_TERM * values * values * values)
    hyper = jnp.tanh(tanh_input)
    result = 0.5 * values * (1.0 + hyper)
    derivative = 0.5 * (1.0 + hyper) + 0.5 * values * (1.0 - hyper * hyper) * TANH_SCALE * (
        1.0 + 3.0 * CUBIC_TERM * values * values
    )
    return (result, derivative)


def mode_tables(lon_count, mode_count):
    angles_int = (
        np.arange(lon_count, dtype=np.int64)[:, None]
        * np.arange(mode_count, dtype=np.int64)[None, :]
        % lon_count
    )
    angles = angles_int.astype(np.float64) * (2.0 * math.pi / lon_count)
    stacked = np.stack([np.cos(angles), -np.sin(angles)], axis=1)
    factor = np.where(np.arange(mode_count) == 0, 1.0, 2.0)
    to_modes = (stacked * (2.0 * math.pi / lon_count)).astype(ml_dtypes.bfloat16)
    from_modes = (stacked * factor[None, None, :]).astype(ml_dtypes.bfloat16)
    return lax.optimization_barrier((jnp.asarray(to_modes), jnp.asarray(from_modes)))


def _legendre_kernel(order_ref, gain_ref, cos_ref, seed_ref, out_ref, rows_ref):
    share = out_ref.shape[0]
    degree_count = rows_ref.shape[0]
    cosine = cos_ref[...]
    for o in range(share):
        order = order_ref[o]
        seed = seed_ref[pl.ds(o, 1), :]

        def step(j, carry):
            p_now, p_before, log_scale = carry
            gain = gain_ref[2 * o, j]
            cross = gain_ref[2 * o + 1, j]
            active = j > order
            grown = (gain * cosine) * p_now - cross * p_before
            p_next = jnp.where(active, grown, p_now)
            p_prev = jnp.where(active, p_now, p_before)
            largest = jnp.maximum(jnp.maximum(jnp.abs(p_next), jnp.abs(p_prev)), 1e-30)
            inverse = 1.0 / largest
            p_next = p_next * inverse
            p_prev = p_prev * inverse
            log_scale = log_scale + jnp.log(largest)
            value = jnp.where(j >= order, p_next * jnp.exp(log_scale + seed), 0.0)
            rows_ref[pl.ds(j, 1), :] = value
            return (p_next, p_prev, log_scale)

        ones = jnp.ones_like(cosine)
        zeros = jnp.zeros_like(cosine)
        lax.fori_loop(0, degree_count, step, (ones, zeros, zeros), unroll=4)
        out_ref[o] = rows_ref[...].T


def legendre_rows(orders, degree_count, colatitude):
    lat_count = colatitude.shape[0]
    cosine = jnp.cos(colatitude)
    sine_part = jnp.sin(colatitude)
    order_real = orders.astype(jnp.float32)
    seed_log = 0.5 * (
        jnp.log((2.0 * order_real + 1.0) / (4.0 * math.pi))
        + lax.lgamma(order_real + 0.5)
        - lax.lgamma(order_real + 1.0)
        - 0.5 * math.log(math.pi)
    )
    seed_log = seed_log[:, None] + order_real[:, None] * jnp.log(sine_part)[None, :]
    degree_real = jnp.arange(degree_count, dtype=jnp.float32)[None, :]
    order_col = order_real[:, None]
    forward_gain = jnp.sqrt(
        jnp.maximum(4.0 * degree_real * degree_real - 1.0, 1.0)
        / jnp.maximum(degree_real * degree_real - order_col * order_col, 1.0)
    )
    backward_gain = jnp.sqrt(
        jnp.maximum((degree_real - 1.0) ** 2 - order_col * order_col, 0.0)
        / jnp.maximum(4.0 * (degree_real - 1.0) ** 2 - 1.0, 1.0)
    )
    share = orders.shape[0]
    gains = jnp.stack([forward_gain, forward_gain * backward_gain], axis=1).reshape(
        2 * share, degree_count
    )
    return pl.pallas_call(
        _legendre_kernel,
        out_shape=jax.ShapeDtypeStruct((share, lat_count, degree_count), jnp.float32),
        in_specs=[
            pl.BlockSpec(memory_space=pltpu.SMEM),
            pl.BlockSpec(memory_space=pltpu.SMEM),
            pl.BlockSpec(memory_space=pltpu.VMEM),
            pl.BlockSpec(memory_space=pltpu.VMEM),
        ],
        out_specs=pl.BlockSpec(memory_space=pltpu.VMEM),
        scratch_shapes=[pltpu.VMEM((degree_count, lat_count), jnp.float32)],
        cost_estimate=pl.CostEstimate(
            flops=20 * share * degree_count * lat_count,
            transcendentals=3 * share * degree_count * lat_count,
            bytes_accessed=4 * share * degree_count * lat_count,
        ),
    )(orders.astype(jnp.int32), gains, cosine[None, :], seed_log)


def swap_longitude(blocks):
    return lax.all_to_all(blocks, "lon", split_axis=1, concat_axis=1, tiled=True)


def swap_latitude(blocks):
    return lax.all_to_all(blocks, "lat", split_axis=2, concat_axis=2, tiled=True)


def swap_middle(blocks):
    shape = blocks.shape
    joined = blocks.reshape(shape[0], shape[1] * shape[2], *shape[3:])
    swapped = lax.all_to_all(joined, ("lon", "lat"), split_axis=1, concat_axis=1, tiled=True)
    return swapped.reshape(shape)


def margin(blocks):
    return extended(blocks, (("lat", 1), ("lon", 2)), HW)


def analysis(field_blocks, dft_table, degree_table, lon_count, lat_count):
    mem_count, lat_dev, lon_dev, channels = field_blocks.shape
    row_count = lat_dev // lon_count
    grouped = swap_longitude(
        field_blocks.reshape(mem_count, lon_count, row_count, lon_dev, channels)
    )
    fourier = jnp.einsum(
        "aqrfc,qfkjbe->ajbrkec", grouped, dft_table, preferred_element_type=jnp.float32
    ).astype(jnp.bfloat16)
    columns = swap_middle(fourier)
    if callable(degree_table):
        degree_table = degree_table(fourier)
    a, s, p, r, k, e, c = columns.shape
    flat = columns.transpose(5, 1, 2, 3, 0, 4, 6).reshape(e, s * p * r, a * k * c)
    degrees = jnp.einsum(
        "eln,eld->edn", flat, degree_table, preferred_element_type=jnp.float32
    ).astype(jnp.bfloat16)
    degree_total = degree_table.shape[2]
    degrees = degrees.reshape(e, lat_count, degree_total // lat_count, a, k, c)
    degrees = degrees.transpose(1, 0, 2, 3, 4, 5)
    return lax.all_to_all(degrees, "lat", split_axis=0, concat_axis=0, tiled=True)


def synthesis(spectrum, degree_table, dft_table, lon_count):
    by_degree = lax.all_to_all(spectrum, "lat", split_axis=0, concat_axis=0, tiled=True)
    b, e, d, a, k, c = by_degree.shape
    flat = by_degree.transpose(1, 0, 2, 3, 4, 5).reshape(e, b * d, a * k * c)
    zonal = jnp.einsum(
        "edn,eld->eln", flat, degree_table, preferred_element_type=jnp.float32
    ).astype(jnp.bfloat16)
    total_lat = zonal.shape[1]
    row_count = total_lat // (lon_count * b)
    zonal_modes = zonal.reshape(e, lon_count, b, row_count, a, k, c).transpose(4, 1, 2, 3, 5, 0, 6)
    by_order = swap_middle(zonal_modes)
    grid_blocks = jnp.einsum(
        "ajbrkec,qfkjbe->aqrfc", by_order, dft_table, preferred_element_type=jnp.float32
    ).astype(jnp.bfloat16)
    returned = swap_longitude(grid_blocks)
    return returned.reshape(
        a, returned.shape[1] * returned.shape[2], returned.shape[3], returned.shape[4]
    )


def per_device(fields, cotangent, spectral_weight, local_weight, filter_basis, neighbor_rows):
    lat_count = lax.axis_size("lat")
    lon_count = lax.axis_size("lon")
    lat_index = lax.axis_index("lat")
    lon_index = lax.axis_index("lon")
    mem_count, lat_dev, lon_dev, channels = fields.shape
    degree_dev = spectral_weight.shape[0]
    kernel_count = filter_basis.shape[0]
    band_count = filter_basis.shape[2]
    support = filter_basis.shape[3]
    half_width = HW
    total_lat = lat_dev * lat_count
    total_lon = lon_dev * lon_count
    mode_dev = MDEV
    order_share = mode_dev // lat_count
    row_count = lat_dev // lon_count
    to_modes, from_modes = mode_tables(total_lon, mode_dev * lon_count)
    table_shape = (lon_count, lon_dev, 2, lon_count, lat_count, order_share)
    to_modes = to_modes.reshape(table_shape)
    from_modes = from_modes.reshape(table_shape)
    orders = (
        lon_index * mode_dev + lat_index * order_share + jnp.arange(order_share, dtype=jnp.int32)
    )
    lat_order = (
        jnp.arange(lat_count, dtype=jnp.int32)[None, :, None] * lat_dev
        + jnp.arange(lon_count, dtype=jnp.int32)[:, None, None] * row_count
        + jnp.arange(row_count, dtype=jnp.int32)[None, None, :]
    ).reshape(total_lat)
    colatitude = math.pi * (lat_order.astype(jnp.float32) + 0.5) / total_lat
    tables = {}

    def weighted_after(gate):
        _, colat = lax.optimization_barrier((gate, colatitude))
        legendre = legendre_rows(orders, degree_dev * lat_count, colat)
        quadrature = math.pi / total_lat * jnp.sin(colat)
        tables["weighted"] = (legendre * quadrature[None, :, None]).astype(jnp.bfloat16)
        tables["unweighted"] = legendre.astype(jnp.bfloat16)
        return tables["weighted"]

    real_part = spectral_weight[:, 0]
    imag_part = spectral_weight[:, 1]
    harmonics = analysis(fields, to_modes, weighted_after, lon_count, lat_count)
    weighted = tables["weighted"]
    unweighted = tables["unweighted"]
    harmonics, local_fields, filter_basis, neighbor_rows = lax.optimization_barrier(
        (harmonics, fields, filter_basis, neighbor_rows)
    )
    by_real = jnp.einsum(
        "pedakc,dcx->pedakx", harmonics, real_part, preferred_element_type=jnp.float32
    )
    by_imag = jnp.einsum(
        "pedakc,dcx->pedakx", harmonics, imag_part, preferred_element_type=jnp.float32
    )
    filtered = jnp.stack(
        [by_real[:, :, :, :, 0] - by_imag[:, :, :, :, 1], by_imag[:, :, :, :, 0] + by_real[:, :, :, :, 1]],
        axis=4,
    ).astype(jnp.bfloat16)
    spectral = synthesis(filtered, unweighted, from_modes, lon_count)
    padded = margin(local_fields)
    row_base = lat_index * lat_dev
    my_rows = lax.dynamic_slice_in_dim(neighbor_rows, row_base, lat_dev, 0)
    my_basis = lax.dynamic_slice_in_dim(filter_basis, row_base, lat_dev, 1)
    wide_count = lon_dev + 2 * half_width
    out_pos = jnp.arange(lon_dev, dtype=jnp.int32)[:, None, None]
    in_pos = jnp.arange(wide_count, dtype=jnp.int32)[None, :, None]
    tap_pos = jnp.arange(support, dtype=jnp.int32)[None, None, :]
    forward_pick = (in_pos - out_pos == tap_pos).astype(jnp.float32)
    local_sum = jnp.zeros((kernel_count, mem_count, lat_dev, lon_dev, channels), jnp.float32)
    for band_index in range(band_count):
        source_rows = my_rows[:, band_index] - row_base + half_width
        sources = jnp.take(padded, source_rows, axis=1)
        banded = jnp.einsum(
            "kis,fts->kift", my_basis[:, :, band_index, :].astype(jnp.float32), forward_pick
        ).astype(jnp.bfloat16)
        local_sum = local_sum + jnp.einsum(
            "kift,aitc->kaifc", banded, sources, preferred_element_type=jnp.float32
        )
    local_terms = local_sum.astype(jnp.bfloat16)
    pre_act = spectral.astype(jnp.float32) + jnp.einsum(
        "kaifc,kcd->aifd", local_terms, local_weight, preferred_element_type=jnp.float32
    )
    activation, derivative = gelu_parts(pre_act)
    block_output = (fields.astype(jnp.float32) + activation).astype(jnp.bfloat16)
    grad_mix = (cotangent.astype(jnp.float32) * derivative).astype(jnp.bfloat16)
    grad_filtered = analysis(grad_mix, from_modes, unweighted, lon_count, lat_count)
    back_real = jnp.einsum(
        "pedajx,dcx->pedajc", grad_filtered, real_part, preferred_element_type=jnp.float32
    )
    back_imag = jnp.einsum(
        "pedajx,dcx->pedajc", grad_filtered, imag_part, preferred_element_type=jnp.float32
    )
    grad_harmonics = jnp.stack(
        [
            back_real[:, :, :, :, 0] + back_imag[:, :, :, :, 1],
            back_real[:, :, :, :, 1] - back_imag[:, :, :, :, 0],
        ],
        axis=4,
    ).astype(jnp.bfloat16)
    grad_spectral = synthesis(grad_harmonics, weighted, to_modes, lon_count)
    grad_padded = margin(grad_mix)
    grad_local = jnp.einsum(
        "aitd,kcd->kaitc", grad_padded, local_weight, preferred_element_type=jnp.float32
    ).astype(jnp.bfloat16)
    tall_count = lat_dev + 2 * half_width
    padded_rows = row_base - half_width + jnp.arange(tall_count, dtype=jnp.int32)
    inside = (padded_rows >= 0) & (padded_rows < total_lat)
    safe_rows = jnp.clip(padded_rows, 0, total_lat - 1)
    pad_neighbors = jnp.take(neighbor_rows, safe_rows, axis=0)
    pad_basis = jnp.take(filter_basis, safe_rows, axis=1)
    back_pick = (out_pos - in_pos + 2 * half_width == tap_pos).astype(jnp.float32)
    targets = jnp.arange(lat_dev, dtype=jnp.int32)
    grad_sum = jnp.zeros((mem_count, lat_dev, lon_dev, channels), jnp.float32)
    for band_index in range(band_count):
        banded = jnp.einsum(
            "kis,qts->kiqt", pad_basis[:, :, band_index, :].astype(jnp.float32), back_pick
        ).astype(jnp.bfloat16)
        spread = jnp.einsum(
            "kiqt,kaitc->aiqc", banded, grad_local, preferred_element_type=jnp.float32
        )
        placing = (
            (pad_neighbors[:, band_index][None, :] - row_base == targets[:, None]) & inside[None, :]
        ).astype(jnp.float32)
        spread_rows = spread.transpose(1, 0, 2, 3).reshape(spread.shape[1], -1)
        grad_sum = grad_sum + jnp.einsum(
            "ji,im->jm", placing, spread_rows, precision=lax.Precision.HIGHEST
        ).reshape(lat_dev, mem_count, lon_dev, channels).transpose(1, 0, 2, 3)
    grad_sum = lax.optimization_barrier(grad_sum)
    input_grad = (
        cotangent.astype(jnp.float32) + grad_spectral.astype(jnp.float32) + grad_sum
    ).astype(jnp.bfloat16)
    return (block_output, input_grad)


def solution(mesh):
    in_specs = (
        P(None, "lat", "lon", None),
        P(None, "lat", "lon", None),
        P("lat", None, None, None),
        P(),
        P(),
        P(),
    )
    out_specs = (P(None, "lat", "lon", None), P(None, "lat", "lon", None))
    return jax.shard_map(
        per_device, mesh=mesh, in_specs=in_specs, out_specs=out_specs, check_vma=False
    )
```

```python
import math

import ml_dtypes
import numpy as np

import jax
import jax.numpy as jnp
from jax import lax
from jax.experimental import pallas as pl
from jax.experimental.pallas import tpu as pltpu
from jax.sharding import PartitionSpec as P

MDEV = 16
HW = 8


TANH_SCALE = 0.7978845608028654
CUBIC_TERM = 0.044715


def extended(cells, sides, width):
    for axis, dim in sides:
        count = lax.axis_size(axis)
        head = lax.slice_in_dim(cells, 0, width, axis=dim)
        tail = lax.slice_in_dim(cells, cells.shape[dim] - width, cells.shape[dim], axis=dim)
        cells = jnp.concatenate(
            [
                lax.ppermute(tail, axis, [(i, (i + 1) % count) for i in range(count)]),
                cells,
                lax.ppermute(head, axis, [((i + 1) % count, i) for i in range(count)]),
            ],
            axis=dim,
        )
    return cells


def gelu_parts(values):
    tanh_input = TANH_SCALE * (values + CUBIC_TERM * values * values * values)
    hyper = jnp.tanh(tanh_input)
    result = 0.5 * values * (1.0 + hyper)
    derivative = 0.5 * (1.0 + hyper) + 0.5 * values * (1.0 - hyper * hyper) * TANH_SCALE * (
        1.0 + 3.0 * CUBIC_TERM * values * values
    )
    return (result, derivative)


def mode_tables(lon_count, mode_count):
    angles_int = (
        np.arange(lon_count, dtype=np.int64)[:, None]
        * np.arange(mode_count, dtype=np.int64)[None, :]
        % lon_count
    )
    angles = angles_int.astype(np.float64) * (2.0 * math.pi / lon_count)
    stacked = np.stack([np.cos(angles), -np.sin(angles)], axis=1)
    factor = np.where(np.arange(mode_count) == 0, 1.0, 2.0)
    to_modes = (stacked * (2.0 * math.pi / lon_count)).astype(ml_dtypes.bfloat16)
    from_modes = (stacked * factor[None, None, :]).astype(ml_dtypes.bfloat16)
    return lax.optimization_barrier((jnp.asarray(to_modes), jnp.asarray(from_modes)))


def _legendre_kernel(order_ref, gain_ref, cos_ref, seed_ref, out_ref, rows_ref):
    share = out_ref.shape[0]
    degree_count = rows_ref.shape[0]
    cosine = cos_ref[...]
    for o in range(share):
        order = order_ref[o]
        seed = seed_ref[pl.ds(o, 1), :]

        def step(j, carry):
            p_now, p_before, log_scale = carry
            gain = gain_ref[2 * o, j]
            cross = gain_ref[2 * o + 1, j]
            active = j > order
            grown = (gain * cosine) * p_now - cross * p_before
            p_next = jnp.where(active, grown, p_now)
            p_prev = jnp.where(active, p_now, p_before)
            largest = jnp.maximum(jnp.maximum(jnp.abs(p_next), jnp.abs(p_prev)), 1e-30)
            inverse = 1.0 / largest
            p_next = p_next * inverse
            p_prev = p_prev * inverse
            log_scale = log_scale + jnp.log(largest)
            value = jnp.where(j >= order, p_next * jnp.exp(log_scale + seed), 0.0)
            rows_ref[pl.ds(j, 1), :] = value
            return (p_next, p_prev, log_scale)

        ones = jnp.ones_like(cosine)
        zeros = jnp.zeros_like(cosine)
        lax.fori_loop(0, degree_count, step, (ones, zeros, zeros), unroll=4)
        out_ref[o] = rows_ref[...].T


def legendre_rows(orders, degree_count, colatitude):
    lat_count = colatitude.shape[0]
    cosine = jnp.cos(colatitude)
    sine_part = jnp.sin(colatitude)
    order_real = orders.astype(jnp.float32)
    seed_log = 0.5 * (
        jnp.log((2.0 * order_real + 1.0) / (4.0 * math.pi))
        + lax.lgamma(order_real + 0.5)
        - lax.lgamma(order_real + 1.0)
        - 0.5 * math.log(math.pi)
    )
    seed_log = seed_log[:, None] + order_real[:, None] * jnp.log(sine_part)[None, :]
    degree_real = jnp.arange(degree_count, dtype=jnp.float32)[None, :]
    order_col = order_real[:, None]
    forward_gain = jnp.sqrt(
        jnp.maximum(4.0 * degree_real * degree_real - 1.0, 1.0)
        / jnp.maximum(degree_real * degree_real - order_col * order_col, 1.0)
    )
    backward_gain = jnp.sqrt(
        jnp.maximum((degree_real - 1.0) ** 2 - order_col * order_col, 0.0)
        / jnp.maximum(4.0 * (degree_real - 1.0) ** 2 - 1.0, 1.0)
    )
    share = orders.shape[0]
    gains = jnp.stack([forward_gain, forward_gain * backward_gain], axis=1).reshape(
        2 * share, degree_count
    )
    return pl.pallas_call(
        _legendre_kernel,
        out_shape=jax.ShapeDtypeStruct((share, lat_count, degree_count), jnp.float32),
        in_specs=[
            pl.BlockSpec(memory_space=pltpu.SMEM),
            pl.BlockSpec(memory_space=pltpu.SMEM),
            pl.BlockSpec(memory_space=pltpu.VMEM),
            pl.BlockSpec(memory_space=pltpu.VMEM),
        ],
        out_specs=pl.BlockSpec(memory_space=pltpu.VMEM),
        scratch_shapes=[pltpu.VMEM((degree_count, lat_count), jnp.float32)],
        cost_estimate=pl.CostEstimate(
            flops=20 * share * degree_count * lat_count,
            transcendentals=3 * share * degree_count * lat_count,
            bytes_accessed=4 * share * degree_count * lat_count,
        ),
    )(orders.astype(jnp.int32), gains, cosine[None, :], seed_log)


def swap_longitude(blocks):
    return lax.all_to_all(blocks, "lon", split_axis=1, concat_axis=1, tiled=True)


def swap_latitude(blocks):
    return lax.all_to_all(blocks, "lat", split_axis=2, concat_axis=2, tiled=True)


def swap_middle(blocks):
    shape = blocks.shape
    joined = blocks.reshape(shape[0], shape[1] * shape[2], *shape[3:])
    swapped = lax.all_to_all(joined, ("lon", "lat"), split_axis=1, concat_axis=1, tiled=True)
    return swapped.reshape(shape)


def margin(blocks):
    return extended(blocks, (("lat", 1), ("lon", 2)), HW)


def analysis(field_blocks, dft_table, degree_table, lon_count, lat_count):
    mem_count, lat_dev, lon_dev, channels = field_blocks.shape
    row_count = lat_dev // lon_count
    grouped = swap_longitude(
        field_blocks.reshape(mem_count, lon_count, row_count, lon_dev, channels)
    )
    fourier = jnp.einsum(
        "aqrfc,qfkjbe->ajbrkec", grouped, dft_table, preferred_element_type=jnp.float32
    ).astype(jnp.bfloat16)
    columns = swap_middle(fourier)
    if callable(degree_table):
        degree_table = degree_table(fourier)
    a, s, p, r, k, e, c = columns.shape
    flat = columns.transpose(5, 1, 2, 3, 0, 4, 6).reshape(e, s * p * r, a * k * c)
    degrees = jnp.einsum(
        "eln,eld->edn", flat, degree_table, preferred_element_type=jnp.float32
    ).astype(jnp.bfloat16)
    degree_total = degree_table.shape[2]
    degrees = degrees.reshape(e, lat_count, degree_total // lat_count, a, k, c)
    degrees = degrees.transpose(1, 0, 2, 3, 4, 5)
    return lax.all_to_all(degrees, "lat", split_axis=0, concat_axis=0, tiled=True)


def synthesis(spectrum, degree_table, dft_table, lon_count):
    by_degree = lax.all_to_all(spectrum, "lat", split_axis=0, concat_axis=0, tiled=True)
    b, e, d, a, k, c = by_degree.shape
    flat = by_degree.transpose(1, 0, 2, 3, 4, 5).reshape(e, b * d, a * k * c)
    zonal = jnp.einsum(
        "edn,eld->eln", flat, degree_table, preferred_element_type=jnp.float32
    ).astype(jnp.bfloat16)
    total_lat = zonal.shape[1]
    row_count = total_lat // (lon_count * b)
    zonal_modes = zonal.reshape(e, lon_count, b, row_count, a, k, c).transpose(4, 1, 2, 3, 5, 0, 6)
    by_order = swap_middle(zonal_modes)
    grid_blocks = jnp.einsum(
        "ajbrkec,qfkjbe->aqrfc", by_order, dft_table, preferred_element_type=jnp.float32
    ).astype(jnp.bfloat16)
    returned = swap_longitude(grid_blocks)
    return returned.reshape(
        a, returned.shape[1] * returned.shape[2], returned.shape[3], returned.shape[4]
    )


def per_device(fields, cotangent, spectral_weight, local_weight, filter_basis, neighbor_rows):
    lat_count = lax.axis_size("lat")
    lon_count = lax.axis_size("lon")
    lat_index = lax.axis_index("lat")
    lon_index = lax.axis_index("lon")
    mem_count, lat_dev, lon_dev, channels = fields.shape
    degree_dev = spectral_weight.shape[0]
    kernel_count = filter_basis.shape[0]
    band_count = filter_basis.shape[2]
    support = filter_basis.shape[3]
    half_width = HW
    total_lat = lat_dev * lat_count
    total_lon = lon_dev * lon_count
    mode_dev = MDEV
    order_share = mode_dev // lat_count
    row_count = lat_dev // lon_count
    to_modes, from_modes = mode_tables(total_lon, mode_dev * lon_count)
    table_shape = (lon_count, lon_dev, 2, lon_count, lat_count, order_share)
    to_modes = to_modes.reshape(table_shape)
    from_modes = from_modes.reshape(table_shape)
    orders = (
        lon_index * mode_dev + lat_index * order_share + jnp.arange(order_share, dtype=jnp.int32)
    )
    lat_order = (
        jnp.arange(lat_count, dtype=jnp.int32)[None, :, None] * lat_dev
        + jnp.arange(lon_count, dtype=jnp.int32)[:, None, None] * row_count
        + jnp.arange(row_count, dtype=jnp.int32)[None, None, :]
    ).reshape(total_lat)
    colatitude = math.pi * (lat_order.astype(jnp.float32) + 0.5) / total_lat
    tables = {}

    def weighted_after(gate):
        _, colat = lax.optimization_barrier((gate, colatitude))
        legendre = legendre_rows(orders, degree_dev * lat_count, colat)
        quadrature = math.pi / total_lat * jnp.sin(colat)
        tables["weighted"] = (legendre * quadrature[None, :, None]).astype(jnp.bfloat16)
        tables["unweighted"] = legendre.astype(jnp.bfloat16)
        return tables["weighted"]

    real_part = spectral_weight[:, 0]
    imag_part = spectral_weight[:, 1]
    harmonics = analysis(fields, to_modes, weighted_after, lon_count, lat_count)
    weighted = tables["weighted"]
    unweighted = tables["unweighted"]
    row_base = lat_index * lat_dev
    tall_count = lat_dev + 2 * half_width
    padded_rows = row_base - half_width + jnp.arange(tall_count, dtype=jnp.int32)
    safe_rows = jnp.clip(padded_rows, 0, total_lat - 1)
    harmonics, local_fields, my_rows, my_basis, pad_neighbors, pad_basis = (
        lax.optimization_barrier(
            (
                harmonics,
                fields,
                lax.dynamic_slice_in_dim(neighbor_rows, row_base, lat_dev, 0),
                lax.dynamic_slice_in_dim(filter_basis, row_base, lat_dev, 1),
                jnp.take(neighbor_rows, safe_rows, axis=0),
                jnp.take(filter_basis, safe_rows, axis=1),
            )
        )
    )
    by_real = jnp.einsum(
        "pedakc,dcx->pedakx", harmonics, real_part, preferred_element_type=jnp.float32
    )
    by_imag = jnp.einsum(
        "pedakc,dcx->pedakx", harmonics, imag_part, preferred_element_type=jnp.float32
    )
    filtered = jnp.stack(
        [by_real[:, :, :, :, 0] - by_imag[:, :, :, :, 1], by_imag[:, :, :, :, 0] + by_real[:, :, :, :, 1]],
        axis=4,
    ).astype(jnp.bfloat16)
    spectral = synthesis(filtered, unweighted, from_modes, lon_count)
    padded = margin(local_fields)
    wide_count = lon_dev + 2 * half_width
    out_pos = jnp.arange(lon_dev, dtype=jnp.int32)[:, None, None]
    in_pos = jnp.arange(wide_count, dtype=jnp.int32)[None, :, None]
    tap_pos = jnp.arange(support, dtype=jnp.int32)[None, None, :]
    forward_pick = (in_pos - out_pos == tap_pos).astype(jnp.float32)
    local_sum = jnp.zeros((kernel_count, mem_count, lat_dev, lon_dev, channels), jnp.float32)
    for band_index in range(band_count):
        source_rows = my_rows[:, band_index] - row_base + half_width
        sources = jnp.take(padded, source_rows, axis=1)
        banded = jnp.einsum(
            "kis,fts->kift", my_basis[:, :, band_index, :].astype(jnp.float32), forward_pick
        ).astype(jnp.bfloat16)
        local_sum = local_sum + jnp.einsum(
            "kift,aitc->kaifc", banded, sources, preferred_element_type=jnp.float32
        )
    local_terms = local_sum.astype(jnp.bfloat16)
    pre_act = spectral.astype(jnp.float32) + jnp.einsum(
        "kaifc,kcd->aifd", local_terms, local_weight, preferred_element_type=jnp.float32
    )
    activation, derivative = gelu_parts(pre_act)
    block_output = (fields.astype(jnp.float32) + activation).astype(jnp.bfloat16)
    grad_mix = (cotangent.astype(jnp.float32) * derivative).astype(jnp.bfloat16)
    grad_filtered = analysis(grad_mix, from_modes, unweighted, lon_count, lat_count)
    back_real = jnp.einsum(
        "pedajx,dcx->pedajc", grad_filtered, real_part, preferred_element_type=jnp.float32
    )
    back_imag = jnp.einsum(
        "pedajx,dcx->pedajc", grad_filtered, imag_part, preferred_element_type=jnp.float32
    )
    grad_harmonics = jnp.stack(
        [
            back_real[:, :, :, :, 0] + back_imag[:, :, :, :, 1],
            back_real[:, :, :, :, 1] - back_imag[:, :, :, :, 0],
        ],
        axis=4,
    ).astype(jnp.bfloat16)
    grad_spectral = synthesis(grad_harmonics, weighted, to_modes, lon_count)
    grad_padded = margin(grad_mix)
    grad_local = jnp.einsum(
        "aitd,kcd->kaitc", grad_padded, local_weight, preferred_element_type=jnp.float32
    ).astype(jnp.bfloat16)
    inside = (padded_rows >= 0) & (padded_rows < total_lat)
    back_pick = (out_pos - in_pos + 2 * half_width == tap_pos).astype(jnp.float32)
    targets = jnp.arange(lat_dev, dtype=jnp.int32)
    grad_sum = jnp.zeros((mem_count, lat_dev, lon_dev, channels), jnp.float32)
    for band_index in range(band_count):
        banded = jnp.einsum(
            "kis,qts->kiqt", pad_basis[:, :, band_index, :].astype(jnp.float32), back_pick
        ).astype(jnp.bfloat16)
        spread = jnp.einsum(
            "kiqt,kaitc->aiqc", banded, grad_local, preferred_element_type=jnp.float32
        )
        placing = (
            (pad_neighbors[:, band_index][None, :] - row_base == targets[:, None]) & inside[None, :]
        ).astype(jnp.float32)
        spread_rows = spread.transpose(1, 0, 2, 3).reshape(spread.shape[1], -1)
        grad_sum = grad_sum + jnp.einsum(
            "ji,im->jm", placing, spread_rows, precision=lax.Precision.HIGHEST
        ).reshape(lat_dev, mem_count, lon_dev, channels).transpose(1, 0, 2, 3)
    grad_sum = lax.optimization_barrier(grad_sum)
    input_grad = (
        cotangent.astype(jnp.float32) + grad_spectral.astype(jnp.float32) + grad_sum
    ).astype(jnp.bfloat16)
    return (block_output, input_grad)


def solution(mesh):
    in_specs = (
        P(None, "lat", "lon", None),
        P(None, "lat", "lon", None),
        P("lat", None, None, None),
        P(),
        P(),
        P(),
    )
    out_specs = (P(None, "lat", "lon", None), P(None, "lat", "lon", None))
    return jax.shard_map(
        per_device, mesh=mesh, in_specs=in_specs, out_specs=out_specs, check_vma=False
    )
```

```python
import math

import ml_dtypes
import numpy as np

import jax
import jax.numpy as jnp
from jax import lax
from jax.experimental import pallas as pl
from jax.experimental.pallas import tpu as pltpu
from jax.sharding import PartitionSpec as P

MDEV = 16
HW = 8


TANH_SCALE = 0.7978845608028654
CUBIC_TERM = 0.044715


def extended(cells, sides, width):
    for axis, dim in sides:
        count = lax.axis_size(axis)
        head = lax.slice_in_dim(cells, 0, width, axis=dim)
        tail = lax.slice_in_dim(cells, cells.shape[dim] - width, cells.shape[dim], axis=dim)
        cells = jnp.concatenate(
            [
                lax.ppermute(tail, axis, [(i, (i + 1) % count) for i in range(count)]),
                cells,
                lax.ppermute(head, axis, [((i + 1) % count, i) for i in range(count)]),
            ],
            axis=dim,
        )
    return cells


def gelu_parts(values):
    tanh_input = TANH_SCALE * (values + CUBIC_TERM * values * values * values)
    hyper = jnp.tanh(tanh_input)
    result = 0.5 * values * (1.0 + hyper)
    derivative = 0.5 * (1.0 + hyper) + 0.5 * values * (1.0 - hyper * hyper) * TANH_SCALE * (
        1.0 + 3.0 * CUBIC_TERM * values * values
    )
    return (result, derivative)


def mode_tables(lon_count, mode_count):
    angles_int = (
        np.arange(lon_count, dtype=np.int64)[:, None]
        * np.arange(mode_count, dtype=np.int64)[None, :]
        % lon_count
    )
    angles = angles_int.astype(np.float64) * (2.0 * math.pi / lon_count)
    stacked = np.stack([np.cos(angles), -np.sin(angles)], axis=1)
    factor = np.where(np.arange(mode_count) == 0, 1.0, 2.0)
    to_modes = (stacked * (2.0 * math.pi / lon_count)).astype(ml_dtypes.bfloat16)
    from_modes = (stacked * factor[None, None, :]).astype(ml_dtypes.bfloat16)
    return lax.optimization_barrier((jnp.asarray(to_modes), jnp.asarray(from_modes)))


def _legendre_kernel(order_ref, gain_ref, cos_ref, seed_ref, out_ref, rows_ref):
    share = out_ref.shape[0]
    degree_count = rows_ref.shape[0]
    cosine = cos_ref[...]
    for o in range(share):
        order = order_ref[o]
        seed = seed_ref[pl.ds(o, 1), :]

        def step(j, carry):
            p_now, p_before, log_scale = carry
            gain = gain_ref[2 * o, j]
            cross = gain_ref[2 * o + 1, j]
            active = j > order
            grown = (gain * cosine) * p_now - cross * p_before
            p_next = jnp.where(active, grown, p_now)
            p_prev = jnp.where(active, p_now, p_before)
            largest = jnp.maximum(jnp.maximum(jnp.abs(p_next), jnp.abs(p_prev)), 1e-30)
            inverse = 1.0 / largest
            p_next = p_next * inverse
            p_prev = p_prev * inverse
            log_scale = log_scale + jnp.log(largest)
            value = jnp.where(j >= order, p_next * jnp.exp(log_scale + seed), 0.0)
            rows_ref[pl.ds(j, 1), :] = value
            return (p_next, p_prev, log_scale)

        ones = jnp.ones_like(cosine)
        zeros = jnp.zeros_like(cosine)
        lax.fori_loop(0, degree_count, step, (ones, zeros, zeros), unroll=4)
        out_ref[o] = rows_ref[...].T


def legendre_rows(orders, degree_count, colatitude):
    lat_count = colatitude.shape[0]
    cosine = jnp.cos(colatitude)
    sine_part = jnp.sin(colatitude)
    order_real = orders.astype(jnp.float32)
    seed_log = 0.5 * (
        jnp.log((2.0 * order_real + 1.0) / (4.0 * math.pi))
        + lax.lgamma(order_real + 0.5)
        - lax.lgamma(order_real + 1.0)
        - 0.5 * math.log(math.pi)
    )
    seed_log = seed_log[:, None] + order_real[:, None] * jnp.log(sine_part)[None, :]
    degree_real = jnp.arange(degree_count, dtype=jnp.float32)[None, :]
    order_col = order_real[:, None]
    forward_gain = jnp.sqrt(
        jnp.maximum(4.0 * degree_real * degree_real - 1.0, 1.0)
        / jnp.maximum(degree_real * degree_real - order_col * order_col, 1.0)
    )
    backward_gain = jnp.sqrt(
        jnp.maximum((degree_real - 1.0) ** 2 - order_col * order_col, 0.0)
        / jnp.maximum(4.0 * (degree_real - 1.0) ** 2 - 1.0, 1.0)
    )
    share = orders.shape[0]
    gains = jnp.stack([forward_gain, forward_gain * backward_gain], axis=1).reshape(
        2 * share, degree_count
    )
    return pl.pallas_call(
        _legendre_kernel,
        out_shape=jax.ShapeDtypeStruct((share, lat_count, degree_count), jnp.float32),
        in_specs=[
            pl.BlockSpec(memory_space=pltpu.SMEM),
            pl.BlockSpec(memory_space=pltpu.SMEM),
            pl.BlockSpec(memory_space=pltpu.VMEM),
            pl.BlockSpec(memory_space=pltpu.VMEM),
        ],
        out_specs=pl.BlockSpec(memory_space=pltpu.VMEM),
        scratch_shapes=[pltpu.VMEM((degree_count, lat_count), jnp.float32)],
        cost_estimate=pl.CostEstimate(
            flops=20 * share * degree_count * lat_count,
            transcendentals=3 * share * degree_count * lat_count,
            bytes_accessed=4 * share * degree_count * lat_count,
        ),
    )(orders.astype(jnp.int32), gains, cosine[None, :], seed_log)


def swap_longitude(blocks):
    return lax.all_to_all(blocks, "lon", split_axis=1, concat_axis=1, tiled=True)


def swap_latitude(blocks):
    return lax.all_to_all(blocks, "lat", split_axis=2, concat_axis=2, tiled=True)


def swap_middle(blocks):
    shape = blocks.shape
    joined = blocks.reshape(shape[0], shape[1] * shape[2], *shape[3:])
    swapped = lax.all_to_all(joined, ("lon", "lat"), split_axis=1, concat_axis=1, tiled=True)
    return swapped.reshape(shape)


def margin(blocks):
    return extended(blocks, (("lat", 1), ("lon", 2)), HW)


def analysis(field_blocks, dft_table, degree_table, lon_count, lat_count):
    mem_count, lat_dev, lon_dev, channels = field_blocks.shape
    row_count = lat_dev // lon_count
    grouped = swap_longitude(
        field_blocks.reshape(mem_count, lon_count, row_count, lon_dev, channels)
    )
    fourier = jnp.einsum(
        "aqrfc,qfkjbe->ajbrkec", grouped, dft_table, preferred_element_type=jnp.float32
    ).astype(jnp.bfloat16)
    columns = swap_middle(fourier)
    if callable(degree_table):
        degree_table = degree_table(fourier)
    a, s, p, r, k, e, c = columns.shape
    flat = columns.transpose(5, 1, 2, 3, 0, 4, 6).reshape(e, s * p * r, a * k * c)
    degrees = jnp.einsum(
        "eln,eld->edn", flat, degree_table, preferred_element_type=jnp.float32
    ).astype(jnp.bfloat16)
    degree_total = degree_table.shape[2]
    degrees = degrees.reshape(e, lat_count, degree_total // lat_count, a, k, c)
    degrees = degrees.transpose(1, 0, 2, 3, 4, 5)
    return lax.all_to_all(degrees, "lat", split_axis=0, concat_axis=0, tiled=True)


def synthesis(spectrum, degree_table, dft_table, lon_count):
    by_degree = lax.all_to_all(spectrum, "lat", split_axis=0, concat_axis=0, tiled=True)
    b, e, d, a, k, c = by_degree.shape
    flat = by_degree.transpose(1, 0, 2, 3, 4, 5).reshape(e, b * d, a * k * c)
    zonal = jnp.einsum(
        "edn,eld->eln", flat, degree_table, preferred_element_type=jnp.float32
    ).astype(jnp.bfloat16)
    total_lat = zonal.shape[1]
    row_count = total_lat // (lon_count * b)
    zonal_modes = zonal.reshape(e, lon_count, b, row_count, a, k, c).transpose(4, 1, 2, 3, 5, 0, 6)
    by_order = swap_middle(zonal_modes)
    grid_blocks = jnp.einsum(
        "ajbrkec,qfkjbe->aqrfc", by_order, dft_table, preferred_element_type=jnp.float32
    ).astype(jnp.bfloat16)
    returned = swap_longitude(grid_blocks)
    return returned.reshape(
        a, returned.shape[1] * returned.shape[2], returned.shape[3], returned.shape[4]
    )


def per_device(fields, cotangent, spectral_weight, local_weight, filter_basis, neighbor_rows):
    lat_count = lax.axis_size("lat")
    lon_count = lax.axis_size("lon")
    lat_index = lax.axis_index("lat")
    lon_index = lax.axis_index("lon")
    mem_count, lat_dev, lon_dev, channels = fields.shape
    degree_dev = spectral_weight.shape[0]
    kernel_count = filter_basis.shape[0]
    band_count = filter_basis.shape[2]
    support = filter_basis.shape[3]
    half_width = HW
    total_lat = lat_dev * lat_count
    total_lon = lon_dev * lon_count
    mode_dev = MDEV
    order_share = mode_dev // lat_count
    row_count = lat_dev // lon_count
    to_modes, from_modes = mode_tables(total_lon, mode_dev * lon_count)
    table_shape = (lon_count, lon_dev, 2, lon_count, lat_count, order_share)
    to_modes = to_modes.reshape(table_shape)
    from_modes = from_modes.reshape(table_shape)
    orders = (
        lon_index * mode_dev + lat_index * order_share + jnp.arange(order_share, dtype=jnp.int32)
    )
    lat_order = (
        jnp.arange(lat_count, dtype=jnp.int32)[None, :, None] * lat_dev
        + jnp.arange(lon_count, dtype=jnp.int32)[:, None, None] * row_count
        + jnp.arange(row_count, dtype=jnp.int32)[None, None, :]
    ).reshape(total_lat)
    colatitude = math.pi * (lat_order.astype(jnp.float32) + 0.5) / total_lat
    tables = {}

    def weighted_after(gate):
        _, colat = lax.optimization_barrier((gate, colatitude))
        legendre = legendre_rows(orders, degree_dev * lat_count, colat)
        quadrature = math.pi / total_lat * jnp.sin(colat)
        tables["weighted"] = (legendre * quadrature[None, :, None]).astype(jnp.bfloat16)
        tables["unweighted"] = legendre.astype(jnp.bfloat16)
        return tables["weighted"]

    real_part = spectral_weight[:, 0]
    imag_part = spectral_weight[:, 1]
    harmonics = analysis(fields, to_modes, weighted_after, lon_count, lat_count)
    weighted = tables["weighted"]
    unweighted = tables["unweighted"]
    harmonics, local_fields, neighbor_rows = lax.optimization_barrier(
        (harmonics, fields, neighbor_rows)
    )
    by_real = jnp.einsum(
        "pedakc,dcx->pedakx", harmonics, real_part, preferred_element_type=jnp.float32
    )
    by_imag = jnp.einsum(
        "pedakc,dcx->pedakx", harmonics, imag_part, preferred_element_type=jnp.float32
    )
    filtered = jnp.stack(
        [by_real[:, :, :, :, 0] - by_imag[:, :, :, :, 1], by_imag[:, :, :, :, 0] + by_real[:, :, :, :, 1]],
        axis=4,
    ).astype(jnp.bfloat16)
    spectral = synthesis(filtered, unweighted, from_modes, lon_count)
    padded = margin(local_fields)
    row_base = lat_index * lat_dev
    my_rows = lax.dynamic_slice_in_dim(neighbor_rows, row_base, lat_dev, 0)
    my_basis = lax.dynamic_slice_in_dim(filter_basis, row_base, lat_dev, 1)
    wide_count = lon_dev + 2 * half_width
    out_pos = jnp.arange(lon_dev, dtype=jnp.int32)[:, None, None]
    in_pos = jnp.arange(wide_count, dtype=jnp.int32)[None, :, None]
    tap_pos = jnp.arange(support, dtype=jnp.int32)[None, None, :]
    forward_pick = (in_pos - out_pos == tap_pos).astype(jnp.float32)
    local_sum = jnp.zeros((kernel_count, mem_count, lat_dev, lon_dev, channels), jnp.float32)
    for band_index in range(band_count):
        source_rows = my_rows[:, band_index] - row_base + half_width
        sources = jnp.take(padded, source_rows, axis=1)
        banded = jnp.einsum(
            "kis,fts->kift", my_basis[:, :, band_index, :].astype(jnp.float32), forward_pick
        ).astype(jnp.bfloat16)
        local_sum = local_sum + jnp.einsum(
            "kift,aitc->kaifc", banded, sources, preferred_element_type=jnp.float32
        )
    local_terms = local_sum.astype(jnp.bfloat16)
    pre_act = spectral.astype(jnp.float32) + jnp.einsum(
        "kaifc,kcd->aifd", local_terms, local_weight, preferred_element_type=jnp.float32
    )
    activation, derivative = gelu_parts(pre_act)
    block_output = (fields.astype(jnp.float32) + activation).astype(jnp.bfloat16)
    grad_mix = (cotangent.astype(jnp.float32) * derivative).astype(jnp.bfloat16)
    grad_filtered = analysis(grad_mix, from_modes, unweighted, lon_count, lat_count)
    back_real = jnp.einsum(
        "pedajx,dcx->pedajc", grad_filtered, real_part, preferred_element_type=jnp.float32
    )
    back_imag = jnp.einsum(
        "pedajx,dcx->pedajc", grad_filtered, imag_part, preferred_element_type=jnp.float32
    )
    grad_harmonics = jnp.stack(
        [
            back_real[:, :, :, :, 0] + back_imag[:, :, :, :, 1],
            back_real[:, :, :, :, 1] - back_imag[:, :, :, :, 0],
        ],
        axis=4,
    ).astype(jnp.bfloat16)
    grad_spectral = synthesis(grad_harmonics, weighted, to_modes, lon_count)
    grad_padded = margin(grad_mix)
    grad_local = jnp.einsum(
        "aitd,kcd->kaitc", grad_padded, local_weight, preferred_element_type=jnp.float32
    ).astype(jnp.bfloat16)
    tall_count = lat_dev + 2 * half_width
    padded_rows = row_base - half_width + jnp.arange(tall_count, dtype=jnp.int32)
    inside = (padded_rows >= 0) & (padded_rows < total_lat)
    safe_rows = jnp.clip(padded_rows, 0, total_lat - 1)
    pad_neighbors = jnp.take(neighbor_rows, safe_rows, axis=0)
    pad_basis = jnp.take(filter_basis, safe_rows, axis=1)
    back_pick = (out_pos - in_pos + 2 * half_width == tap_pos).astype(jnp.float32)
    targets = jnp.arange(lat_dev, dtype=jnp.int32)
    grad_sum = jnp.zeros((mem_count, lat_dev, lon_dev, channels), jnp.float32)
    for band_index in range(band_count):
        banded = jnp.einsum(
            "kis,qts->kiqt", pad_basis[:, :, band_index, :].astype(jnp.float32), back_pick
        ).astype(jnp.bfloat16)
        spread = jnp.einsum(
            "kiqt,kaitc->aiqc", banded, grad_local, preferred_element_type=jnp.float32
        )
        placing = (
            (pad_neighbors[:, band_index][None, :] - row_base == targets[:, None]) & inside[None, :]
        ).astype(jnp.float32)
        spread_rows = spread.transpose(1, 0, 2, 3).reshape(spread.shape[1], -1)
        grad_sum = grad_sum + jnp.einsum(
            "ji,im->jm", placing, spread_rows, precision=lax.Precision.HIGHEST
        ).reshape(lat_dev, mem_count, lon_dev, channels).transpose(1, 0, 2, 3)
    grad_sum = lax.optimization_barrier(grad_sum)
    input_grad = (
        cotangent.astype(jnp.float32) + grad_spectral.astype(jnp.float32) + grad_sum
    ).astype(jnp.bfloat16)
    return (block_output, input_grad)


def solution(mesh):
    in_specs = (
        P(None, "lat", "lon", None),
        P(None, "lat", "lon", None),
        P("lat", None, None, None),
        P(),
        P(),
        P(),
    )
    out_specs = (P(None, "lat", "lon", None), P(None, "lat", "lon", None))
    return jax.shard_map(
        per_device, mesh=mesh, in_specs=in_specs, out_specs=out_specs, check_vma=False
    )
```
